256 devices in a mesh: gx: 16 (over z, y_hi), gy: 16 (over y_lo, x, core).
Axes of the slice: x: 4, y: 4 (y_hi: 2, y_lo: 2; y = y_hi * 2 + y_lo), z: 8, core: 2. Of those that a mesh axis runs over, the one named last changes fastest.
Arguments:
- field: float32 [32, 64, 256, 128], P(None, 'gx', 'gy'), may hold values from -6 to 6
- rates: float32 [32], replicated, may hold values from 0.2 to 1
- mixing: float32 [32, 32], replicated, may hold values from -1 to 1
- secretion: float32 [32, 16, 64, 256], P(None, 'gx', 'gy'), may hold values from -6 to 6
- positions: float32 [3, 16, 64, 256], P(None, 'gx', 'gy'), may hold values from 0 to 256, as said below
- stiffness: float32 [16, 64, 256], P('gx', 'gy'), may hold values from 0.5 to 2
- occupancy: int32 [16, 64, 256], P('gx', 'gy'), may hold values from 0 to 1
- offsets: int32 [16, 64, 256], P('gx', 'gy'), may hold values from 0 to 127
- migrant_state: float32 [8, 560, 2048], P(None, 'gx', 'gy'), may hold values from -6 to 6
- migrant_live: int32 [8, 16, 2048], P(None, 'gx', 'gy'), may hold values 0 or 1
Outputs:
- new_field: float32 [32, 64, 256, 128], P(None, 'gx', 'gy')
- displacement: float32 [3, 16, 64, 256], P(None, 'gx', 'gy')
- arrived: float32 [8, 560, 2048], P(None, 'gx', 'gy')
The draws below stay inside these ranges and needn't reach their ends.
Inputs may be any that keep to these rules, and one draw needn't show every extreme that they name: `positions`: a slot's coordinates lie inside the box of its bin.
All inputs are finite; a program needn't handle non-finite values. No bound on the sum of `migrant_live` on one device may be relied on, other than what follows from the above.
Results may differ from the reference program's by a relative error of at most 0.0003.
Values sent between devices are 32-bit elements; how exact they have to be, the bound alone decides.
No kernel may reach another device: no remote copies, remote signals or barrier semaphores. Data moves between devices by JAX's collectives and lax.ppermute only.
A program may use at most 64 MiB of HBM per device.

```python
import functools
import math
import jax
import jax.numpy as jnp
from jax import lax

S = 32
NZ = 128
BIN_XY = 4
BIN_Z = 8
SLOTS = 16
MIG = 128
SUBSTEPS = 4
BZ = 16
NX = 64
NY = 256
NBX = 16
NBY = 64
STATE = 35
N_GX = 16
N_GY = 16


def draw_positions(key, part):
    shape = (3, NBX, NBY, BZ * SLOTS)
    within = jax.random.uniform(key, shape, jnp.float32)
    plane = lax.broadcasted_iota(jnp.int32, shape, 0)
    bin_x = lax.broadcasted_iota(jnp.int32, shape, 1)
    bin_y = lax.broadcasted_iota(jnp.int32, shape, 2)
    bin_z = lax.broadcasted_iota(jnp.int32, shape, 3) // SLOTS
    start = jnp.where(plane == 0, bin_x * BIN_XY, jnp.where(plane == 1, bin_y * BIN_XY, bin_z * BIN_Z))
    extent = jnp.where(plane == 2, BIN_Z, BIN_XY)
    return (start.astype(jnp.float32) + within * extent.astype(jnp.float32) * 0.999).astype(jnp.float32)


def draw_occupancy(key, part):
    shape = (NBX, NBY, BZ * SLOTS)
    bin_x = lax.broadcasted_iota(jnp.int32, shape, 0)
    bin_y = lax.broadcasted_iota(jnp.int32, shape, 1)
    distant = jnp.abs(2 * bin_x + 1 - NBX) * 6 // NBX + jnp.abs(2 * bin_y + 1 - NBY) * 6 // NBY
    level = jnp.maximum(3, 15 - distant)
    rolled = jax.random.randint(key, shape, 0, 16)
    return (rolled < level).astype(jnp.int32)


def plant(values, stream_key, low, top_value):
    shape = values.shape
    place = [jax.random.randint(jax.random.fold_in(stream_key, axis), (), 0, shape[axis]) for axis in range(len(shape))]
    values = values.at[tuple(place)].set(low)
    longest = shape.index(max(shape))
    place[longest] = (place[longest] + 1) % shape[longest]
    return values.at[tuple(place)].set(top_value)


def block_scale(stream_key, dims, shards, smallest, top_value):
    level = 1.0
    for position, blocks in shards:
        heights = jax.random.uniform(jax.random.fold_in(jax.random.fold_in(stream_key, 6), position), (blocks,), jnp.float32, smallest / len(shards), top_value / len(shards))
        level = level * jnp.repeat(jnp.exp(heights), dims[position] // blocks).reshape((-1,) + (1,) * (len(dims) - 1 - position))
    return level


def centred(own_key, shape, spread, most, shards=(), kind=jnp.bfloat16):
    result = jax.random.normal(own_key, shape, jnp.float32) * spread
    if len(shards) > 0:
        result = block_scale(own_key, shape, shards, -0.22, 0.18) * result
    return jnp.clip(result, min=-most, max=most).astype(kind)


def setup_inputs(seed: int = 0) -> dict:
    streams_of = jax.random.split(jax.random.key(seed), 11)
    field = centred(streams_of[0], (S, NX, NY, NZ), 1.0, 6.0, ((1, 16), (2, 16)), jnp.float32)
    rates = jnp.clip(jnp.exp(jax.random.uniform(streams_of[1], (S,), jnp.float32, math.log(0.2), math.log(1.0))), 0.2, 1.0)
    mixing = centred(streams_of[2], (S, S), S ** -0.5, 1.0, (), jnp.float32)
    secretion = centred(streams_of[3], (S, NBX, NBY, BZ * SLOTS), 1.0, 6.0, ((1, 16), (2, 16)), jnp.float32)
    positions = draw_positions(jax.random.fold_in(streams_of[10], 71), 0)
    stiffness = jnp.clip(jnp.exp(math.log(2.0) - 1.3862944 * jax.random.uniform(streams_of[5], (NBX, NBY, BZ * SLOTS), jnp.float32) ** block_scale(streams_of[5], (NBX, NBY, BZ * SLOTS), ((0, 16), (1, 16)), -0.2, 0.2)), 0.5, 2.0)
    occupancy = draw_occupancy(jax.random.fold_in(streams_of[10], 71), 0)
    offsets = plant(jax.random.randint(streams_of[7], (NBX, NBY, BZ * SLOTS), 0, BIN_XY * BIN_XY * BIN_Z), jax.random.fold_in(streams_of[7], 1), 0, (BIN_XY * BIN_XY * BIN_Z) - 1).astype(jnp.int32)
    migrant_state = centred(streams_of[8], (8, STATE * N_GX, MIG * N_GY), 1.0, 6.0, ((1, 16), (2, 16)), jnp.float32)
    migrant_live = plant((jax.random.randint(streams_of[9], (8, N_GX, MIG * N_GY), 0, 2) < 1).astype(jnp.int32), jax.random.fold_in(streams_of[9], 1), 0, 1)
    return {"field": field, "rates": rates, "mixing": mixing, "secretion": secretion, "positions": positions, "stiffness": stiffness, "occupancy": occupancy, "offsets": offsets, "migrant_state": migrant_state, "migrant_live": migrant_live}


time_step = 0.15
move_step = 0.1
spread_sq = 8.0
shifts = ((-1, -1), (-1, 0), (-1, 1), (0, -1), (0, 1), (1, -1), (1, 0), (1, 1))


def advance(padded, source, rates, mixing):
    center = padded[:, 1:-1, 1:-1, :]
    deeper = jnp.pad(center, ((0, 0), (0, 0), (0, 0), (1, 1)))
    beside = padded[:, 2:, 1:-1, :] + padded[:, :-2, 1:-1, :]
    beside = beside + padded[:, 1:-1, 2:, :] + padded[:, 1:-1, :-2, :]
    beside = beside + deeper[:, :, :, 2:] + deeper[:, :, :, :-2]
    laplace = beside - 6.0 * center
    species = center.shape[0]
    mixed = jnp.dot(mixing, center.reshape(species, -1), precision=lax.Precision.HIGHEST).reshape(center.shape)
    return center + time_step * (rates[:, None, None, None] * laplace) + time_step * mixed + time_step * source


def deposit(secretion, occupancy, offsets):
    species, bins_x, bins_y, lanes = secretion.shape
    shape = (bins_x, bins_y, lanes)
    cells_x = bins_x * BIN_XY
    cells_y = bins_y * BIN_XY
    cells_z = (lanes // SLOTS) * BIN_Z
    bin_x = lax.broadcasted_iota(jnp.int32, shape, 0)
    bin_y = lax.broadcasted_iota(jnp.int32, shape, 1)
    bin_z = lax.broadcasted_iota(jnp.int32, shape, 2) // SLOTS
    voxel_x = bin_x * BIN_XY + offsets // (BIN_XY * BIN_Z)
    voxel_y = bin_y * BIN_XY + (offsets // BIN_Z) % BIN_XY
    voxel_z = bin_z * BIN_Z + offsets % BIN_Z
    flat = ((voxel_x * cells_y + voxel_y) * cells_z + voxel_z).reshape(-1).astype(jnp.int32)
    values = (secretion * occupancy.astype(jnp.float32)[None]).reshape(species, -1)
    total = jnp.zeros((species, cells_x * cells_y * cells_z), jnp.float32).at[:, flat].add(values)
    return total.reshape(species, cells_x, cells_y, cells_z)


def pair_forces(points, padded, occupancy):
    planes, bins_x, bins_y, lanes = points.shape
    layers = lanes // SLOTS
    boxed = padded.reshape(planes, bins_x + 2, bins_y + 2, layers, SLOTS)
    boxed = jnp.pad(boxed, ((0, 0), (0, 0), (0, 0), (1, 1), (0, 0)))
    owned = points.reshape(planes, bins_x, bins_y, layers, SLOTS)[:3, :, :, :, :, None]
    force = jnp.zeros((3, bins_x, bins_y, layers, SLOTS), jnp.float32)
    for offset_x in range(3):
        nearby = jnp.concatenate([boxed[:, offset_x:offset_x + bins_x, offset_y:offset_y + bins_y, offset_z:offset_z + layers, :] for offset_y in range(3) for offset_z in range(3)], axis=-1)
        apart = owned - nearby[:3, :, :, :, None, :]
        strength = nearby[3][:, :, :, None, :] * jnp.exp(-jnp.sum(apart * apart, axis=0) / spread_sq)
        force = force + jnp.sum(apart * strength[None], axis=-1)
    active = occupancy.reshape(1, bins_x, bins_y, layers, SLOTS).astype(jnp.float32)
    return (move_step * active * force).reshape(3, bins_x, bins_y, lanes)


def row_forces(points, padded, occupancy, row_index):
    return pair_forces(lax.dynamic_slice_in_dim(points, row_index, 1, 1), lax.dynamic_slice_in_dim(padded, row_index, 3, 1), lax.dynamic_slice_in_dim(occupancy, row_index, 1, 0))


def reference(field, rates, mixing, secretion, positions, stiffness, occupancy, offsets, migrant_state, migrant_live):
    source = deposit(secretion, occupancy, offsets)
    current = field
    for substep in range(SUBSTEPS):
        padded = jnp.pad(current, ((0, 0), (1, 1), (1, 1), (0, 0)))
        current = advance(padded, source, rates, mixing)
    weight = stiffness * occupancy.astype(jnp.float32)
    points = jnp.concatenate([positions, weight[None]], axis=0)
    bordered = jnp.pad(points, ((0, 0), (1, 1), (1, 1), (0, 0)))
    rowwise = lax.map(functools.partial(row_forces, points, bordered, occupancy), jnp.arange(NBX, dtype=jnp.int32))
    displacement = jnp.moveaxis(rowwise[:, :, 0], 0, 1)
    payload = migrant_state.reshape(8, N_GX, STATE, N_GY, MIG) * migrant_live.reshape(8, N_GX, 1, N_GY, MIG).astype(jnp.float32)
    framed = jnp.pad(payload, ((0, 0), (1, 1), (0, 0), (1, 1), (0, 0)))
    pieces = []
    for index in range(8):
        move_x, move_y = shifts[index]
        pieces.append(framed[index, 1 - move_x:1 - move_x + N_GX, :, 1 - move_y:1 - move_y + N_GY, :])
    arrived = jnp.stack(pieces).reshape(migrant_state.shape)
    return current, displacement, arrived
```

```python
import jax
import jax.numpy as jnp
from jax import lax
from jax.sharding import PartitionSpec as P

BIN_XY = 4
BIN_Z = 8
SLOTS = 16
SUBSTEPS = 4


time_step = 0.15
move_step = 0.1
spread_sq = 8.0
shifts = ((-1, -1), (-1, 0), (-1, 1), (0, -1), (0, 1), (1, -1), (1, 0), (1, 1))


def padded_2(cells, sides, width):
    for axis, dim in sides:
        count = lax.axis_size(axis)
        ends = count - 1
        head = lax.slice_in_dim(cells, 0, width, axis=dim)
        tail = lax.slice_in_dim(cells, cells.shape[dim] - width, cells.shape[dim], axis=dim)
        cells = jnp.concatenate(
            [
                lax.ppermute(tail, axis, [(i, (i + 1) % count) for i in range(ends)]),
                cells,
                lax.ppermute(head, axis, [((i + 1) % count, i) for i in range(ends)]),
            ],
            axis=dim,
        )
    return cells


def halos(cells, axis, dim):
    count = lax.axis_size(axis)
    ends = count - 1
    head = lax.slice_in_dim(cells, 0, 1, axis=dim)
    tail = lax.slice_in_dim(cells, cells.shape[dim] - 1, cells.shape[dim], axis=dim)
    low = lax.ppermute(tail, axis, [(i, (i + 1) % count) for i in range(ends)])
    high = lax.ppermute(head, axis, [((i + 1) % count, i) for i in range(ends)])
    return low, high


def framed(cells, x_low, x_high, y_low, y_high):
    species, width, depth, lanes = cells.shape
    corner = jnp.zeros((species, 1, 1, lanes), cells.dtype)
    middle = jnp.concatenate([x_low, cells, x_high], axis=1)
    left = jnp.concatenate([corner, y_low, corner], axis=1)
    right = jnp.concatenate([corner, y_high, corner], axis=1)
    return jnp.concatenate([left, middle, right], axis=2)


def substep(current, source, rates, mixing):
    x_low, x_high = halos(current, "gx", 1)
    y_low, y_high = halos(current, "gy", 2)
    padded = framed(current, x_low, x_high, y_low, y_high)
    return advance(padded, source, rates, mixing)


def shifted(block, axis, distance):
    devices = range(lax.axis_size(axis))
    route = [(i - distance, i) for i in devices if i - distance in devices]
    return lax.ppermute(block, axis, route)


def advance(padded, source, rates, mixing):
    center = padded[:, 1:-1, 1:-1, :]
    deeper = jnp.pad(center, ((0, 0), (0, 0), (0, 0), (1, 1)))
    beside = padded[:, 2:, 1:-1, :] + padded[:, :-2, 1:-1, :]
    beside = beside + padded[:, 1:-1, 2:, :] + padded[:, 1:-1, :-2, :]
    beside = beside + deeper[:, :, :, 2:] + deeper[:, :, :, :-2]
    laplace = beside - 6.0 * center
    species = center.shape[0]
    mixed = jnp.dot(mixing, center.reshape(species, -1), precision=lax.Precision.HIGHEST).reshape(
        center.shape
    )
    return (
        center
        + time_step * (rates[:, None, None, None] * laplace)
        + time_step * mixed
        + time_step * source
    )


def deposit(secretion, occupancy, offsets):
    species, bins_x, bins_y, lanes = secretion.shape
    layers = lanes // SLOTS
    cells = BIN_XY * BIN_XY * BIN_Z
    count = bins_x * bins_y * layers
    rates_slot = secretion.reshape(species, count, SLOTS)
    place = offsets.reshape(count, SLOTS)
    alive = occupancy.reshape(count, SLOTS).astype(jnp.float32)
    voxel_ids = lax.broadcasted_iota(jnp.int32, (count, SLOTS, cells), 2)
    onehot = (place[:, :, None] == voxel_ids).astype(jnp.float32) * alive[:, :, None]
    filled = jnp.einsum("snk,nkc->snc", rates_slot, onehot, precision=lax.Precision.HIGHEST)
    filled = filled.reshape(species, bins_x, bins_y, layers, BIN_XY, BIN_XY, BIN_Z)
    filled = jnp.transpose(filled, (0, 1, 4, 2, 5, 3, 6))
    return filled.reshape(species, bins_x * BIN_XY, bins_y * BIN_XY, layers * BIN_Z)


def pair_forces(points, padded, occupancy):
    planes, bins_x, bins_y, lanes = points.shape
    layers = lanes // SLOTS
    boxed = padded.reshape(planes, bins_x + 2, bins_y + 2, layers, SLOTS)
    boxed = jnp.pad(boxed, ((0, 0), (0, 0), (0, 0), (1, 1), (0, 0)))
    owned = points.reshape(planes, bins_x, bins_y, layers, SLOTS)[:3, :, :, :, :, None]
    force = jnp.zeros((3, bins_x, bins_y, layers, SLOTS), jnp.float32)
    for offset_x in range(3):
        nearby = jnp.concatenate(
            [
                boxed[
                    :,
                    offset_x : offset_x + bins_x,
                    offset_y : offset_y + bins_y,
                    offset_z : offset_z + layers,
                    :,
                ]
                for offset_y in range(3)
                for offset_z in range(3)
            ],
            axis=-1,
        )
        apart = owned - nearby[:3, :, :, :, None, :]
        strength = nearby[3][:, :, :, None, :] * jnp.exp(
            -jnp.sum(apart * apart, axis=0) / spread_sq
        )
        force = force + jnp.sum(apart * strength[None], axis=-1)
    active = occupancy.reshape(1, bins_x, bins_y, layers, SLOTS).astype(jnp.float32)
    return (move_step * active * force).reshape(3, bins_x, bins_y, lanes)


def on_device(
    field,
    rates,
    mixing,
    secretion,
    positions,
    stiffness,
    occupancy,
    offsets,
    migrant_state,
    migrant_live,
):
    weight = stiffness * occupancy.astype(jnp.float32)
    points = jnp.concatenate([positions, weight[None]], axis=0)
    bordered = padded_2(points, (("gx", 1), ("gy", 2)), 1)
    payload = migrant_state * migrant_live.astype(jnp.float32)
    moving = [payload[index] for index in range(8)]
    for stride in (1, -1):
        picked = [index for index in range(8) if shifts[index][0] == stride]
        landed = shifted(jnp.stack([moving[index] for index in picked]), "gx", stride)
        for place, index in enumerate(picked):
            moving[index] = landed[place]
    for stride in (1, -1):
        picked = [index for index in range(8) if shifts[index][1] == stride]
        landed = shifted(jnp.stack([moving[index] for index in picked]), "gy", stride)
        for place, index in enumerate(picked):
            moving[index] = landed[place]
    arrived = jnp.stack(moving)
    source = deposit(secretion, occupancy, offsets)
    current = field
    for _ in range(SUBSTEPS):
        current = substep(current, source, rates, mixing)
    displacement = pair_forces(points, bordered, occupancy)
    return (current, displacement, arrived)


def solution(mesh):
    return jax.shard_map(
        on_device,
        mesh=mesh,
        in_specs=(
            P(None, "gx", "gy", None),
            P(),
            P(),
            P(None, "gx", "gy", None),
            P(None, "gx", "gy", None),
            P("gx", "gy", None),
            P("gx", "gy", None),
            P("gx", "gy", None),
            P(None, "gx", "gy"),
            P(None, "gx", "gy"),
        ),
        out_specs=(P(None, "gx", "gy", None), P(None, "gx", "gy", None), P(None, "gx", "gy")),
        check_vma=False,
    )
```

```python
import jax
import jax.numpy as jnp
from jax import lax
from jax.sharding import PartitionSpec as P

BIN_XY = 4
BIN_Z = 8
SLOTS = 16
SUBSTEPS = 4


time_step = 0.15
move_step = 0.1
spread_sq = 8.0
shifts = ((-1, -1), (-1, 0), (-1, 1), (0, -1), (0, 1), (1, -1), (1, 0), (1, 1))


def padded_2(cells, sides, width):
    for axis, dim in sides:
        count = lax.axis_size(axis)
        ends = count - 1
        head = lax.slice_in_dim(cells, 0, width, axis=dim)
        tail = lax.slice_in_dim(cells, cells.shape[dim] - width, cells.shape[dim], axis=dim)
        cells = jnp.concatenate(
            [
                lax.ppermute(tail, axis, [(i, (i + 1) % count) for i in range(ends)]),
                cells,
                lax.ppermute(head, axis, [((i + 1) % count, i) for i in range(ends)]),
            ],
            axis=dim,
        )
    return cells


def halos(cells, axis, dim):
    count = lax.axis_size(axis)
    ends = count - 1
    head = lax.slice_in_dim(cells, 0, 1, axis=dim)
    tail = lax.slice_in_dim(cells, cells.shape[dim] - 1, cells.shape[dim], axis=dim)
    low = lax.ppermute(tail, axis, [(i, (i + 1) % count) for i in range(ends)])
    high = lax.ppermute(head, axis, [((i + 1) % count, i) for i in range(ends)])
    return low, high


def framed(cells, x_low, x_high, y_low, y_high):
    species, width, depth, lanes = cells.shape
    corner = jnp.zeros((species, 1, 1, lanes), cells.dtype)
    middle = jnp.concatenate([x_low, cells, x_high], axis=1)
    left = jnp.concatenate([corner, y_low, corner], axis=1)
    right = jnp.concatenate([corner, y_high, corner], axis=1)
    return jnp.concatenate([left, middle, right], axis=2)


def substep(current, source, rates, mixing):
    x_low, x_high = halos(current, "gx", 1)
    y_low, y_high = halos(current, "gy", 2)
    padded = framed(current, x_low, x_high, y_low, y_high)
    return advance(padded, source, rates, mixing)


def shifted(block, axis, distance):
    devices = range(lax.axis_size(axis))
    route = [(i - distance, i) for i in devices if i - distance in devices]
    return lax.ppermute(block, axis, route)


def advance(padded, source, rates, mixing):
    center = padded[:, 1:-1, 1:-1, :]
    deeper = jnp.pad(center, ((0, 0), (0, 0), (0, 0), (1, 1)))
    beside = padded[:, 2:, 1:-1, :] + padded[:, :-2, 1:-1, :]
    beside = beside + padded[:, 1:-1, 2:, :] + padded[:, 1:-1, :-2, :]
    beside = beside + deeper[:, :, :, 2:] + deeper[:, :, :, :-2]
    laplace = beside - 6.0 * center
    species = center.shape[0]
    mixed = jnp.dot(mixing, center.reshape(species, -1), precision=lax.Precision.HIGHEST).reshape(
        center.shape
    )
    return (
        center
        + time_step * (rates[:, None, None, None] * laplace)
        + time_step * mixed
        + time_step * source
    )


def deposit(secretion, occupancy, offsets):
    species, bins_x, bins_y, lanes = secretion.shape
    layers = lanes // SLOTS
    cells = BIN_XY * BIN_XY * BIN_Z
    count = bins_x * bins_y * layers
    rates_slot = secretion.reshape(species, count, SLOTS)
    place = offsets.reshape(count, SLOTS)
    alive = occupancy.reshape(count, SLOTS).astype(jnp.float32)
    voxel_ids = lax.broadcasted_iota(jnp.int32, (count, SLOTS, cells), 2)
    onehot = (place[:, :, None] == voxel_ids).astype(jnp.float32) * alive[:, :, None]
    filled = jnp.einsum("snk,nkc->snc", rates_slot, onehot, precision=lax.Precision.HIGHEST)
    filled = filled.reshape(species, bins_x, bins_y, layers, BIN_XY, BIN_XY, BIN_Z)
    filled = jnp.transpose(filled, (0, 1, 4, 2, 5, 3, 6))
    return filled.reshape(species, bins_x * BIN_XY, bins_y * BIN_XY, layers * BIN_Z)


def pair_forces(points, padded, occupancy):
    planes, bins_x, bins_y, lanes = points.shape
    layers = lanes // SLOTS
    boxed = padded.reshape(planes, bins_x + 2, bins_y + 2, layers, SLOTS)
    boxed = jnp.pad(boxed, ((0, 0), (0, 0), (0, 0), (1, 1), (0, 0)))
    owned = points.reshape(planes, bins_x, bins_y, layers, SLOTS)[:3, :, :, :, :, None]
    force = jnp.zeros((3, bins_x, bins_y, layers, SLOTS), jnp.float32)
    for offset_x in range(3):
        nearby = jnp.concatenate(
            [
                boxed[
                    :,
                    offset_x : offset_x + bins_x,
                    offset_y : offset_y + bins_y,
                    offset_z : offset_z + layers,
                    :,
                ]
                for offset_y in range(3)
                for offset_z in range(3)
            ],
            axis=-1,
        )
        apart = owned - nearby[:3, :, :, :, None, :]
        strength = nearby[3][:, :, :, None, :] * jnp.exp(
            -jnp.sum(apart * apart, axis=0) / spread_sq
        )
        force = force + jnp.sum(apart * strength[None], axis=-1)
    active = occupancy.reshape(1, bins_x, bins_y, layers, SLOTS).astype(jnp.float32)
    return (move_step * active * force).reshape(3, bins_x, bins_y, lanes)


def pack(pieces):
    return jnp.concatenate([piece.reshape(-1, 128) for piece in pieces], axis=0)


def unpack(flat, pieces):
    out = []
    row = 0
    for piece in pieces:
        rows = piece.size // 128
        out.append(flat[row : row + rows].reshape(piece.shape))
        row += rows
    return out


def send_pair(axis, upward, downward):
    count = lax.axis_size(axis)
    up = [(i, i + 1) for i in range(count - 1)]
    down = [(i + 1, i) for i in range(count - 1)]
    from_below = unpack(lax.ppermute(pack(upward), axis, up), upward)
    from_above = unpack(lax.ppermute(pack(downward), axis, down), downward)
    return from_below, from_above


def on_device(
    field,
    rates,
    mixing,
    secretion,
    positions,
    stiffness,
    occupancy,
    offsets,
    migrant_state,
    migrant_live,
):
    weight = stiffness * occupancy.astype(jnp.float32)
    points = jnp.concatenate([positions, weight[None]], axis=0)
    payload = migrant_state * migrant_live.astype(jnp.float32)
    source = deposit(secretion, occupancy, offsets)
    current = field

    (x_low, points_low, moved_up), (x_high, points_high, moved_down) = send_pair(
        "gx",
        [current[:, -1:], points, payload[5:8]],
        [current[:, :1], points, payload[0:3]],
    )
    (y_low, beside_up), (y_high, beside_down) = send_pair(
        "gy",
        [current[:, :, -1:], payload[4:5]],
        [current[:, :, :1], payload[3:4]],
    )
    current = advance(framed(current, x_low, x_high, y_low, y_high), source, rates, mixing)

    row_points = jnp.concatenate([points_low, points, points_high], axis=1)
    x_low, x_high = halos(current, "gx", 1)
    (y_low, points_low, corner_up), (y_high, points_high, corner_down) = send_pair(
        "gy",
        [current[:, :, -1:], row_points[:, :, -1:], jnp.stack([moved_down[2], moved_up[2]])],
        [current[:, :, :1], row_points[:, :, :1], jnp.stack([moved_down[0], moved_up[0]])],
    )
    current = advance(framed(current, x_low, x_high, y_low, y_high), source, rates, mixing)
    bordered = jnp.concatenate([points_low, row_points, points_high], axis=2)
    arrived = jnp.stack(
        [
            corner_down[0],
            moved_down[1],
            corner_up[0],
            beside_down[0],
            beside_up[0],
            corner_down[1],
            moved_up[1],
            corner_up[1],
        ]
    )

    for _ in range(SUBSTEPS - 2):
        current = substep(current, source, rates, mixing)
    displacement = pair_forces(points, bordered, occupancy)
    return (current, displacement, arrived)


def solution(mesh):
    return jax.shard_map(
        on_device,
        mesh=mesh,
        in_specs=(
            P(None, "gx", "gy", None),
            P(),
            P(),
            P(None, "gx", "gy", None),
            P(None, "gx", "gy", None),
            P("gx", "gy", None),
            P("gx", "gy", None),
            P("gx", "gy", None),
            P(None, "gx", "gy"),
            P(None, "gx", "gy"),
        ),
        out_specs=(P(None, "gx", "gy", None), P(None, "gx", "gy", None), P(None, "gx", "gy")),
        check_vma=False,
    )
```

```python
import jax
import jax.numpy as jnp
from jax import lax
from jax.experimental import pallas as pl
from jax.experimental.pallas import tpu as pltpu
from jax.sharding import PartitionSpec as P

BIN_XY = 4
BIN_Z = 8
SLOTS = 16
SUBSTEPS = 4


time_step = 0.15
move_step = 0.1
spread_sq = 8.0
shifts = ((-1, -1), (-1, 0), (-1, 1), (0, -1), (0, 1), (1, -1), (1, 0), (1, 1))


def padded_2(cells, sides, width):
    for axis, dim in sides:
        count = lax.axis_size(axis)
        ends = count - 1
        head = lax.slice_in_dim(cells, 0, width, axis=dim)
        tail = lax.slice_in_dim(cells, cells.shape[dim] - width, cells.shape[dim], axis=dim)
        cells = jnp.concatenate(
            [
                lax.ppermute(tail, axis, [(i, (i + 1) % count) for i in range(ends)]),
                cells,
                lax.ppermute(head, axis, [((i + 1) % count, i) for i in range(ends)]),
            ],
            axis=dim,
        )
    return cells


def halos(cells, axis, dim):
    count = lax.axis_size(axis)
    ends = count - 1
    head = lax.slice_in_dim(cells, 0, 1, axis=dim)
    tail = lax.slice_in_dim(cells, cells.shape[dim] - 1, cells.shape[dim], axis=dim)
    low = lax.ppermute(tail, axis, [(i, (i + 1) % count) for i in range(ends)])
    high = lax.ppermute(head, axis, [((i + 1) % count, i) for i in range(ends)])
    return low, high


def framed(cells, x_low, x_high, y_low, y_high):
    species, width, depth, lanes = cells.shape
    corner = jnp.zeros((species, 1, 1, lanes), cells.dtype)
    middle = jnp.concatenate([x_low, cells, x_high], axis=1)
    left = jnp.concatenate([corner, y_low, corner], axis=1)
    right = jnp.concatenate([corner, y_high, corner], axis=1)
    return jnp.concatenate([left, middle, right], axis=2)


def substep(current, source, rates, mixing):
    x_low, x_high = halos(current, "gx", 1)
    y_low, y_high = halos(current, "gy", 2)
    padded = framed(current, x_low, x_high, y_low, y_high)
    return advance(padded, source, rates, mixing)


def shifted(block, axis, distance):
    devices = range(lax.axis_size(axis))
    route = [(i - distance, i) for i in devices if i - distance in devices]
    return lax.ppermute(block, axis, route)


def advance(padded, source, rates, mixing):
    center = padded[:, 1:-1, 1:-1, :]
    deeper = jnp.pad(center, ((0, 0), (0, 0), (0, 0), (1, 1)))
    beside = padded[:, 2:, 1:-1, :] + padded[:, :-2, 1:-1, :]
    beside = beside + padded[:, 1:-1, 2:, :] + padded[:, 1:-1, :-2, :]
    beside = beside + deeper[:, :, :, 2:] + deeper[:, :, :, :-2]
    laplace = beside - 6.0 * center
    species = center.shape[0]
    mixed = jnp.dot(mixing, center.reshape(species, -1), precision=lax.Precision.HIGHEST).reshape(
        center.shape
    )
    return (
        center
        + time_step * (rates[:, None, None, None] * laplace)
        + time_step * mixed
        + time_step * source
    )


def deposit(secretion, occupancy, offsets):
    species, bins_x, bins_y, lanes = secretion.shape
    layers = lanes // SLOTS
    cells = BIN_XY * BIN_XY * BIN_Z
    count = bins_x * bins_y * layers
    rates_slot = secretion.reshape(species, count, SLOTS)
    place = offsets.reshape(count, SLOTS)
    alive = occupancy.reshape(count, SLOTS).astype(jnp.float32)
    voxel_ids = lax.broadcasted_iota(jnp.int32, (count, SLOTS, cells), 2)
    onehot = (place[:, :, None] == voxel_ids).astype(jnp.float32) * alive[:, :, None]
    filled = jnp.einsum("snk,nkc->snc", rates_slot, onehot, precision=lax.Precision.HIGHEST)
    filled = filled.reshape(species, bins_x, bins_y, layers, BIN_XY, BIN_XY, BIN_Z)
    filled = jnp.transpose(filled, (0, 1, 4, 2, 5, 3, 6))
    return filled.reshape(species, bins_x * BIN_XY, bins_y * BIN_XY, layers * BIN_Z)


def pair_forces(points, padded, occupancy):
    planes, bins_x, bins_y, lanes = points.shape
    layers = lanes // SLOTS
    boxed = padded.reshape(planes, bins_x + 2, bins_y + 2, layers, SLOTS)
    boxed = jnp.pad(boxed, ((0, 0), (0, 0), (0, 0), (1, 1), (0, 0)))
    owned = points.reshape(planes, bins_x, bins_y, layers, SLOTS)[:3, :, :, :, :, None]
    force = jnp.zeros((3, bins_x, bins_y, layers, SLOTS), jnp.float32)
    for offset_x in range(3):
        nearby = jnp.concatenate(
            [
                boxed[
                    :,
                    offset_x : offset_x + bins_x,
                    offset_y : offset_y + bins_y,
                    offset_z : offset_z + layers,
                    :,
                ]
                for offset_y in range(3)
                for offset_z in range(3)
            ],
            axis=-1,
        )
        apart = owned - nearby[:3, :, :, :, None, :]
        strength = nearby[3][:, :, :, None, :] * jnp.exp(
            -jnp.sum(apart * apart, axis=0) / spread_sq
        )
        force = force + jnp.sum(apart * strength[None], axis=-1)
    active = occupancy.reshape(1, bins_x, bins_y, layers, SLOTS).astype(jnp.float32)
    return (move_step * active * force).reshape(3, bins_x, bins_y, lanes)


def pack(pieces):
    return jnp.concatenate([piece.reshape(-1, 128) for piece in pieces], axis=0)


def unpack(flat, pieces):
    out = []
    row = 0
    for piece in pieces:
        rows = piece.size // 128
        out.append(flat[row : row + rows].reshape(piece.shape))
        row += rows
    return out


def send_pair(axis, upward, downward):
    count = lax.axis_size(axis)
    up = [(i, i + 1) for i in range(count - 1)]
    down = [(i + 1, i) for i in range(count - 1)]
    from_below = unpack(lax.ppermute(pack(upward), axis, up), upward)
    from_above = unpack(lax.ppermute(pack(downward), axis, down), downward)
    return from_below, from_above


def forces_kernel(own_ref, near_ref, occ_ref, out_ref):
    rows = own_ref.shape[1]
    lanes = own_ref.shape[-1]
    layers = lanes // SLOTS
    px = own_ref[0]
    py = own_ref[1]
    pz = own_ref[2]
    lane = lax.broadcasted_iota(jnp.int32, px.shape, 1)
    slot = lane % SLOTS
    layer = lane // SLOTS

    def body(offset_x, carry):
        fx, fy, fz = carry
        for offset_y in range(3):
            row = [near_ref[plane, offset_x, offset_y : offset_y + rows, :] for plane in range(4)]
            for offset_z in (-1, 0, 1):
                if offset_z == 0:
                    base = row
                else:
                    inside = (layer + offset_z >= 0) & (layer + offset_z < layers)
                    base = [
                        jnp.where(inside, pltpu.roll(part, (-offset_z * SLOTS) % lanes, 1), 0.0)
                        for part in row
                    ]
                for turn in range(SLOTS):
                    if turn == 0:
                        other = base
                    else:
                        keep = slot + turn < SLOTS
                        other = [
                            jnp.where(keep, pltpu.roll(part, lanes - turn, 1), pltpu.roll(part, SLOTS - turn, 1))
                            for part in base
                        ]
                    dx = px - other[0]
                    dy = py - other[1]
                    dz = pz - other[2]
                    strength = other[3] * jnp.exp(-(dx * dx + dy * dy + dz * dz) / spread_sq)
                    fx = fx + dx * strength
                    fy = fy + dy * strength
                    fz = fz + dz * strength
        return fx, fy, fz

    zero = jnp.zeros_like(px)
    fx, fy, fz = lax.fori_loop(0, 3, body, (zero, zero, zero))
    active = move_step * occ_ref[...]
    out_ref[0] = active * fx
    out_ref[1] = active * fy
    out_ref[2] = active * fz


def pallas_forces(points, bordered, occupancy):
    planes, _, rows, lanes = points.shape
    out = pl.pallas_call(
        forces_kernel,
        out_shape=jax.ShapeDtypeStruct((3, rows, lanes), jnp.float32),
        cost_estimate=pl.CostEstimate(flops=9_000_000, transcendentals=450_000, bytes_accessed=120_000),
    )(points[:, 0], bordered, occupancy[0].astype(jnp.float32))
    return out.reshape(3, 1, rows, lanes)


def on_device(
    field,
    rates,
    mixing,
    secretion,
    positions,
    stiffness,
    occupancy,
    offsets,
    migrant_state,
    migrant_live,
):
    weight = stiffness * occupancy.astype(jnp.float32)
    points = jnp.concatenate([positions, weight[None]], axis=0)
    payload = migrant_state * migrant_live.astype(jnp.float32)
    source = deposit(secretion, occupancy, offsets)
    current = field

    (x_low, points_low, moved_up), (x_high, points_high, moved_down) = send_pair(
        "gx",
        [current[:, -1:], points, payload[5:8]],
        [current[:, :1], points, payload[0:3]],
    )
    (y_low, beside_up), (y_high, beside_down) = send_pair(
        "gy",
        [current[:, :, -1:], payload[4:5]],
        [current[:, :, :1], payload[3:4]],
    )
    current = advance(framed(current, x_low, x_high, y_low, y_high), source, rates, mixing)

    row_points = jnp.concatenate([points_low, points, points_high], axis=1)
    x_low, x_high = halos(current, "gx", 1)
    (y_low, points_low, corner_up), (y_high, points_high, corner_down) = send_pair(
        "gy",
        [current[:, :, -1:], row_points[:, :, -1:], jnp.stack([moved_down[2], moved_up[2]])],
        [current[:, :, :1], row_points[:, :, :1], jnp.stack([moved_down[0], moved_up[0]])],
    )
    current = advance(framed(current, x_low, x_high, y_low, y_high), source, rates, mixing)
    bordered = jnp.concatenate([points_low, row_points, points_high], axis=2)
    arrived = jnp.stack(
        [
            corner_down[0],
            moved_down[1],
            corner_up[0],
            beside_down[0],
            beside_up[0],
            corner_down[1],
            moved_up[1],
            corner_up[1],
        ]
    )

    for _ in range(SUBSTEPS - 2):
        current = substep(current, source, rates, mixing)
    displacement = pallas_forces(points, bordered, occupancy)
    return (current, displacement, arrived)


def solution(mesh):
    return jax.shard_map(
        on_device,
        mesh=mesh,
        in_specs=(
            P(None, "gx", "gy", None),
            P(),
            P(),
            P(None, "gx", "gy", None),
            P(None, "gx", "gy", None),
            P("gx", "gy", None),
            P("gx", "gy", None),
            P("gx", "gy", None),
            P(None, "gx", "gy"),
            P(None, "gx", "gy"),
        ),
        out_specs=(P(None, "gx", "gy", None), P(None, "gx", "gy", None), P(None, "gx", "gy")),
        check_vma=False,
    )
```

```python
import functools

import jax
import jax.numpy as jnp
from jax import lax
from jax.experimental import pallas as pl
from jax.experimental.pallas import tpu as pltpu
from jax.sharding import PartitionSpec as P

BIN_XY = 4
BIN_Z = 8
SLOTS = 16
SUBSTEPS = 4


time_step = 0.15
move_step = 0.1
spread_sq = 8.0
shifts = ((-1, -1), (-1, 0), (-1, 1), (0, -1), (0, 1), (1, -1), (1, 0), (1, 1))


def padded_2(cells, sides, width):
    for axis, dim in sides:
        count = lax.axis_size(axis)
        ends = count - 1
        head = lax.slice_in_dim(cells, 0, width, axis=dim)
        tail = lax.slice_in_dim(cells, cells.shape[dim] - width, cells.shape[dim], axis=dim)
        cells = jnp.concatenate(
            [
                lax.ppermute(tail, axis, [(i, (i + 1) % count) for i in range(ends)]),
                cells,
                lax.ppermute(head, axis, [((i + 1) % count, i) for i in range(ends)]),
            ],
            axis=dim,
        )
    return cells


def halos(cells, axis, dim):
    count = lax.axis_size(axis)
    ends = count - 1
    head = lax.slice_in_dim(cells, 0, 1, axis=dim)
    tail = lax.slice_in_dim(cells, cells.shape[dim] - 1, cells.shape[dim], axis=dim)
    low = lax.ppermute(tail, axis, [(i, (i + 1) % count) for i in range(ends)])
    high = lax.ppermute(head, axis, [((i + 1) % count, i) for i in range(ends)])
    return low, high


def framed(cells, x_low, x_high, y_low, y_high):
    species, width, depth, lanes = cells.shape
    corner = jnp.zeros((species, 1, 1, lanes), cells.dtype)
    middle = jnp.concatenate([x_low, cells, x_high], axis=1)
    left = jnp.concatenate([corner, y_low, corner], axis=1)
    right = jnp.concatenate([corner, y_high, corner], axis=1)
    return jnp.concatenate([left, middle, right], axis=2)


def substep(current, source, rates, mixing):
    x_low, x_high = halos(current, "gx", 1)
    y_low, y_high = halos(current, "gy", 2)
    padded = framed(current, x_low, x_high, y_low, y_high)
    return advance(padded, source, rates, mixing)


def shifted(block, axis, distance):
    devices = range(lax.axis_size(axis))
    route = [(i - distance, i) for i in devices if i - distance in devices]
    return lax.ppermute(block, axis, route)


def advance(padded, source, rates, mixing):
    center = padded[:, 1:-1, 1:-1, :]
    deeper = jnp.pad(center, ((0, 0), (0, 0), (0, 0), (1, 1)))
    beside = padded[:, 2:, 1:-1, :] + padded[:, :-2, 1:-1, :]
    beside = beside + padded[:, 1:-1, 2:, :] + padded[:, 1:-1, :-2, :]
    beside = beside + deeper[:, :, :, 2:] + deeper[:, :, :, :-2]
    laplace = beside - 6.0 * center
    species = center.shape[0]
    mixed = jnp.dot(mixing, center.reshape(species, -1), precision=lax.Precision.HIGHEST).reshape(
        center.shape
    )
    return (
        center
        + time_step * (rates[:, None, None, None] * laplace)
        + time_step * mixed
        + time_step * source
    )


def deposit(secretion, occupancy, offsets):
    species, bins_x, bins_y, lanes = secretion.shape
    layers = lanes // SLOTS
    cells = BIN_XY * BIN_XY * BIN_Z
    count = bins_x * bins_y * layers
    rates_slot = secretion.reshape(species, count, SLOTS)
    place = offsets.reshape(count, SLOTS)
    alive = occupancy.reshape(count, SLOTS).astype(jnp.float32)
    voxel_ids = lax.broadcasted_iota(jnp.int32, (count, SLOTS, cells), 2)
    onehot = (place[:, :, None] == voxel_ids).astype(jnp.float32) * alive[:, :, None]
    filled = jnp.einsum("snk,nkc->snc", rates_slot, onehot, precision=lax.Precision.HIGHEST)
    filled = filled.reshape(species, bins_x, bins_y, layers, BIN_XY, BIN_XY, BIN_Z)
    filled = jnp.transpose(filled, (0, 1, 4, 2, 5, 3, 6))
    return filled.reshape(species, bins_x * BIN_XY, bins_y * BIN_XY, layers * BIN_Z)


def pair_forces(points, padded, occupancy):
    planes, bins_x, bins_y, lanes = points.shape
    layers = lanes // SLOTS
    boxed = padded.reshape(planes, bins_x + 2, bins_y + 2, layers, SLOTS)
    boxed = jnp.pad(boxed, ((0, 0), (0, 0), (0, 0), (1, 1), (0, 0)))
    owned = points.reshape(planes, bins_x, bins_y, layers, SLOTS)[:3, :, :, :, :, None]
    force = jnp.zeros((3, bins_x, bins_y, layers, SLOTS), jnp.float32)
    for offset_x in range(3):
        nearby = jnp.concatenate(
            [
                boxed[
                    :,
                    offset_x : offset_x + bins_x,
                    offset_y : offset_y + bins_y,
                    offset_z : offset_z + layers,
                    :,
                ]
                for offset_y in range(3)
                for offset_z in range(3)
            ],
            axis=-1,
        )
        apart = owned - nearby[:3, :, :, :, None, :]
        strength = nearby[3][:, :, :, None, :] * jnp.exp(
            -jnp.sum(apart * apart, axis=0) / spread_sq
        )
        force = force + jnp.sum(apart * strength[None], axis=-1)
    active = occupancy.reshape(1, bins_x, bins_y, layers, SLOTS).astype(jnp.float32)
    return (move_step * active * force).reshape(3, bins_x, bins_y, lanes)


def storage_order(piece):
    if piece.ndim == 4 and piece.shape[0] > 4:
        return (1, 2, 0, 3)
    return tuple(range(piece.ndim))


def pack(pieces):
    return jnp.concatenate(
        [jnp.transpose(piece, storage_order(piece)).reshape(-1, 128) for piece in pieces], axis=0
    )


def unpack(flat, pieces):
    out = []
    row = 0
    for piece in pieces:
        rows = piece.size // 128
        order = storage_order(piece)
        stored = flat[row : row + rows].reshape(tuple(piece.shape[axis] for axis in order))
        out.append(jnp.transpose(stored, tuple(order.index(axis) for axis in range(piece.ndim))))
        row += rows
    return out


def send_pair(axis, upward, downward):
    count = lax.axis_size(axis)
    up = [(i, i + 1) for i in range(count - 1)]
    down = [(i + 1, i) for i in range(count - 1)]
    below = lax.ppermute(pack(upward), axis, up)
    above = lax.ppermute(pack(downward), axis, down)
    return unpack(below, upward), unpack(above, downward), below, above


def forces_kernel(own_ref, near_ref, occ_ref, out_ref):
    rows = own_ref.shape[1]
    lanes = own_ref.shape[-1]
    layers = lanes // SLOTS
    px = own_ref[0]
    py = own_ref[1]
    pz = own_ref[2]
    lane = lax.broadcasted_iota(jnp.int32, px.shape, 1)
    slot = lane % SLOTS
    layer = lane // SLOTS

    def body(offset_x, carry):
        fx, fy, fz = carry
        for offset_y in range(3):
            row = [near_ref[plane, offset_x, offset_y : offset_y + rows, :] for plane in range(4)]
            for offset_z in (-1, 0, 1):
                if offset_z == 0:
                    base = row
                else:
                    inside = (layer + offset_z >= 0) & (layer + offset_z < layers)
                    base = [
                        jnp.where(inside, pltpu.roll(part, (-offset_z * SLOTS) % lanes, 1), 0.0)
                        for part in row
                    ]
                for turn in range(SLOTS):
                    if turn == 0:
                        other = base
                    else:
                        keep = slot + turn < SLOTS
                        other = [
                            jnp.where(keep, pltpu.roll(part, lanes - turn, 1), pltpu.roll(part, SLOTS - turn, 1))
                            for part in base
                        ]
                    dx = px - other[0]
                    dy = py - other[1]
                    dz = pz - other[2]
                    strength = other[3] * jnp.exp(-(dx * dx + dy * dy + dz * dz) / spread_sq)
                    fx = fx + dx * strength
                    fy = fy + dy * strength
                    fz = fz + dz * strength
        return fx, fy, fz

    zero = jnp.zeros_like(px)
    fx, fy, fz = lax.fori_loop(0, 3, body, (zero, zero, zero))
    active = move_step * occ_ref[...]
    out_ref[0] = active * fx
    out_ref[1] = active * fy
    out_ref[2] = active * fz


def pallas_forces(points, bordered, occupancy):
    planes, _, rows, lanes = points.shape
    out = pl.pallas_call(
        forces_kernel,
        out_shape=jax.ShapeDtypeStruct((3, rows, lanes), jnp.float32),
        cost_estimate=pl.CostEstimate(flops=9_000_000, transcendentals=450_000, bytes_accessed=120_000),
    )(points[:, 0], bordered, occupancy[0].astype(jnp.float32))
    return out.reshape(3, 1, rows, lanes)


def arrived_kernel(starts, state, x_below, x_above, side_below, side_above, corner_below, corner_above, out_ref):
    along_x, beside, corner = starts
    span = state

    def rows(ref, first):
        return ref[first : first + span, :]

    out_ref[0] = rows(corner_above, corner)
    out_ref[1] = rows(x_above, along_x + span)
    out_ref[2] = rows(corner_below, corner)
    out_ref[3] = rows(side_above, beside)
    out_ref[4] = rows(side_below, beside)
    out_ref[5] = rows(corner_above, corner + span)
    out_ref[6] = rows(x_below, along_x + span)
    out_ref[7] = rows(corner_below, corner + span)


def gather_arrived(x_flats, side_flats, corner_flats, along_x, beside, corner, shape):
    state, lanes = shape
    return pl.pallas_call(
        functools.partial(arrived_kernel, (along_x, beside, corner), state),
        out_shape=jax.ShapeDtypeStruct((8, state, lanes), jnp.float32),
        cost_estimate=pl.CostEstimate(flops=0, transcendentals=0, bytes_accessed=300_000),
    )(*x_flats, *side_flats, *corner_flats)


def on_device(
    field,
    rates,
    mixing,
    secretion,
    positions,
    stiffness,
    occupancy,
    offsets,
    migrant_state,
    migrant_live,
):
    weight = stiffness * occupancy.astype(jnp.float32)
    points = jnp.concatenate([positions, weight[None]], axis=0)
    payload = migrant_state * migrant_live.astype(jnp.float32)
    source = deposit(secretion, occupancy, offsets)
    current = field

    (x_low, points_low, moved_up), (x_high, points_high, moved_down), *x_flats = send_pair(
        "gx",
        [current[:, -1:], points, payload[5:8]],
        [current[:, :1], points, payload[0:3]],
    )
    (y_low, beside_up), (y_high, beside_down), *side_flats = send_pair(
        "gy",
        [current[:, :, -1:], payload[4:5]],
        [current[:, :, :1], payload[3:4]],
    )
    current = advance(framed(current, x_low, x_high, y_low, y_high), source, rates, mixing)

    row_points = jnp.concatenate([points_low, points, points_high], axis=1)
    x_low, x_high = halos(current, "gx", 1)
    (y_low, points_low, corner_up), (y_high, points_high, corner_down), *corner_flats = send_pair(
        "gy",
        [current[:, :, -1:], row_points[:, :, -1:], jnp.stack([moved_down[2], moved_up[2]])],
        [current[:, :, :1], row_points[:, :, :1], jnp.stack([moved_down[0], moved_up[0]])],
    )
    current = advance(framed(current, x_low, x_high, y_low, y_high), source, rates, mixing)
    bordered = jnp.concatenate([points_low, row_points, points_high], axis=2)
    field_rows = x_low.size // 128
    side_rows = y_low.size // 128
    arrived = gather_arrived(
        x_flats,
        side_flats,
        corner_flats,
        field_rows + points.size // 128,
        side_rows,
        side_rows + points_low.size // 128,
        payload.shape[1:],
    )

    for _ in range(SUBSTEPS - 2):
        current = substep(current, source, rates, mixing)
    displacement = pallas_forces(points, bordered, occupancy)
    return (current, displacement, arrived)


def solution(mesh):
    return jax.shard_map(
        on_device,
        mesh=mesh,
        in_specs=(
            P(None, "gx", "gy", None),
            P(),
            P(),
            P(None, "gx", "gy", None),
            P(None, "gx", "gy", None),
            P("gx", "gy", None),
            P("gx", "gy", None),
            P("gx", "gy", None),
            P(None, "gx", "gy"),
            P(None, "gx", "gy"),
        ),
        out_specs=(P(None, "gx", "gy", None), P(None, "gx", "gy", None), P(None, "gx", "gy")),
        check_vma=False,
    )
```

```python
import functools

import jax
import jax.numpy as jnp
from jax import lax
from jax.experimental import pallas as pl
from jax.experimental.pallas import tpu as pltpu
from jax.sharding import PartitionSpec as P

BIN_XY = 4
BIN_Z = 8
SLOTS = 16
SUBSTEPS = 4


time_step = 0.15
move_step = 0.1
spread_sq = 8.0
shifts = ((-1, -1), (-1, 0), (-1, 1), (0, -1), (0, 1), (1, -1), (1, 0), (1, 1))


def padded_2(cells, sides, width):
    for axis, dim in sides:
        count = lax.axis_size(axis)
        ends = count - 1
        head = lax.slice_in_dim(cells, 0, width, axis=dim)
        tail = lax.slice_in_dim(cells, cells.shape[dim] - width, cells.shape[dim], axis=dim)
        cells = jnp.concatenate(
            [
                lax.ppermute(tail, axis, [(i, (i + 1) % count) for i in range(ends)]),
                cells,
                lax.ppermute(head, axis, [((i + 1) % count, i) for i in range(ends)]),
            ],
            axis=dim,
        )
    return cells


def halos(cells, axis, dim):
    count = lax.axis_size(axis)
    ends = count - 1
    head = lax.slice_in_dim(cells, 0, 1, axis=dim)
    tail = lax.slice_in_dim(cells, cells.shape[dim] - 1, cells.shape[dim], axis=dim)
    low = lax.ppermute(tail, axis, [(i, (i + 1) % count) for i in range(ends)])
    high = lax.ppermute(head, axis, [((i + 1) % count, i) for i in range(ends)])
    return low, high


def framed(cells, x_low, x_high, y_low, y_high):
    species, width, depth, lanes = cells.shape
    corner = jnp.zeros((species, 1, 1, lanes), cells.dtype)
    middle = jnp.concatenate([x_low, cells, x_high], axis=1)
    left = jnp.concatenate([corner, y_low, corner], axis=1)
    right = jnp.concatenate([corner, y_high, corner], axis=1)
    return jnp.concatenate([left, middle, right], axis=2)


def substep(current, source, rates, mixing):
    x_low, x_high = halos(current, "gx", 1)
    y_low, y_high = halos(current, "gy", 2)
    padded = framed(current, x_low, x_high, y_low, y_high)
    return advance(padded, source, rates, mixing)


def shifted(block, axis, distance):
    devices = range(lax.axis_size(axis))
    route = [(i - distance, i) for i in devices if i - distance in devices]
    return lax.ppermute(block, axis, route)


def advance(padded, source, rates, mixing):
    center = padded[:, 1:-1, 1:-1, :]
    deeper = jnp.pad(center, ((0, 0), (0, 0), (0, 0), (1, 1)))
    beside = padded[:, 2:, 1:-1, :] + padded[:, :-2, 1:-1, :]
    beside = beside + padded[:, 1:-1, 2:, :] + padded[:, 1:-1, :-2, :]
    beside = beside + deeper[:, :, :, 2:] + deeper[:, :, :, :-2]
    laplace = beside - 6.0 * center
    species = center.shape[0]
    mixed = jnp.dot(mixing, center.reshape(species, -1), precision=lax.Precision.HIGHEST).reshape(
        center.shape
    )
    return (
        center
        + time_step * (rates[:, None, None, None] * laplace)
        + time_step * mixed
        + time_step * source
    )


def deposit_kernel(rates_ref, code_ref, out_ref, spread_ref, place_ref):
    slots, rows, layers = rates_ref.shape
    bins_y = code_ref.shape[1]
    species = rows // bins_y
    lanes = layers * BIN_Z
    layer_of = lax.broadcasted_iota(jnp.int32, (layers, lanes), 1) // BIN_Z
    expand = (lax.broadcasted_iota(jnp.int32, (layers, lanes), 0) == layer_of).astype(jnp.float32)
    for slot in range(slots):
        spread_ref[slot] = jnp.dot(rates_ref[slot], expand, precision=lax.Precision.HIGHEST, preferred_element_type=jnp.float32)
        place_ref[slot] = jnp.dot(code_ref[slot], expand, precision=lax.Precision.HIGHEST, preferred_element_type=jnp.float32)
    depth = lax.broadcasted_iota(jnp.int32, (1, lanes), 1) % BIN_Z

    def body(index, carry):
        cell_x = index // (bins_y * BIN_XY)
        row_y = index % (bins_y * BIN_XY)
        bin_y = row_y // BIN_XY
        cell_y = row_y % BIN_XY
        target = (depth + (cell_x * (BIN_XY * BIN_Z) + cell_y * BIN_Z)).astype(jnp.float32)
        first = pl.multiple_of(bin_y * species, species)
        total = jnp.zeros((species, lanes), jnp.float32)
        for slot in range(slots):
            hit = place_ref[slot, pl.ds(bin_y, 1), :] == target
            total = total + jnp.where(hit, spread_ref[slot, pl.ds(first, species), :], 0.0)
        out_ref[cell_x, row_y] = total
        return carry

    lax.fori_loop(0, BIN_XY * bins_y * BIN_XY, body, 0)


def deposit(secretion, occupancy, offsets):
    species, bins_x, bins_y, lanes = secretion.shape
    layers = lanes // SLOTS
    rates_slot = secretion.reshape(species, bins_y, layers, SLOTS)
    rates_slot = jnp.transpose(rates_slot, (3, 1, 0, 2)).reshape(SLOTS, bins_y * species, layers)
    code = jnp.where(occupancy != 0, offsets, -1).astype(jnp.float32).reshape(bins_y, layers, SLOTS)
    code = jnp.transpose(code, (2, 0, 1))
    out = pl.pallas_call(
        deposit_kernel,
        out_shape=jax.ShapeDtypeStruct((BIN_XY, bins_y * BIN_XY, species, layers * BIN_Z), jnp.float32),
        scratch_shapes=[
            pltpu.VMEM((SLOTS, bins_y * species, layers * BIN_Z), jnp.float32),
            pltpu.VMEM((SLOTS, bins_y, layers * BIN_Z), jnp.float32),
        ],
        cost_estimate=pl.CostEstimate(flops=10_000_000, transcendentals=0, bytes_accessed=1_300_000),
    )(rates_slot, code)
    return jnp.transpose(out, (2, 0, 1, 3))

def pair_forces(points, padded, occupancy):
    planes, bins_x, bins_y, lanes = points.shape
    layers = lanes // SLOTS
    boxed = padded.reshape(planes, bins_x + 2, bins_y + 2, layers, SLOTS)
    boxed = jnp.pad(boxed, ((0, 0), (0, 0), (0, 0), (1, 1), (0, 0)))
    owned = points.reshape(planes, bins_x, bins_y, layers, SLOTS)[:3, :, :, :, :, None]
    force = jnp.zeros((3, bins_x, bins_y, layers, SLOTS), jnp.float32)
    for offset_x in range(3):
        nearby = jnp.concatenate(
            [
                boxed[
                    :,
                    offset_x : offset_x + bins_x,
                    offset_y : offset_y + bins_y,
                    offset_z : offset_z + layers,
                    :,
                ]
                for offset_y in range(3)
                for offset_z in range(3)
            ],
            axis=-1,
        )
        apart = owned - nearby[:3, :, :, :, None, :]
        strength = nearby[3][:, :, :, None, :] * jnp.exp(
            -jnp.sum(apart * apart, axis=0) / spread_sq
        )
        force = force + jnp.sum(apart * strength[None], axis=-1)
    active = occupancy.reshape(1, bins_x, bins_y, layers, SLOTS).astype(jnp.float32)
    return (move_step * active * force).reshape(3, bins_x, bins_y, lanes)


def storage_order(piece):
    if piece.ndim == 4 and piece.shape[0] > 4:
        return (1, 2, 0, 3)
    return tuple(range(piece.ndim))


def pack(pieces):
    return jnp.concatenate(
        [jnp.transpose(piece, storage_order(piece)).reshape(-1, 128) for piece in pieces], axis=0
    )


def unpack(flat, pieces):
    out = []
    row = 0
    for piece in pieces:
        rows = piece.size // 128
        order = storage_order(piece)
        stored = flat[row : row + rows].reshape(tuple(piece.shape[axis] for axis in order))
        out.append(jnp.transpose(stored, tuple(order.index(axis) for axis in range(piece.ndim))))
        row += rows
    return out


def send_pair(axis, upward, downward):
    count = lax.axis_size(axis)
    up = [(i, i + 1) for i in range(count - 1)]
    down = [(i + 1, i) for i in range(count - 1)]
    below = lax.ppermute(pack(upward), axis, up)
    above = lax.ppermute(pack(downward), axis, down)
    return unpack(below, upward), unpack(above, downward), below, above


def forces_kernel(own_ref, near_ref, occ_ref, out_ref):
    rows = own_ref.shape[1]
    lanes = own_ref.shape[-1]
    layers = lanes // SLOTS
    px = own_ref[0]
    py = own_ref[1]
    pz = own_ref[2]
    lane = lax.broadcasted_iota(jnp.int32, px.shape, 1)
    slot = lane % SLOTS
    layer = lane // SLOTS

    def body(offset_x, carry):
        fx, fy, fz = carry
        for offset_y in range(3):
            row = [near_ref[plane, offset_x, offset_y : offset_y + rows, :] for plane in range(4)]
            for offset_z in (-1, 0, 1):
                if offset_z == 0:
                    base = row
                else:
                    inside = (layer + offset_z >= 0) & (layer + offset_z < layers)
                    base = [
                        jnp.where(inside, pltpu.roll(part, (-offset_z * SLOTS) % lanes, 1), 0.0)
                        for part in row
                    ]
                for turn in range(SLOTS):
                    if turn == 0:
                        other = base
                    else:
                        keep = slot + turn < SLOTS
                        other = [
                            jnp.where(keep, pltpu.roll(part, lanes - turn, 1), pltpu.roll(part, SLOTS - turn, 1))
                            for part in base
                        ]
                    dx = px - other[0]
                    dy = py - other[1]
                    dz = pz - other[2]
                    strength = other[3] * jnp.exp(-(dx * dx + dy * dy + dz * dz) / spread_sq)
                    fx = fx + dx * strength
                    fy = fy + dy * strength
                    fz = fz + dz * strength
        return fx, fy, fz

    zero = jnp.zeros_like(px)
    fx, fy, fz = lax.fori_loop(0, 3, body, (zero, zero, zero))
    active = move_step * occ_ref[...]
    out_ref[0] = active * fx
    out_ref[1] = active * fy
    out_ref[2] = active * fz


def pallas_forces(points, bordered, occupancy):
    planes, _, rows, lanes = points.shape
    out = pl.pallas_call(
        forces_kernel,
        out_shape=jax.ShapeDtypeStruct((3, rows, lanes), jnp.float32),
        cost_estimate=pl.CostEstimate(flops=9_000_000, transcendentals=450_000, bytes_accessed=120_000),
    )(points[:, 0], bordered, occupancy[0].astype(jnp.float32))
    return out.reshape(3, 1, rows, lanes)


def arrived_kernel(starts, state, x_below, x_above, side_below, side_above, corner_below, corner_above, out_ref):
    along_x, beside, corner = starts
    span = state

    def rows(ref, first):
        return ref[first : first + span, :]

    out_ref[0] = rows(corner_above, corner)
    out_ref[1] = rows(x_above, along_x + span)
    out_ref[2] = rows(corner_below, corner)
    out_ref[3] = rows(side_above, beside)
    out_ref[4] = rows(side_below, beside)
    out_ref[5] = rows(corner_above, corner + span)
    out_ref[6] = rows(x_below, along_x + span)
    out_ref[7] = rows(corner_below, corner + span)


def gather_arrived(x_flats, side_flats, corner_flats, along_x, beside, corner, shape):
    state, lanes = shape
    return pl.pallas_call(
        functools.partial(arrived_kernel, (along_x, beside, corner), state),
        out_shape=jax.ShapeDtypeStruct((8, state, lanes), jnp.float32),
        cost_estimate=pl.CostEstimate(flops=0, transcendentals=0, bytes_accessed=300_000),
    )(*x_flats, *side_flats, *corner_flats)


def on_device(
    field,
    rates,
    mixing,
    secretion,
    positions,
    stiffness,
    occupancy,
    offsets,
    migrant_state,
    migrant_live,
):
    weight = stiffness * occupancy.astype(jnp.float32)
    points = jnp.concatenate([positions, weight[None]], axis=0)
    payload = migrant_state * migrant_live.astype(jnp.float32)
    source = deposit(secretion, occupancy, offsets)
    current = field

    (x_low, points_low, moved_up), (x_high, points_high, moved_down), *x_flats = send_pair(
        "gx",
        [current[:, -1:], points, payload[5:8]],
        [current[:, :1], points, payload[0:3]],
    )
    (y_low, beside_up), (y_high, beside_down), *side_flats = send_pair(
        "gy",
        [current[:, :, -1:], payload[4:5]],
        [current[:, :, :1], payload[3:4]],
    )
    current = advance(framed(current, x_low, x_high, y_low, y_high), source, rates, mixing)

    row_points = jnp.concatenate([points_low, points, points_high], axis=1)
    x_low, x_high = halos(current, "gx", 1)
    (y_low, points_low, corner_up), (y_high, points_high, corner_down), *corner_flats = send_pair(
        "gy",
        [current[:, :, -1:], row_points[:, :, -1:], jnp.stack([moved_down[2], moved_up[2]])],
        [current[:, :, :1], row_points[:, :, :1], jnp.stack([moved_down[0], moved_up[0]])],
    )
    current = advance(framed(current, x_low, x_high, y_low, y_high), source, rates, mixing)
    bordered = jnp.concatenate([points_low, row_points, points_high], axis=2)
    field_rows = x_low.size // 128
    side_rows = y_low.size // 128
    arrived = gather_arrived(
        x_flats,
        side_flats,
        corner_flats,
        field_rows + points.size // 128,
        side_rows,
        side_rows + points_low.size // 128,
        payload.shape[1:],
    )

    for _ in range(SUBSTEPS - 2):
        current = substep(current, source, rates, mixing)
    displacement = pallas_forces(points, bordered, occupancy)
    return (current, displacement, arrived)


def solution(mesh):
    return jax.shard_map(
        on_device,
        mesh=mesh,
        in_specs=(
            P(None, "gx", "gy", None),
            P(),
            P(),
            P(None, "gx", "gy", None),
            P(None, "gx", "gy", None),
            P("gx", "gy", None),
            P("gx", "gy", None),
            P("gx", "gy", None),
            P(None, "gx", "gy"),
            P(None, "gx", "gy"),
        ),
        out_specs=(P(None, "gx", "gy", None), P(None, "gx", "gy", None), P(None, "gx", "gy")),
        check_vma=False,
    )
```

```python
import functools

import jax
import jax.numpy as jnp
from jax import lax
from jax.experimental import pallas as pl
from jax.experimental.pallas import tpu as pltpu
from jax.sharding import PartitionSpec as P

BIN_XY = 4
BIN_Z = 8
SLOTS = 16
SUBSTEPS = 4


time_step = 0.15
move_step = 0.1
spread_sq = 8.0
shifts = ((-1, -1), (-1, 0), (-1, 1), (0, -1), (0, 1), (1, -1), (1, 0), (1, 1))


def padded_2(cells, sides, width):
    for axis, dim in sides:
        count = lax.axis_size(axis)
        ends = count - 1
        head = lax.slice_in_dim(cells, 0, width, axis=dim)
        tail = lax.slice_in_dim(cells, cells.shape[dim] - width, cells.shape[dim], axis=dim)
        cells = jnp.concatenate(
            [
                lax.ppermute(tail, axis, [(i, (i + 1) % count) for i in range(ends)]),
                cells,
                lax.ppermute(head, axis, [((i + 1) % count, i) for i in range(ends)]),
            ],
            axis=dim,
        )
    return cells


def halos(cells, axis, dim):
    count = lax.axis_size(axis)
    ends = count - 1
    head = lax.slice_in_dim(cells, 0, 1, axis=dim)
    tail = lax.slice_in_dim(cells, cells.shape[dim] - 1, cells.shape[dim], axis=dim)
    low = lax.ppermute(tail, axis, [(i, (i + 1) % count) for i in range(ends)])
    high = lax.ppermute(head, axis, [((i + 1) % count, i) for i in range(ends)])
    return low, high


def framed(cells, x_low, x_high, y_low, y_high):
    species, width, depth, lanes = cells.shape
    corner = jnp.zeros((species, 1, 1, lanes), cells.dtype)
    middle = jnp.concatenate([x_low, cells, x_high], axis=1)
    left = jnp.concatenate([corner, y_low, corner], axis=1)
    right = jnp.concatenate([corner, y_high, corner], axis=1)
    return jnp.concatenate([left, middle, right], axis=2)


def substep_beside(current, source, rates, mixing, work):
    x_low, x_high = halos(current, "gx", 1)
    y_low, y_high = halos(current, "gy", 2)
    done = work()
    current, done = lax.optimization_barrier((current, done))
    padded = framed(current, x_low, x_high, y_low, y_high)
    return advance(padded, source, rates, mixing), done


def substep(current, source, rates, mixing):
    x_low, x_high = halos(current, "gx", 1)
    y_low, y_high = halos(current, "gy", 2)
    padded = framed(current, x_low, x_high, y_low, y_high)
    return advance(padded, source, rates, mixing)


def shifted(block, axis, distance):
    devices = range(lax.axis_size(axis))
    route = [(i - distance, i) for i in devices if i - distance in devices]
    return lax.ppermute(block, axis, route)


def advance(padded, source, rates, mixing):
    center = padded[:, 1:-1, 1:-1, :]
    deeper = jnp.pad(center, ((0, 0), (0, 0), (0, 0), (1, 1)))
    beside = padded[:, 2:, 1:-1, :] + padded[:, :-2, 1:-1, :]
    beside = beside + padded[:, 1:-1, 2:, :] + padded[:, 1:-1, :-2, :]
    beside = beside + deeper[:, :, :, 2:] + deeper[:, :, :, :-2]
    laplace = beside - 6.0 * center
    species = center.shape[0]
    mixed = jnp.dot(mixing, center.reshape(species, -1), precision=lax.Precision.HIGHEST).reshape(
        center.shape
    )
    return (
        center
        + time_step * (rates[:, None, None, None] * laplace)
        + time_step * mixed
        + time_step * source
    )


def deposit_kernel(rates_ref, code_ref, out_ref, spread_ref, place_ref):
    slots, rows, layers = rates_ref.shape
    bins_y = code_ref.shape[1]
    species = rows // bins_y
    lanes = layers * BIN_Z
    layer_of = lax.broadcasted_iota(jnp.int32, (layers, lanes), 1) // BIN_Z
    expand = (lax.broadcasted_iota(jnp.int32, (layers, lanes), 0) == layer_of).astype(jnp.float32)
    for slot in range(slots):
        spread_ref[slot] = jnp.dot(rates_ref[slot], expand, precision=lax.Precision.HIGHEST, preferred_element_type=jnp.float32)
        place_ref[slot] = jnp.dot(code_ref[slot], expand, precision=lax.Precision.HIGHEST, preferred_element_type=jnp.float32)
    depth = lax.broadcasted_iota(jnp.int32, (1, lanes), 1) % BIN_Z

    def body(index, carry):
        cell_x = index // (bins_y * BIN_XY)
        row_y = index % (bins_y * BIN_XY)
        bin_y = row_y // BIN_XY
        cell_y = row_y % BIN_XY
        target = (depth + (cell_x * (BIN_XY * BIN_Z) + cell_y * BIN_Z)).astype(jnp.float32)
        first = pl.multiple_of(bin_y * species, species)
        total = jnp.zeros((species, lanes), jnp.float32)
        for slot in range(slots):
            hit = place_ref[slot, pl.ds(bin_y, 1), :] == target
            total = total + jnp.where(hit, spread_ref[slot, pl.ds(first, species), :], 0.0)
        out_ref[cell_x, row_y] = total
        return carry

    lax.fori_loop(0, BIN_XY * bins_y * BIN_XY, body, 0)


def deposit(secretion, occupancy, offsets):
    species, bins_x, bins_y, lanes = secretion.shape
    layers = lanes // SLOTS
    rates_slot = secretion.reshape(species, bins_y, layers, SLOTS)
    rates_slot = jnp.transpose(rates_slot, (3, 1, 0, 2)).reshape(SLOTS, bins_y * species, layers)
    code = jnp.where(occupancy != 0, offsets, -1).astype(jnp.float32).reshape(bins_y, layers, SLOTS)
    code = jnp.transpose(code, (2, 0, 1))
    out = pl.pallas_call(
        deposit_kernel,
        out_shape=jax.ShapeDtypeStruct((BIN_XY, bins_y * BIN_XY, species, layers * BIN_Z), jnp.float32),
        scratch_shapes=[
            pltpu.VMEM((SLOTS, bins_y * species, layers * BIN_Z), jnp.float32),
            pltpu.VMEM((SLOTS, bins_y, layers * BIN_Z), jnp.float32),
        ],
        cost_estimate=pl.CostEstimate(flops=10_000_000, transcendentals=0, bytes_accessed=1_300_000),
    )(rates_slot, code)
    return jnp.transpose(out, (2, 0, 1, 3))

def pair_forces(points, padded, occupancy):
    planes, bins_x, bins_y, lanes = points.shape
    layers = lanes // SLOTS
    boxed = padded.reshape(planes, bins_x + 2, bins_y + 2, layers, SLOTS)
    boxed = jnp.pad(boxed, ((0, 0), (0, 0), (0, 0), (1, 1), (0, 0)))
    owned = points.reshape(planes, bins_x, bins_y, layers, SLOTS)[:3, :, :, :, :, None]
    force = jnp.zeros((3, bins_x, bins_y, layers, SLOTS), jnp.float32)
    for offset_x in range(3):
        nearby = jnp.concatenate(
            [
                boxed[
                    :,
                    offset_x : offset_x + bins_x,
                    offset_y : offset_y + bins_y,
                    offset_z : offset_z + layers,
                    :,
                ]
                for offset_y in range(3)
                for offset_z in range(3)
            ],
            axis=-1,
        )
        apart = owned - nearby[:3, :, :, :, None, :]
        strength = nearby[3][:, :, :, None, :] * jnp.exp(
            -jnp.sum(apart * apart, axis=0) / spread_sq
        )
        force = force + jnp.sum(apart * strength[None], axis=-1)
    active = occupancy.reshape(1, bins_x, bins_y, layers, SLOTS).astype(jnp.float32)
    return (move_step * active * force).reshape(3, bins_x, bins_y, lanes)


def storage_order(piece):
    if piece.ndim == 4 and piece.shape[0] > 4:
        return (1, 2, 0, 3)
    return tuple(range(piece.ndim))


def pack(pieces):
    return jnp.concatenate(
        [jnp.transpose(piece, storage_order(piece)).reshape(-1, 128) for piece in pieces], axis=0
    )


def unpack(flat, pieces):
    out = []
    row = 0
    for piece in pieces:
        rows = piece.size // 128
        order = storage_order(piece)
        stored = flat[row : row + rows].reshape(tuple(piece.shape[axis] for axis in order))
        out.append(jnp.transpose(stored, tuple(order.index(axis) for axis in range(piece.ndim))))
        row += rows
    return out


def send_pair(axis, upward, downward):
    count = lax.axis_size(axis)
    up = [(i, i + 1) for i in range(count - 1)]
    down = [(i + 1, i) for i in range(count - 1)]
    below = lax.ppermute(pack(upward), axis, up)
    above = lax.ppermute(pack(downward), axis, down)
    return unpack(below, upward), unpack(above, downward), below, above


def forces_kernel(span, scale, own_ref, near_ref, occ_ref, start_ref, out_ref):
    rows = own_ref.shape[1]
    lanes = own_ref.shape[-1]
    layers = lanes // SLOTS
    px = own_ref[0]
    py = own_ref[1]
    pz = own_ref[2]
    lane = lax.broadcasted_iota(jnp.int32, px.shape, 1)
    slot = lane % SLOTS
    layer = lane // SLOTS

    def body(offset_x, carry):
        fx, fy, fz = carry
        for offset_y in range(3):
            row = [near_ref[plane, offset_x, offset_y : offset_y + rows, :] for plane in range(4)]
            for offset_z in (-1, 0, 1):
                if offset_z == 0:
                    base = row
                else:
                    inside = (layer + offset_z >= 0) & (layer + offset_z < layers)
                    base = [
                        jnp.where(inside, pltpu.roll(part, (-offset_z * SLOTS) % lanes, 1), 0.0)
                        for part in row
                    ]
                for turn in range(SLOTS):
                    if turn == 0:
                        other = base
                    else:
                        keep = slot + turn < SLOTS
                        other = [
                            jnp.where(keep, pltpu.roll(part, lanes - turn, 1), pltpu.roll(part, SLOTS - turn, 1))
                            for part in base
                        ]
                    dx = px - other[0]
                    dy = py - other[1]
                    dz = pz - other[2]
                    strength = other[3] * jnp.exp(-(dx * dx + dy * dy + dz * dz) / spread_sq)
                    fx = fx + dx * strength
                    fy = fy + dy * strength
                    fz = fz + dz * strength
        return fx, fy, fz

    fx, fy, fz = lax.fori_loop(span[0], span[1], body, (start_ref[0], start_ref[1], start_ref[2]))
    if scale:
        active = move_step * occ_ref[...]
        fx = active * fx
        fy = active * fy
        fz = active * fz
    out_ref[0] = fx
    out_ref[1] = fy
    out_ref[2] = fz


def pallas_forces(points, bordered, occupancy, partial, span, scale):
    planes, _, rows, lanes = points.shape
    share = span[1] - span[0]
    return pl.pallas_call(
        functools.partial(forces_kernel, span, scale),
        out_shape=jax.ShapeDtypeStruct((3, rows, lanes), jnp.float32),
        cost_estimate=pl.CostEstimate(
            flops=3_000_000 * share, transcendentals=150_000 * share, bytes_accessed=120_000
        ),
    )(points[:, 0], bordered, occupancy[0].astype(jnp.float32), partial)


def arrived_kernel(starts, state, x_below, x_above, side_below, side_above, corner_below, corner_above, out_ref):
    along_x, beside, corner = starts
    span = state

    def rows(ref, first):
        return ref[first : first + span, :]

    out_ref[0] = rows(corner_above, corner)
    out_ref[1] = rows(x_above, along_x + span)
    out_ref[2] = rows(corner_below, corner)
    out_ref[3] = rows(side_above, beside)
    out_ref[4] = rows(side_below, beside)
    out_ref[5] = rows(corner_above, corner + span)
    out_ref[6] = rows(x_below, along_x + span)
    out_ref[7] = rows(corner_below, corner + span)


def gather_arrived(x_flats, side_flats, corner_flats, along_x, beside, corner, shape):
    state, lanes = shape
    return pl.pallas_call(
        functools.partial(arrived_kernel, (along_x, beside, corner), state),
        out_shape=jax.ShapeDtypeStruct((8, state, lanes), jnp.float32),
        cost_estimate=pl.CostEstimate(flops=0, transcendentals=0, bytes_accessed=300_000),
    )(*x_flats, *side_flats, *corner_flats)


def on_device(
    field,
    rates,
    mixing,
    secretion,
    positions,
    stiffness,
    occupancy,
    offsets,
    migrant_state,
    migrant_live,
):
    weight = stiffness * occupancy.astype(jnp.float32)
    points = jnp.concatenate([positions, weight[None]], axis=0)
    payload = migrant_state * migrant_live.astype(jnp.float32)
    source = deposit(secretion, occupancy, offsets)
    current = field

    (x_low, points_low, moved_up), (x_high, points_high, moved_down), *x_flats = send_pair(
        "gx",
        [current[:, -1:], points, payload[5:8]],
        [current[:, :1], points, payload[0:3]],
    )
    (y_low, beside_up), (y_high, beside_down), *side_flats = send_pair(
        "gy",
        [current[:, :, -1:], payload[4:5]],
        [current[:, :, :1], payload[3:4]],
    )
    current = advance(framed(current, x_low, x_high, y_low, y_high), source, rates, mixing)

    row_points = jnp.concatenate([points_low, points, points_high], axis=1)
    x_low, x_high = halos(current, "gx", 1)
    (y_low, points_low, corner_up), (y_high, points_high, corner_down), *corner_flats = send_pair(
        "gy",
        [current[:, :, -1:], row_points[:, :, -1:], jnp.stack([moved_down[2], moved_up[2]])],
        [current[:, :, :1], row_points[:, :, :1], jnp.stack([moved_down[0], moved_up[0]])],
    )
    current = advance(framed(current, x_low, x_high, y_low, y_high), source, rates, mixing)
    bordered = jnp.concatenate([points_low, row_points, points_high], axis=2)
    field_rows = x_low.size // 128
    side_rows = y_low.size // 128
    starts = (field_rows + points.size // 128, side_rows, side_rows + points_low.size // 128)
    current, bordered, x_flats, side_flats, corner_flats = lax.optimization_barrier(
        (current, bordered, x_flats, side_flats, corner_flats)
    )
    rows = points.shape[2]
    zero = jnp.zeros((3, rows, points.shape[3]), jnp.float32)

    def first_work():
        arrived = gather_arrived(x_flats, side_flats, corner_flats, *starts, payload.shape[1:])
        return arrived, pallas_forces(points, bordered, occupancy, zero, (0, 2), False)

    current, (arrived, partial) = substep_beside(current, source, rates, mixing, first_work)
    current, partial = lax.optimization_barrier((current, partial))

    def second_work():
        return pallas_forces(points, bordered, occupancy, partial, (2, 3), True)

    current, force = substep_beside(current, source, rates, mixing, second_work)
    displacement = force.reshape(3, 1, rows, points.shape[3])
    return (current, displacement, arrived)


def solution(mesh):
    return jax.shard_map(
        on_device,
        mesh=mesh,
        in_specs=(
            P(None, "gx", "gy", None),
            P(),
            P(),
            P(None, "gx", "gy", None),
            P(None, "gx", "gy", None),
            P("gx", "gy", None),
            P("gx", "gy", None),
            P("gx", "gy", None),
            P(None, "gx", "gy"),
            P(None, "gx", "gy"),
        ),
        out_specs=(P(None, "gx", "gy", None), P(None, "gx", "gy", None), P(None, "gx", "gy")),
        check_vma=False,
    )
```

```python
import functools

import jax
import jax.numpy as jnp
from jax import lax
from jax.experimental import pallas as pl
from jax.experimental.pallas import tpu as pltpu
from jax.sharding import PartitionSpec as P

BIN_XY = 4
BIN_Z = 8
SLOTS = 16
SUBSTEPS = 4


time_step = 0.15
move_step = 0.1
spread_sq = 8.0
shifts = ((-1, -1), (-1, 0), (-1, 1), (0, -1), (0, 1), (1, -1), (1, 0), (1, 1))


def padded_2(cells, sides, width):
    for axis, dim in sides:
        count = lax.axis_size(axis)
        ends = count - 1
        head = lax.slice_in_dim(cells, 0, width, axis=dim)
        tail = lax.slice_in_dim(cells, cells.shape[dim] - width, cells.shape[dim], axis=dim)
        cells = jnp.concatenate(
            [
                lax.ppermute(tail, axis, [(i, (i + 1) % count) for i in range(ends)]),
                cells,
                lax.ppermute(head, axis, [((i + 1) % count, i) for i in range(ends)]),
            ],
            axis=dim,
        )
    return cells


def halos(cells, axis, dim):
    count = lax.axis_size(axis)
    ends = count - 1
    head = lax.slice_in_dim(cells, 0, 1, axis=dim)
    tail = lax.slice_in_dim(cells, cells.shape[dim] - 1, cells.shape[dim], axis=dim)
    low = lax.ppermute(tail, axis, [(i, (i + 1) % count) for i in range(ends)])
    high = lax.ppermute(head, axis, [((i + 1) % count, i) for i in range(ends)])
    return low, high


def framed(cells, x_low, x_high, y_low, y_high):
    species, width, depth, lanes = cells.shape
    corner = jnp.zeros((species, 1, 1, lanes), cells.dtype)
    middle = jnp.concatenate([x_low, cells, x_high], axis=1)
    left = jnp.concatenate([corner, y_low, corner], axis=1)
    right = jnp.concatenate([corner, y_high, corner], axis=1)
    return jnp.concatenate([left, middle, right], axis=2)


def substep_beside(current, source, rates, mixing, work):
    x_low, x_high = halos(current, "gx", 1)
    y_low, y_high = halos(current, "gy", 2)
    done = work()
    current, done = lax.optimization_barrier((current, done))
    padded = framed(current, x_low, x_high, y_low, y_high)
    return advance(padded, source, rates, mixing), done


def substep(current, source, rates, mixing):
    x_low, x_high = halos(current, "gx", 1)
    y_low, y_high = halos(current, "gy", 2)
    padded = framed(current, x_low, x_high, y_low, y_high)
    return advance(padded, source, rates, mixing)


def shifted(block, axis, distance):
    devices = range(lax.axis_size(axis))
    route = [(i - distance, i) for i in devices if i - distance in devices]
    return lax.ppermute(block, axis, route)


def advance(padded, source, rates, mixing):
    center = padded[:, 1:-1, 1:-1, :]
    deeper = jnp.pad(center, ((0, 0), (0, 0), (0, 0), (1, 1)))
    beside = padded[:, 2:, 1:-1, :] + padded[:, :-2, 1:-1, :]
    beside = beside + padded[:, 1:-1, 2:, :] + padded[:, 1:-1, :-2, :]
    beside = beside + deeper[:, :, :, 2:] + deeper[:, :, :, :-2]
    laplace = beside - 6.0 * center
    species = center.shape[0]
    mixed = jnp.dot(mixing, center.reshape(species, -1), precision=lax.Precision.HIGHEST).reshape(
        center.shape
    )
    return (
        center
        + time_step * (rates[:, None, None, None] * laplace)
        + time_step * mixed
        + time_step * source
    )


def deposit_kernel(rates_ref, code_ref, out_ref, spread_ref, place_ref):
    slots, rows, layers = rates_ref.shape
    bins_y = code_ref.shape[1]
    species = rows // bins_y
    lanes = layers * BIN_Z
    layer_of = lax.broadcasted_iota(jnp.int32, (layers, lanes), 1) // BIN_Z
    expand = (lax.broadcasted_iota(jnp.int32, (layers, lanes), 0) == layer_of).astype(jnp.float32)
    for slot in range(slots):
        spread_ref[slot] = jnp.dot(rates_ref[slot], expand, precision=lax.Precision.HIGHEST, preferred_element_type=jnp.float32)
        place_ref[slot] = jnp.dot(code_ref[slot], expand, precision=lax.Precision.HIGHEST, preferred_element_type=jnp.float32)
    depth = lax.broadcasted_iota(jnp.int32, (1, lanes), 1) % BIN_Z

    def body(index, carry):
        cell_x = index // (bins_y * BIN_XY)
        row_y = index % (bins_y * BIN_XY)
        bin_y = row_y // BIN_XY
        cell_y = row_y % BIN_XY
        target = (depth + (cell_x * (BIN_XY * BIN_Z) + cell_y * BIN_Z)).astype(jnp.float32)
        first = pl.multiple_of(bin_y * species, species)
        total = jnp.zeros((species, lanes), jnp.float32)
        for slot in range(slots):
            hit = place_ref[slot, pl.ds(bin_y, 1), :] == target
            total = total + jnp.where(hit, spread_ref[slot, pl.ds(first, species), :], 0.0)
        out_ref[cell_x, row_y] = total
        return carry

    lax.fori_loop(0, BIN_XY * bins_y * BIN_XY, body, 0)


def deposit(secretion, occupancy, offsets):
    species, bins_x, bins_y, lanes = secretion.shape
    layers = lanes // SLOTS
    rates_slot = secretion.reshape(species, bins_y, layers, SLOTS)
    rates_slot = jnp.transpose(rates_slot, (3, 1, 0, 2)).reshape(SLOTS, bins_y * species, layers)
    code = jnp.where(occupancy != 0, offsets, -1).astype(jnp.float32).reshape(bins_y, layers, SLOTS)
    code = jnp.transpose(code, (2, 0, 1))
    out = pl.pallas_call(
        deposit_kernel,
        out_shape=jax.ShapeDtypeStruct((BIN_XY, bins_y * BIN_XY, species, layers * BIN_Z), jnp.float32),
        scratch_shapes=[
            pltpu.VMEM((SLOTS, bins_y * species, layers * BIN_Z), jnp.float32),
            pltpu.VMEM((SLOTS, bins_y, layers * BIN_Z), jnp.float32),
        ],
        cost_estimate=pl.CostEstimate(flops=10_000_000, transcendentals=0, bytes_accessed=1_300_000),
    )(rates_slot, code)
    return jnp.transpose(out, (2, 0, 1, 3))

def pair_forces(points, padded, occupancy):
    planes, bins_x, bins_y, lanes = points.shape
    layers = lanes // SLOTS
    boxed = padded.reshape(planes, bins_x + 2, bins_y + 2, layers, SLOTS)
    boxed = jnp.pad(boxed, ((0, 0), (0, 0), (0, 0), (1, 1), (0, 0)))
    owned = points.reshape(planes, bins_x, bins_y, layers, SLOTS)[:3, :, :, :, :, None]
    force = jnp.zeros((3, bins_x, bins_y, layers, SLOTS), jnp.float32)
    for offset_x in range(3):
        nearby = jnp.concatenate(
            [
                boxed[
                    :,
                    offset_x : offset_x + bins_x,
                    offset_y : offset_y + bins_y,
                    offset_z : offset_z + layers,
                    :,
                ]
                for offset_y in range(3)
                for offset_z in range(3)
            ],
            axis=-1,
        )
        apart = owned - nearby[:3, :, :, :, None, :]
        strength = nearby[3][:, :, :, None, :] * jnp.exp(
            -jnp.sum(apart * apart, axis=0) / spread_sq
        )
        force = force + jnp.sum(apart * strength[None], axis=-1)
    active = occupancy.reshape(1, bins_x, bins_y, layers, SLOTS).astype(jnp.float32)
    return (move_step * active * force).reshape(3, bins_x, bins_y, lanes)


def storage_order(piece):
    if piece.ndim == 4 and piece.shape[0] > 4:
        return (1, 2, 0, 3)
    return tuple(range(piece.ndim))


def pack(pieces):
    return jnp.concatenate(
        [jnp.transpose(piece, storage_order(piece)).reshape(-1, 128) for piece in pieces], axis=0
    )


def unpack(flat, pieces):
    out = []
    row = 0
    for piece in pieces:
        rows = piece.size // 128
        order = storage_order(piece)
        stored = flat[row : row + rows].reshape(tuple(piece.shape[axis] for axis in order))
        out.append(jnp.transpose(stored, tuple(order.index(axis) for axis in range(piece.ndim))))
        row += rows
    return out


def send_pair(axis, upward, downward):
    count = lax.axis_size(axis)
    up = [(i, i + 1) for i in range(count - 1)]
    down = [(i + 1, i) for i in range(count - 1)]
    below = lax.ppermute(pack(upward), axis, up)
    above = lax.ppermute(pack(downward), axis, down)
    return unpack(below, upward), unpack(above, downward), below, above


def forces_kernel(span, scale, own_ref, near_ref, occ_ref, start_ref, out_ref):
    rows = own_ref.shape[1]
    lanes = own_ref.shape[-1]
    layers = lanes // SLOTS
    px = own_ref[0]
    py = own_ref[1]
    pz = own_ref[2]
    lane = lax.broadcasted_iota(jnp.int32, px.shape, 1)
    slot = lane % SLOTS
    layer = lane // SLOTS

    def body(offset_x, carry):
        fx, fy, fz = carry
        for offset_y in range(3):
            row = [near_ref[plane, offset_x, offset_y : offset_y + rows, :] for plane in range(4)]
            for offset_z in (-1, 0, 1):
                if offset_z == 0:
                    base = row
                else:
                    inside = (layer + offset_z >= 0) & (layer + offset_z < layers)
                    base = [
                        jnp.where(inside, pltpu.roll(part, (-offset_z * SLOTS) % lanes, 1), 0.0)
                        for part in row
                    ]
                for turn in range(SLOTS):
                    if turn == 0:
                        other = base
                    else:
                        keep = slot + turn < SLOTS
                        other = [
                            jnp.where(keep, pltpu.roll(part, lanes - turn, 1), pltpu.roll(part, SLOTS - turn, 1))
                            for part in base
                        ]
                    dx = px - other[0]
                    dy = py - other[1]
                    dz = pz - other[2]
                    strength = other[3] * jnp.exp(-(dx * dx + dy * dy + dz * dz) / spread_sq)
                    fx = fx + dx * strength
                    fy = fy + dy * strength
                    fz = fz + dz * strength
        return fx, fy, fz

    fx, fy, fz = lax.fori_loop(span[0], span[1], body, (start_ref[0], start_ref[1], start_ref[2]))
    if scale:
        active = move_step * occ_ref[...]
        fx = active * fx
        fy = active * fy
        fz = active * fz
    out_ref[0] = fx
    out_ref[1] = fy
    out_ref[2] = fz


def pallas_forces(points, bordered, occupancy, partial, span, scale):
    planes, _, rows, lanes = points.shape
    share = span[1] - span[0]
    return pl.pallas_call(
        functools.partial(forces_kernel, span, scale),
        out_shape=jax.ShapeDtypeStruct((3, rows, lanes), jnp.float32),
        cost_estimate=pl.CostEstimate(
            flops=3_000_000 * share, transcendentals=150_000 * share, bytes_accessed=120_000
        ),
    )(points[:, 0], bordered, occupancy[0].astype(jnp.float32), partial)


def arrived_kernel(starts, state, x_below, x_above, side_below, side_above, corner_below, corner_above, out_ref):
    along_x, beside, corner = starts
    span = state

    def rows(ref, first):
        return ref[first : first + span, :]

    out_ref[0] = rows(corner_above, corner)
    out_ref[1] = rows(x_above, along_x + span)
    out_ref[2] = rows(corner_below, corner)
    out_ref[3] = rows(side_above, beside)
    out_ref[4] = rows(side_below, beside)
    out_ref[5] = rows(corner_above, corner + span)
    out_ref[6] = rows(x_below, along_x + span)
    out_ref[7] = rows(corner_below, corner + span)


def gather_arrived(x_flats, side_flats, corner_flats, along_x, beside, corner, shape):
    state, lanes = shape
    return pl.pallas_call(
        functools.partial(arrived_kernel, (along_x, beside, corner), state),
        out_shape=jax.ShapeDtypeStruct((8, state, lanes), jnp.float32),
        cost_estimate=pl.CostEstimate(flops=0, transcendentals=0, bytes_accessed=300_000),
    )(*x_flats, *side_flats, *corner_flats)


def on_device(
    field,
    rates,
    mixing,
    secretion,
    positions,
    stiffness,
    occupancy,
    offsets,
    migrant_state,
    migrant_live,
):
    weight = stiffness * occupancy.astype(jnp.float32)
    points = jnp.concatenate([positions, weight[None]], axis=0)
    payload = migrant_state * migrant_live.astype(jnp.float32)
    source = deposit(secretion, occupancy, offsets)
    current = field

    (x_low, points_low, moved_up), (x_high, points_high, moved_down), *x_flats = send_pair(
        "gx",
        [current[:, -1:], points, payload[5:8]],
        [current[:, :1], points, payload[0:3]],
    )
    (y_low, beside_up), (y_high, beside_down), *side_flats = send_pair(
        "gy",
        [current[:, :, -1:], payload[4:5]],
        [current[:, :, :1], payload[3:4]],
    )
    current = advance(framed(current, x_low, x_high, y_low, y_high), source, rates, mixing)

    row_points = jnp.concatenate([points_low, points, points_high], axis=1)
    x_low, x_high = halos(current, "gx", 1)
    (y_low, points_low, corner_up), (y_high, points_high, corner_down), *corner_flats = send_pair(
        "gy",
        [current[:, :, -1:], row_points[:, :, -1:], jnp.stack([moved_down[2], moved_up[2]])],
        [current[:, :, :1], row_points[:, :, :1], jnp.stack([moved_down[0], moved_up[0]])],
    )
    bordered = jnp.concatenate([points_low, row_points, points_high], axis=2)
    field_rows = x_low.size // 128
    side_rows = y_low.size // 128
    starts = (field_rows + points.size // 128, side_rows, side_rows + points_low.size // 128)
    rows = points.shape[2]
    zero = jnp.zeros((3, rows, points.shape[3]), jnp.float32)
    arrived = gather_arrived(x_flats, side_flats, corner_flats, *starts, payload.shape[1:])
    partial = pallas_forces(points, bordered, occupancy, zero, (0, 2), False)
    current, arrived, partial = lax.optimization_barrier((current, arrived, partial))
    current = advance(framed(current, x_low, x_high, y_low, y_high), source, rates, mixing)
    current, bordered, partial = lax.optimization_barrier((current, bordered, partial))

    def later_work():
        return pallas_forces(points, bordered, occupancy, partial, (2, 3), True)

    current, force = substep_beside(current, source, rates, mixing, later_work)
    current = substep(current, source, rates, mixing)
    displacement = force.reshape(3, 1, rows, points.shape[3])
    return (current, displacement, arrived)


def solution(mesh):
    return jax.shard_map(
        on_device,
        mesh=mesh,
        in_specs=(
            P(None, "gx", "gy", None),
            P(),
            P(),
            P(None, "gx", "gy", None),
            P(None, "gx", "gy", None),
            P("gx", "gy", None),
            P("gx", "gy", None),
            P("gx", "gy", None),
            P(None, "gx", "gy"),
            P(None, "gx", "gy"),
        ),
        out_specs=(P(None, "gx", "gy", None), P(None, "gx", "gy", None), P(None, "gx", "gy")),
        check_vma=False,
    )
```

```python
import functools

import jax
import jax.numpy as jnp
from jax import lax
from jax.experimental import pallas as pl
from jax.experimental.pallas import tpu as pltpu
from jax.sharding import PartitionSpec as P

BIN_XY = 4
BIN_Z = 8
SLOTS = 16
SUBSTEPS = 4


time_step = 0.15
move_step = 0.1
spread_sq = 8.0
shifts = ((-1, -1), (-1, 0), (-1, 1), (0, -1), (0, 1), (1, -1), (1, 0), (1, 1))


def padded_2(cells, sides, width):
    for axis, dim in sides:
        count = lax.axis_size(axis)
        ends = count - 1
        head = lax.slice_in_dim(cells, 0, width, axis=dim)
        tail = lax.slice_in_dim(cells, cells.shape[dim] - width, cells.shape[dim], axis=dim)
        cells = jnp.concatenate(
            [
                lax.ppermute(tail, axis, [(i, (i + 1) % count) for i in range(ends)]),
                cells,
                lax.ppermute(head, axis, [((i + 1) % count, i) for i in range(ends)]),
            ],
            axis=dim,
        )
    return cells


def halos(cells, axis, dim):
    count = lax.axis_size(axis)
    ends = count - 1
    head = lax.slice_in_dim(cells, 0, 1, axis=dim)
    tail = lax.slice_in_dim(cells, cells.shape[dim] - 1, cells.shape[dim], axis=dim)
    low = lax.ppermute(tail, axis, [(i, (i + 1) % count) for i in range(ends)])
    high = lax.ppermute(head, axis, [((i + 1) % count, i) for i in range(ends)])
    return low, high


def framed(cells, x_low, x_high, y_low, y_high):
    species, width, depth, lanes = cells.shape
    corner = jnp.zeros((species, 1, 1, lanes), cells.dtype)
    middle = jnp.concatenate([x_low, cells, x_high], axis=1)
    left = jnp.concatenate([corner, y_low, corner], axis=1)
    right = jnp.concatenate([corner, y_high, corner], axis=1)
    return jnp.concatenate([left, middle, right], axis=2)


def substep_beside(current, source, rates, mixing, work):
    x_low, x_high = halos(current, "gx", 1)
    y_low, y_high = halos(current, "gy", 2)
    done = work()
    current, done = lax.optimization_barrier((current, done))
    padded = framed(current, x_low, x_high, y_low, y_high)
    return advance(padded, source, rates, mixing), done


def substep(current, source, rates, mixing):
    x_low, x_high = halos(current, "gx", 1)
    y_low, y_high = halos(current, "gy", 2)
    padded = framed(current, x_low, x_high, y_low, y_high)
    return advance(padded, source, rates, mixing)


def shifted(block, axis, distance):
    devices = range(lax.axis_size(axis))
    route = [(i - distance, i) for i in devices if i - distance in devices]
    return lax.ppermute(block, axis, route)


def advance(padded, source, rates, mixing):
    center = padded[:, 1:-1, 1:-1, :]
    deeper = jnp.pad(center, ((0, 0), (0, 0), (0, 0), (1, 1)))
    beside = padded[:, 2:, 1:-1, :] + padded[:, :-2, 1:-1, :]
    beside = beside + padded[:, 1:-1, 2:, :] + padded[:, 1:-1, :-2, :]
    beside = beside + deeper[:, :, :, 2:] + deeper[:, :, :, :-2]
    laplace = beside - 6.0 * center
    species = center.shape[0]
    mixed = jnp.dot(mixing, center.reshape(species, -1), precision=lax.Precision.HIGHEST).reshape(
        center.shape
    )
    return (
        center
        + time_step * (rates[:, None, None, None] * laplace)
        + time_step * mixed
        + time_step * source
    )


def deposit_kernel(rates_ref, code_ref, out_ref, spread_ref, place_ref):
    slots, rows, layers = rates_ref.shape
    bins_y = code_ref.shape[1]
    species = rows // bins_y
    lanes = layers * BIN_Z
    layer_of = lax.broadcasted_iota(jnp.int32, (layers, lanes), 1) // BIN_Z
    expand = (lax.broadcasted_iota(jnp.int32, (layers, lanes), 0) == layer_of).astype(jnp.float32)
    for slot in range(slots):
        spread_ref[slot] = jnp.dot(rates_ref[slot], expand, precision=lax.Precision.HIGHEST, preferred_element_type=jnp.float32)
        place_ref[slot] = jnp.dot(code_ref[slot], expand, precision=lax.Precision.HIGHEST, preferred_element_type=jnp.float32)
    depth = lax.broadcasted_iota(jnp.int32, (1, lanes), 1) % BIN_Z

    def body(index, carry):
        cell_x = index // (bins_y * BIN_XY)
        row_y = index % (bins_y * BIN_XY)
        bin_y = row_y // BIN_XY
        cell_y = row_y % BIN_XY
        target = (depth + (cell_x * (BIN_XY * BIN_Z) + cell_y * BIN_Z)).astype(jnp.float32)
        first = pl.multiple_of(bin_y * species, species)
        total = jnp.zeros((species, lanes), jnp.float32)
        for slot in range(slots):
            hit = place_ref[slot, pl.ds(bin_y, 1), :] == target
            total = total + jnp.where(hit, spread_ref[slot, pl.ds(first, species), :], 0.0)
        out_ref[cell_x, row_y] = total
        return carry

    lax.fori_loop(0, BIN_XY * bins_y * BIN_XY, body, 0)


def deposit(secretion, occupancy, offsets):
    species, bins_x, bins_y, lanes = secretion.shape
    layers = lanes // SLOTS
    rates_slot = secretion.reshape(species, bins_y, layers, SLOTS)
    rates_slot = jnp.transpose(rates_slot, (3, 1, 0, 2)).reshape(SLOTS, bins_y * species, layers)
    code = jnp.where(occupancy != 0, offsets, -1).astype(jnp.float32).reshape(bins_y, layers, SLOTS)
    code = jnp.transpose(code, (2, 0, 1))
    out = pl.pallas_call(
        deposit_kernel,
        out_shape=jax.ShapeDtypeStruct((BIN_XY, bins_y * BIN_XY, species, layers * BIN_Z), jnp.float32),
        scratch_shapes=[
            pltpu.VMEM((SLOTS, bins_y * species, layers * BIN_Z), jnp.float32),
            pltpu.VMEM((SLOTS, bins_y, layers * BIN_Z), jnp.float32),
        ],
        cost_estimate=pl.CostEstimate(flops=10_000_000, transcendentals=0, bytes_accessed=1_300_000),
    )(rates_slot, code)
    return jnp.transpose(out, (2, 0, 1, 3))

def pair_forces(points, padded, occupancy):
    planes, bins_x, bins_y, lanes = points.shape
    layers = lanes // SLOTS
    boxed = padded.reshape(planes, bins_x + 2, bins_y + 2, layers, SLOTS)
    boxed = jnp.pad(boxed, ((0, 0), (0, 0), (0, 0), (1, 1), (0, 0)))
    owned = points.reshape(planes, bins_x, bins_y, layers, SLOTS)[:3, :, :, :, :, None]
    force = jnp.zeros((3, bins_x, bins_y, layers, SLOTS), jnp.float32)
    for offset_x in range(3):
        nearby = jnp.concatenate(
            [
                boxed[
                    :,
                    offset_x : offset_x + bins_x,
                    offset_y : offset_y + bins_y,
                    offset_z : offset_z + layers,
                    :,
                ]
                for offset_y in range(3)
                for offset_z in range(3)
            ],
            axis=-1,
        )
        apart = owned - nearby[:3, :, :, :, None, :]
        strength = nearby[3][:, :, :, None, :] * jnp.exp(
            -jnp.sum(apart * apart, axis=0) / spread_sq
        )
        force = force + jnp.sum(apart * strength[None], axis=-1)
    active = occupancy.reshape(1, bins_x, bins_y, layers, SLOTS).astype(jnp.float32)
    return (move_step * active * force).reshape(3, bins_x, bins_y, lanes)


def storage_order(piece):
    if piece.ndim == 4 and piece.shape[0] > 4:
        return (1, 2, 0, 3)
    return tuple(range(piece.ndim))


def pack(pieces):
    return jnp.concatenate(
        [jnp.transpose(piece, storage_order(piece)).reshape(-1, 128) for piece in pieces], axis=0
    )


def unpack(flat, pieces):
    out = []
    row = 0
    for piece in pieces:
        rows = piece.size // 128
        order = storage_order(piece)
        stored = flat[row : row + rows].reshape(tuple(piece.shape[axis] for axis in order))
        out.append(jnp.transpose(stored, tuple(order.index(axis) for axis in range(piece.ndim))))
        row += rows
    return out


def send_pair(axis, upward, downward):
    count = lax.axis_size(axis)
    up = [(i, i + 1) for i in range(count - 1)]
    down = [(i + 1, i) for i in range(count - 1)]
    below = lax.ppermute(pack(upward), axis, up)
    above = lax.ppermute(pack(downward), axis, down)
    return unpack(below, upward), unpack(above, downward), below, above


def forces_kernel(span, scale, own_ref, near_ref, occ_ref, start_ref, out_ref):
    rows = own_ref.shape[1]
    lanes = own_ref.shape[-1]
    layers = lanes // SLOTS
    px = own_ref[0]
    py = own_ref[1]
    pz = own_ref[2]
    lane = lax.broadcasted_iota(jnp.int32, px.shape, 1)
    slot = lane % SLOTS
    layer = lane // SLOTS

    def body(offset_x, carry):
        fx, fy, fz = carry
        for offset_y in range(3):
            row = [near_ref[plane, offset_x, offset_y : offset_y + rows, :] for plane in range(4)]
            for offset_z in (-1, 0, 1):
                if offset_z == 0:
                    base = row
                else:
                    inside = (layer + offset_z >= 0) & (layer + offset_z < layers)
                    base = [
                        jnp.where(inside, pltpu.roll(part, (-offset_z * SLOTS) % lanes, 1), 0.0)
                        for part in row
                    ]
                for turn in range(SLOTS):
                    if turn == 0:
                        other = base
                    else:
                        keep = slot + turn < SLOTS
                        other = [
                            jnp.where(keep, pltpu.roll(part, lanes - turn, 1), pltpu.roll(part, SLOTS - turn, 1))
                            for part in base
                        ]
                    dx = px - other[0]
                    dy = py - other[1]
                    dz = pz - other[2]
                    strength = other[3] * jnp.exp(-(dx * dx + dy * dy + dz * dz) / spread_sq)
                    fx = fx + dx * strength
                    fy = fy + dy * strength
                    fz = fz + dz * strength
        return fx, fy, fz

    fx, fy, fz = lax.fori_loop(span[0], span[1], body, (start_ref[0], start_ref[1], start_ref[2]))
    if scale:
        active = move_step * occ_ref[...]
        fx = active * fx
        fy = active * fy
        fz = active * fz
    out_ref[0] = fx
    out_ref[1] = fy
    out_ref[2] = fz


def pallas_forces(points, bordered, occupancy, partial, span, scale):
    planes, _, rows, lanes = points.shape
    share = span[1] - span[0]
    return pl.pallas_call(
        functools.partial(forces_kernel, span, scale),
        out_shape=jax.ShapeDtypeStruct((3, rows, lanes), jnp.float32),
        cost_estimate=pl.CostEstimate(
            flops=3_000_000 * share, transcendentals=150_000 * share, bytes_accessed=120_000
        ),
    )(points[:, 0], bordered, occupancy[0].astype(jnp.float32), partial)


def arrived_kernel(starts, state, x_below, x_above, side_below, side_above, corner_below, corner_above, out_ref):
    along_x, beside, corner = starts
    span = state

    def rows(ref, first):
        return ref[first : first + span, :]

    out_ref[0] = rows(corner_above, corner)
    out_ref[1] = rows(x_above, along_x + span)
    out_ref[2] = rows(corner_below, corner)
    out_ref[3] = rows(side_above, beside)
    out_ref[4] = rows(side_below, beside)
    out_ref[5] = rows(corner_above, corner + span)
    out_ref[6] = rows(x_below, along_x + span)
    out_ref[7] = rows(corner_below, corner + span)


def gather_arrived(x_flats, side_flats, corner_flats, along_x, beside, corner, shape):
    state, lanes = shape
    return pl.pallas_call(
        functools.partial(arrived_kernel, (along_x, beside, corner), state),
        out_shape=jax.ShapeDtypeStruct((8, state, lanes), jnp.float32),
        cost_estimate=pl.CostEstimate(flops=0, transcendentals=0, bytes_accessed=300_000),
    )(*x_flats, *side_flats, *corner_flats)


def diagonal(block, step_x, step_y):
    count_x = lax.axis_size("gx")
    count_y = lax.axis_size("gy")
    pairs = []
    for i in range(count_x):
        for j in range(count_y):
            if 0 <= i + step_x < count_x and 0 <= j + step_y < count_y:
                pairs.append((i * count_y + j, (i + step_x) * count_y + j + step_y))
    return lax.ppermute(block, ("gx", "gy"), pairs)


def two_substeps(current, source, source_halos, rates, mixing, work):
    species, width, depth, lanes = current.shape
    (x_low,), (x_high,), *_ = send_pair("gx", [current[:, -2:]], [current[:, :2]])
    (y_low,), (y_high,), *_ = send_pair("gy", [current[:, :, -2:]], [current[:, :, :2]])
    low_low = diagonal(current[:, -1:, -1:], 1, 1)
    low_high = diagonal(current[:, -1:, :1], 1, -1)
    high_low = diagonal(current[:, :1, -1:], -1, 1)
    high_high = diagonal(current[:, :1, :1], -1, -1)
    done = work()
    current, done = lax.optimization_barrier((current, done))
    gap = jnp.zeros((species, 2, 2, lanes), current.dtype)
    left = jnp.concatenate([gap, y_low, gap], axis=1)
    right = jnp.concatenate([gap, y_high, gap], axis=1)
    padded = jnp.concatenate([left, jnp.concatenate([x_low, current, x_high], axis=1), right], axis=2)
    padded = padded.at[:, 1:2, 1:2].set(low_low)
    padded = padded.at[:, 1:2, depth + 2 : depth + 3].set(low_high)
    padded = padded.at[:, width + 2 : width + 3, 1:2].set(high_low)
    padded = padded.at[:, width + 2 : width + 3, depth + 2 : depth + 3].set(high_high)
    s_x_low, s_x_high, s_y_low, s_y_high = source_halos
    corner = jnp.zeros((species, 1, 1, lanes), current.dtype)
    s_left = jnp.concatenate([corner, s_y_low, corner], axis=1)
    s_right = jnp.concatenate([corner, s_y_high, corner], axis=1)
    wide_source = jnp.concatenate(
        [s_left, jnp.concatenate([s_x_low, source, s_x_high], axis=1), s_right], axis=2
    )
    wide = advance(padded, wide_source, rates, mixing)
    row = lax.broadcasted_iota(jnp.int32, (1, width + 2, depth + 2, 1), 1)
    col = lax.broadcasted_iota(jnp.int32, (1, width + 2, depth + 2, 1), 2)
    edge_x = lax.axis_size("gx") - 1
    edge_y = lax.axis_size("gy") - 1
    outside = (row == 0) & (lax.axis_index("gx") == 0)
    outside = outside | ((row == width + 1) & (lax.axis_index("gx") == edge_x))
    outside = outside | ((col == 0) & (lax.axis_index("gy") == 0))
    outside = outside | ((col == depth + 1) & (lax.axis_index("gy") == edge_y))
    wide = jnp.where(outside, 0.0, wide)
    return advance(wide, source, rates, mixing), done


def on_device(
    field,
    rates,
    mixing,
    secretion,
    positions,
    stiffness,
    occupancy,
    offsets,
    migrant_state,
    migrant_live,
):
    weight = stiffness * occupancy.astype(jnp.float32)
    points = jnp.concatenate([positions, weight[None]], axis=0)
    payload = migrant_state * migrant_live.astype(jnp.float32)
    source = deposit(secretion, occupancy, offsets)
    current = field

    (x_low, points_low, moved_up), (x_high, points_high, moved_down), *x_flats = send_pair(
        "gx",
        [current[:, -1:], points, payload[5:8]],
        [current[:, :1], points, payload[0:3]],
    )
    (y_low, beside_up), (y_high, beside_down), *side_flats = send_pair(
        "gy",
        [current[:, :, -1:], payload[4:5]],
        [current[:, :, :1], payload[3:4]],
    )
    current = advance(framed(current, x_low, x_high, y_low, y_high), source, rates, mixing)

    row_points = jnp.concatenate([points_low, points, points_high], axis=1)
    (x_low, s_x_low), (x_high, s_x_high), *_ = send_pair(
        "gx", [current[:, -1:], source[:, -1:]], [current[:, :1], source[:, :1]]
    )
    (y_low, points_low, corner_up, s_y_low), (y_high, points_high, corner_down, s_y_high), *corner_flats = send_pair(
        "gy",
        [current[:, :, -1:], row_points[:, :, -1:], jnp.stack([moved_down[2], moved_up[2]]), source[:, :, -1:]],
        [current[:, :, :1], row_points[:, :, :1], jnp.stack([moved_down[0], moved_up[0]]), source[:, :, :1]],
    )
    bordered = jnp.concatenate([points_low, row_points, points_high], axis=2)
    field_rows = x_low.size // 128
    side_rows = y_low.size // 128
    starts = (field_rows + points.size // 128, side_rows, side_rows + points_low.size // 128)
    rows = points.shape[2]
    zero = jnp.zeros((3, rows, points.shape[3]), jnp.float32)
    arrived = gather_arrived(x_flats, side_flats, corner_flats, *starts, payload.shape[1:])
    partial = pallas_forces(points, bordered, occupancy, zero, (0, 2), False)
    current, arrived, partial = lax.optimization_barrier((current, arrived, partial))
    current = advance(framed(current, x_low, x_high, y_low, y_high), source, rates, mixing)
    current, bordered, partial = lax.optimization_barrier((current, bordered, partial))

    def later_work():
        return pallas_forces(points, bordered, occupancy, partial, (2, 3), True)

    source_halos = (s_x_low, s_x_high, s_y_low, s_y_high)
    current, force = two_substeps(current, source, source_halos, rates, mixing, later_work)
    displacement = force.reshape(3, 1, rows, points.shape[3])
    return (current, displacement, arrived)


def solution(mesh):
    return jax.shard_map(
        on_device,
        mesh=mesh,
        in_specs=(
            P(None, "gx", "gy", None),
            P(),
            P(),
            P(None, "gx", "gy", None),
            P(None, "gx", "gy", None),
            P("gx", "gy", None),
            P("gx", "gy", None),
            P("gx", "gy", None),
            P(None, "gx", "gy"),
            P(None, "gx", "gy"),
        ),
        out_specs=(P(None, "gx", "gy", None), P(None, "gx", "gy", None), P(None, "gx", "gy")),
        check_vma=False,
    )
```

```python
import functools

import jax
import jax.numpy as jnp
from jax import lax
from jax.experimental import pallas as pl
from jax.experimental.pallas import tpu as pltpu
from jax.sharding import PartitionSpec as P

BIN_XY = 4
BIN_Z = 8
SLOTS = 16
SUBSTEPS = 4


time_step = 0.15
move_step = 0.1
spread_sq = 8.0
shifts = ((-1, -1), (-1, 0), (-1, 1), (0, -1), (0, 1), (1, -1), (1, 0), (1, 1))


def padded_2(cells, sides, width):
    for axis, dim in sides:
        count = lax.axis_size(axis)
        ends = count - 1
        head = lax.slice_in_dim(cells, 0, width, axis=dim)
        tail = lax.slice_in_dim(cells, cells.shape[dim] - width, cells.shape[dim], axis=dim)
        cells = jnp.concatenate(
            [
                lax.ppermute(tail, axis, [(i, (i + 1) % count) for i in range(ends)]),
                cells,
                lax.ppermute(head, axis, [((i + 1) % count, i) for i in range(ends)]),
            ],
            axis=dim,
        )
    return cells


def halos(cells, axis, dim):
    count = lax.axis_size(axis)
    ends = count - 1
    head = lax.slice_in_dim(cells, 0, 1, axis=dim)
    tail = lax.slice_in_dim(cells, cells.shape[dim] - 1, cells.shape[dim], axis=dim)
    low = lax.ppermute(tail, axis, [(i, (i + 1) % count) for i in range(ends)])
    high = lax.ppermute(head, axis, [((i + 1) % count, i) for i in range(ends)])
    return low, high


def framed(cells, x_low, x_high, y_low, y_high):
    species, width, depth, lanes = cells.shape
    corner = jnp.zeros((species, 1, 1, lanes), cells.dtype)
    middle = jnp.concatenate([x_low, cells, x_high], axis=1)
    left = jnp.concatenate([corner, y_low, corner], axis=1)
    right = jnp.concatenate([corner, y_high, corner], axis=1)
    return jnp.concatenate([left, middle, right], axis=2)


def substep_beside(current, source, rates, mixing, work):
    x_low, x_high = halos(current, "gx", 1)
    y_low, y_high = halos(current, "gy", 2)
    done = work()
    current, done = lax.optimization_barrier((current, done))
    padded = framed(current, x_low, x_high, y_low, y_high)
    return advance(padded, source, rates, mixing), done


def substep(current, source, rates, mixing):
    x_low, x_high = halos(current, "gx", 1)
    y_low, y_high = halos(current, "gy", 2)
    padded = framed(current, x_low, x_high, y_low, y_high)
    return advance(padded, source, rates, mixing)


def shifted(block, axis, distance):
    devices = range(lax.axis_size(axis))
    route = [(i - distance, i) for i in devices if i - distance in devices]
    return lax.ppermute(block, axis, route)


def advance(padded, source, rates, mixing):
    center = padded[:, 1:-1, 1:-1, :]
    deeper = jnp.pad(center, ((0, 0), (0, 0), (0, 0), (1, 1)))
    beside = padded[:, 2:, 1:-1, :] + padded[:, :-2, 1:-1, :]
    beside = beside + padded[:, 1:-1, 2:, :] + padded[:, 1:-1, :-2, :]
    beside = beside + deeper[:, :, :, 2:] + deeper[:, :, :, :-2]
    laplace = beside - 6.0 * center
    species = center.shape[0]
    mixed = jnp.dot(mixing, center.reshape(species, -1), precision=lax.Precision.HIGHEST).reshape(
        center.shape
    )
    return (
        center
        + time_step * (rates[:, None, None, None] * laplace)
        + time_step * mixed
        + time_step * source
    )


def deposit_kernel(rates_ref, code_ref, out_ref, spread_ref, place_ref):
    slots, rows, layers = rates_ref.shape
    bins_y = code_ref.shape[1]
    species = rows // bins_y
    lanes = layers * BIN_Z
    layer_of = lax.broadcasted_iota(jnp.int32, (layers, lanes), 1) // BIN_Z
    expand = (lax.broadcasted_iota(jnp.int32, (layers, lanes), 0) == layer_of).astype(jnp.float32)
    for slot in range(slots):
        spread_ref[slot] = jnp.dot(rates_ref[slot], expand, precision=lax.Precision.HIGHEST, preferred_element_type=jnp.float32)
        place_ref[slot] = jnp.dot(code_ref[slot], expand, precision=lax.Precision.HIGHEST, preferred_element_type=jnp.float32)
    depth = lax.broadcasted_iota(jnp.int32, (1, lanes), 1) % BIN_Z

    def body(index, carry):
        cell_x = index // (bins_y * BIN_XY)
        row_y = index % (bins_y * BIN_XY)
        bin_y = row_y // BIN_XY
        cell_y = row_y % BIN_XY
        target = (depth + (cell_x * (BIN_XY * BIN_Z) + cell_y * BIN_Z)).astype(jnp.float32)
        first = pl.multiple_of(bin_y * species, species)
        total = jnp.zeros((species, lanes), jnp.float32)
        for slot in range(slots):
            hit = place_ref[slot, pl.ds(bin_y, 1), :] == target
            total = total + jnp.where(hit, spread_ref[slot, pl.ds(first, species), :], 0.0)
        out_ref[cell_x, row_y] = total
        return carry

    lax.fori_loop(0, BIN_XY * bins_y * BIN_XY, body, 0)


def deposit(secretion, occupancy, offsets):
    species, bins_x, bins_y, lanes = secretion.shape
    layers = lanes // SLOTS
    rates_slot = secretion.reshape(species, bins_y, layers, SLOTS)
    rates_slot = jnp.transpose(rates_slot, (3, 1, 0, 2)).reshape(SLOTS, bins_y * species, layers)
    code = jnp.where(occupancy != 0, offsets, -1).astype(jnp.float32).reshape(bins_y, layers, SLOTS)
    code = jnp.transpose(code, (2, 0, 1))
    out = pl.pallas_call(
        deposit_kernel,
        out_shape=jax.ShapeDtypeStruct((BIN_XY, bins_y * BIN_XY, species, layers * BIN_Z), jnp.float32),
        scratch_shapes=[
            pltpu.VMEM((SLOTS, bins_y * species, layers * BIN_Z), jnp.float32),
            pltpu.VMEM((SLOTS, bins_y, layers * BIN_Z), jnp.float32),
        ],
        cost_estimate=pl.CostEstimate(flops=10_000_000, transcendentals=0, bytes_accessed=1_300_000),
    )(rates_slot, code)
    return jnp.transpose(out, (2, 0, 1, 3))

def pair_forces(points, padded, occupancy):
    planes, bins_x, bins_y, lanes = points.shape
    layers = lanes // SLOTS
    boxed = padded.reshape(planes, bins_x + 2, bins_y + 2, layers, SLOTS)
    boxed = jnp.pad(boxed, ((0, 0), (0, 0), (0, 0), (1, 1), (0, 0)))
    owned = points.reshape(planes, bins_x, bins_y, layers, SLOTS)[:3, :, :, :, :, None]
    force = jnp.zeros((3, bins_x, bins_y, layers, SLOTS), jnp.float32)
    for offset_x in range(3):
        nearby = jnp.concatenate(
            [
                boxed[
                    :,
                    offset_x : offset_x + bins_x,
                    offset_y : offset_y + bins_y,
                    offset_z : offset_z + layers,
                    :,
                ]
                for offset_y in range(3)
                for offset_z in range(3)
            ],
            axis=-1,
        )
        apart = owned - nearby[:3, :, :, :, None, :]
        strength = nearby[3][:, :, :, None, :] * jnp.exp(
            -jnp.sum(apart * apart, axis=0) / spread_sq
        )
        force = force + jnp.sum(apart * strength[None], axis=-1)
    active = occupancy.reshape(1, bins_x, bins_y, layers, SLOTS).astype(jnp.float32)
    return (move_step * active * force).reshape(3, bins_x, bins_y, lanes)


def storage_order(piece):
    if piece.ndim == 4 and piece.shape[0] > 4:
        return (1, 2, 0, 3)
    return tuple(range(piece.ndim))


def pack(pieces):
    return jnp.concatenate(
        [jnp.transpose(piece, storage_order(piece)).reshape(-1, 128) for piece in pieces], axis=0
    )


def unpack(flat, pieces):
    out = []
    row = 0
    for piece in pieces:
        rows = piece.size // 128
        order = storage_order(piece)
        stored = flat[row : row + rows].reshape(tuple(piece.shape[axis] for axis in order))
        out.append(jnp.transpose(stored, tuple(order.index(axis) for axis in range(piece.ndim))))
        row += rows
    return out


def send_pair(axis, upward, downward):
    count = lax.axis_size(axis)
    up = [(i, i + 1) for i in range(count - 1)]
    down = [(i + 1, i) for i in range(count - 1)]
    below = lax.ppermute(pack(upward), axis, up)
    above = lax.ppermute(pack(downward), axis, down)
    return unpack(below, upward), unpack(above, downward), below, above


def forces_kernel(shifts, scale, own_ref, near_ref, occ_ref, start_ref, out_ref, mine_ref, other_ref):
    rows = own_ref.shape[1]
    lanes = own_ref.shape[-1]
    layers = lanes // SLOTS
    stacked = mine_ref.shape[1]
    groups = 9
    mine_ref[...] = jnp.zeros_like(mine_ref)
    other_ref[...] = jnp.zeros_like(other_ref)
    for plane in range(4):
        for offset_x in range(3):
            for offset_y in range(3):
                group = (offset_x * 3 + offset_y) * rows
                other_ref[plane, group : group + rows, :] = near_ref[plane, offset_x, offset_y : offset_y + rows, :]
                if plane < 3:
                    mine_ref[plane, group : group + rows, :] = own_ref[plane]
    px = mine_ref[0]
    py = mine_ref[1]
    pz = mine_ref[2]
    lane = lax.broadcasted_iota(jnp.int32, (stacked, lanes), 1)
    slot = lane % SLOTS
    layer = lane // SLOTS
    fx = start_ref[0]
    fy = start_ref[1]
    fz = start_ref[2]
    row = [other_ref[plane] for plane in range(4)]
    for offset_z in shifts:
        if offset_z == 0:
            base = row
        else:
            inside = (layer + offset_z >= 0) & (layer + offset_z < layers)
            base = [jnp.where(inside, pltpu.roll(part, (-offset_z * SLOTS) % lanes, 1), 0.0) for part in row]
        for turn in range(SLOTS):
            if turn == 0:
                other = base
            else:
                keep = slot + turn < SLOTS
                other = [
                    jnp.where(keep, pltpu.roll(part, lanes - turn, 1), pltpu.roll(part, SLOTS - turn, 1))
                    for part in base
                ]
            dx = px - other[0]
            dy = py - other[1]
            dz = pz - other[2]
            strength = other[3] * jnp.exp(-(dx * dx + dy * dy + dz * dz) / spread_sq)
            fx = fx + dx * strength
            fy = fy + dy * strength
            fz = fz + dz * strength
    if scale:
        active = move_step * occ_ref[...]
        for plane, total in enumerate((fx, fy, fz)):
            summed = total[0:rows]
            for group in range(1, groups):
                summed = summed + total[group * rows : (group + 1) * rows]
            out_ref[plane, 0:rows, :] = active * summed
    else:
        out_ref[0] = fx
        out_ref[1] = fy
        out_ref[2] = fz


def pallas_forces(points, bordered, occupancy, partial, shifts, scale):
    planes, _, rows, lanes = points.shape
    stacked = -(-9 * rows // 8) * 8
    if partial is None:
        partial = jnp.zeros((3, stacked, lanes), jnp.float32)
    out_rows = rows if scale else stacked
    return pl.pallas_call(
        functools.partial(forces_kernel, shifts, scale),
        out_shape=jax.ShapeDtypeStruct((3, out_rows, lanes), jnp.float32),
        scratch_shapes=[pltpu.VMEM((3, stacked, lanes), jnp.float32), pltpu.VMEM((4, stacked, lanes), jnp.float32)],
        cost_estimate=pl.CostEstimate(
            flops=3_000_000 * len(shifts), transcendentals=150_000 * len(shifts), bytes_accessed=150_000
        ),
    )(points[:, 0], bordered, occupancy[0].astype(jnp.float32), partial)


def arrived_kernel(starts, state, x_below, x_above, side_below, side_above, corner_below, corner_above, out_ref):
    along_x, beside, corner = starts
    span = state

    def rows(ref, first):
        return ref[first : first + span, :]

    out_ref[0] = rows(corner_above, corner)
    out_ref[1] = rows(x_above, along_x + span)
    out_ref[2] = rows(corner_below, corner)
    out_ref[3] = rows(side_above, beside)
    out_ref[4] = rows(side_below, beside)
    out_ref[5] = rows(corner_above, corner + span)
    out_ref[6] = rows(x_below, along_x + span)
    out_ref[7] = rows(corner_below, corner + span)


def gather_arrived(x_flats, side_flats, corner_flats, along_x, beside, corner, shape):
    state, lanes = shape
    return pl.pallas_call(
        functools.partial(arrived_kernel, (along_x, beside, corner), state),
        out_shape=jax.ShapeDtypeStruct((8, state, lanes), jnp.float32),
        cost_estimate=pl.CostEstimate(flops=0, transcendentals=0, bytes_accessed=300_000),
    )(*x_flats, *side_flats, *corner_flats)


def on_device(
    field,
    rates,
    mixing,
    secretion,
    positions,
    stiffness,
    occupancy,
    offsets,
    migrant_state,
    migrant_live,
):
    weight = stiffness * occupancy.astype(jnp.float32)
    points = jnp.concatenate([positions, weight[None]], axis=0)
    payload = migrant_state * migrant_live.astype(jnp.float32)
    source = deposit(secretion, occupancy, offsets)
    current = field

    (x_low, points_low, moved_up), (x_high, points_high, moved_down), *x_flats = send_pair(
        "gx",
        [current[:, -1:], points, payload[5:8]],
        [current[:, :1], points, payload[0:3]],
    )
    (y_low, beside_up), (y_high, beside_down), *side_flats = send_pair(
        "gy",
        [current[:, :, -1:], payload[4:5]],
        [current[:, :, :1], payload[3:4]],
    )
    current = advance(framed(current, x_low, x_high, y_low, y_high), source, rates, mixing)

    row_points = jnp.concatenate([points_low, points, points_high], axis=1)
    x_low, x_high = halos(current, "gx", 1)
    (y_low, points_low, corner_up), (y_high, points_high, corner_down), *corner_flats = send_pair(
        "gy",
        [current[:, :, -1:], row_points[:, :, -1:], jnp.stack([moved_down[2], moved_up[2]])],
        [current[:, :, :1], row_points[:, :, :1], jnp.stack([moved_down[0], moved_up[0]])],
    )
    bordered = jnp.concatenate([points_low, row_points, points_high], axis=2)
    field_rows = x_low.size // 128
    side_rows = y_low.size // 128
    starts = (field_rows + points.size // 128, side_rows, side_rows + points_low.size // 128)
    rows = points.shape[2]
    arrived = gather_arrived(x_flats, side_flats, corner_flats, *starts, payload.shape[1:])
    partial = pallas_forces(points, bordered, occupancy, None, (-1, 0), False)
    current, arrived, partial = lax.optimization_barrier((current, arrived, partial))
    current = advance(framed(current, x_low, x_high, y_low, y_high), source, rates, mixing)
    current, bordered, partial = lax.optimization_barrier((current, bordered, partial))

    def later_work():
        return pallas_forces(points, bordered, occupancy, partial, (1,), True)

    current, force = substep_beside(current, source, rates, mixing, later_work)
    current = substep(current, source, rates, mixing)
    displacement = force.reshape(3, 1, rows, points.shape[3])
    return (current, displacement, arrived)


def solution(mesh):
    return jax.shard_map(
        on_device,
        mesh=mesh,
        in_specs=(
            P(None, "gx", "gy", None),
            P(),
            P(),
            P(None, "gx", "gy", None),
            P(None, "gx", "gy", None),
            P("gx", "gy", None),
            P("gx", "gy", None),
            P("gx", "gy", None),
            P(None, "gx", "gy"),
            P(None, "gx", "gy"),
        ),
        out_specs=(P(None, "gx", "gy", None), P(None, "gx", "gy", None), P(None, "gx", "gy")),
        check_vma=False,
    )
```

```python
import functools

import jax
import jax.numpy as jnp
from jax import lax
from jax.experimental import pallas as pl
from jax.experimental.pallas import tpu as pltpu
from jax.sharding import PartitionSpec as P

BIN_XY = 4
BIN_Z = 8
SLOTS = 16
SUBSTEPS = 4


time_step = 0.15
move_step = 0.1
spread_sq = 8.0
shifts = ((-1, -1), (-1, 0), (-1, 1), (0, -1), (0, 1), (1, -1), (1, 0), (1, 1))


def padded_2(cells, sides, width):
    for axis, dim in sides:
        count = lax.axis_size(axis)
        ends = count - 1
        head = lax.slice_in_dim(cells, 0, width, axis=dim)
        tail = lax.slice_in_dim(cells, cells.shape[dim] - width, cells.shape[dim], axis=dim)
        cells = jnp.concatenate(
            [
                lax.ppermute(tail, axis, [(i, (i + 1) % count) for i in range(ends)]),
                cells,
                lax.ppermute(head, axis, [((i + 1) % count, i) for i in range(ends)]),
            ],
            axis=dim,
        )
    return cells


def halos(cells, axis, dim):
    count = lax.axis_size(axis)
    ends = count - 1
    head = lax.slice_in_dim(cells, 0, 1, axis=dim)
    tail = lax.slice_in_dim(cells, cells.shape[dim] - 1, cells.shape[dim], axis=dim)
    low = lax.ppermute(tail, axis, [(i, (i + 1) % count) for i in range(ends)])
    high = lax.ppermute(head, axis, [((i + 1) % count, i) for i in range(ends)])
    return low, high


def framed(cells, x_low, x_high, y_low, y_high):
    species, width, depth, lanes = cells.shape
    corner = jnp.zeros((species, 1, 1, lanes), cells.dtype)
    middle = jnp.concatenate([x_low, cells, x_high], axis=1)
    left = jnp.concatenate([corner, y_low, corner], axis=1)
    right = jnp.concatenate([corner, y_high, corner], axis=1)
    return jnp.concatenate([left, middle, right], axis=2)


def substep_beside(current, source, rates, mixing, work):
    x_low, x_high = halos(current, "gx", 1)
    y_low, y_high = halos(current, "gy", 2)
    done = work()
    current, done = lax.optimization_barrier((current, done))
    return fused_step(current, x_low, x_high, y_low, y_high, source, rates, mixing), done


def substep(current, source, rates, mixing):
    x_low, x_high = halos(current, "gx", 1)
    y_low, y_high = halos(current, "gy", 2)
    return fused_step(current, x_low, x_high, y_low, y_high, source, rates, mixing)


def shifted(block, axis, distance):
    devices = range(lax.axis_size(axis))
    route = [(i - distance, i) for i in devices if i - distance in devices]
    return lax.ppermute(block, axis, route)


def advance(padded, source, rates, mixing):
    center = padded[:, 1:-1, 1:-1, :]
    deeper = jnp.pad(center, ((0, 0), (0, 0), (0, 0), (1, 1)))
    beside = padded[:, 2:, 1:-1, :] + padded[:, :-2, 1:-1, :]
    beside = beside + padded[:, 1:-1, 2:, :] + padded[:, 1:-1, :-2, :]
    beside = beside + deeper[:, :, :, 2:] + deeper[:, :, :, :-2]
    laplace = beside - 6.0 * center
    species = center.shape[0]
    mixed = jnp.dot(mixing, center.reshape(species, -1), precision=lax.Precision.HIGHEST).reshape(
        center.shape
    )
    return (
        center
        + time_step * (rates[:, None, None, None] * laplace)
        + time_step * mixed
        + time_step * source
    )


def step_kernel(width, depth, c_ref, xlo_ref, xhi_ref, ylo_ref, yhi_ref, src_ref, rates_ref, mixing_ref, out_ref):
    species, total = c_ref.shape
    lanes = total // (width * depth)
    plane = depth * lanes
    chunk = 4 * lanes
    mixing = mixing_ref[...]
    rate = rates_ref[...]
    z = lax.broadcasted_iota(jnp.int32, (species, chunk), 1) % lanes
    for x in range(width):
        for part in range(depth // 4):
            first = x * plane + part * chunk
            center = c_ref[:, first : first + chunk]
            if x > 0:
                below = c_ref[:, first - plane : first - plane + chunk]
            else:
                below = xlo_ref[:, part * chunk : (part + 1) * chunk]
            if x < width - 1:
                above = c_ref[:, first + plane : first + plane + chunk]
            else:
                above = xhi_ref[:, part * chunk : (part + 1) * chunk]
            if part > 0:
                left = c_ref[:, first - lanes : first - lanes + chunk]
            else:
                left = jnp.concatenate([ylo_ref[:, x * lanes : (x + 1) * lanes], c_ref[:, first : first + chunk - lanes]], axis=1)
            if part < depth // 4 - 1:
                right = c_ref[:, first + lanes : first + lanes + chunk]
            else:
                right = jnp.concatenate([c_ref[:, first + lanes : first + chunk], yhi_ref[:, x * lanes : (x + 1) * lanes]], axis=1)
            deeper = jnp.where(z == lanes - 1, 0.0, pltpu.roll(center, chunk - 1, 1))
            shallower = jnp.where(z == 0, 0.0, pltpu.roll(center, 1, 1))
            beside = above + below
            beside = beside + right + left
            beside = beside + deeper + shallower
            laplace = beside - 6.0 * center
            mixed = jnp.dot(mixing, center, precision=lax.Precision.HIGHEST, preferred_element_type=jnp.float32)
            source = src_ref[:, first : first + chunk]
            out_ref[:, first : first + chunk] = (
                center + time_step * (rate * laplace) + time_step * mixed + time_step * source
            )


def fused_step(current, x_low, x_high, y_low, y_high, source, rates, mixing):
    species, width, depth, lanes = current.shape
    out = pl.pallas_call(
        functools.partial(step_kernel, width, depth),
        out_shape=jax.ShapeDtypeStruct((species, width * depth * lanes), jnp.float32),
        cost_estimate=pl.CostEstimate(flops=60_000_000, transcendentals=0, bytes_accessed=2_500_000),
    )(*[part.reshape(species, -1) for part in (current, x_low, x_high, y_low, y_high, source)], rates.reshape(species, 1), mixing)
    return out.reshape(current.shape)


def deposit_kernel(rates_ref, code_ref, out_ref, spread_ref, place_ref):
    slots, rows, layers = rates_ref.shape
    bins_y = code_ref.shape[1]
    species = rows // bins_y
    lanes = layers * BIN_Z
    layer_of = lax.broadcasted_iota(jnp.int32, (layers, lanes), 1) // BIN_Z
    expand = (lax.broadcasted_iota(jnp.int32, (layers, lanes), 0) == layer_of).astype(jnp.float32)
    for slot in range(slots):
        spread_ref[slot] = jnp.dot(rates_ref[slot], expand, precision=lax.Precision.HIGHEST, preferred_element_type=jnp.float32)
        place_ref[slot] = jnp.dot(code_ref[slot], expand, precision=lax.Precision.HIGHEST, preferred_element_type=jnp.float32)
    depth = lax.broadcasted_iota(jnp.int32, (1, lanes), 1) % BIN_Z

    def body(index, carry):
        cell_x = index // (bins_y * BIN_XY)
        row_y = index % (bins_y * BIN_XY)
        bin_y = row_y // BIN_XY
        cell_y = row_y % BIN_XY
        target = (depth + (cell_x * (BIN_XY * BIN_Z) + cell_y * BIN_Z)).astype(jnp.float32)
        first = pl.multiple_of(bin_y * species, species)
        total = jnp.zeros((species, lanes), jnp.float32)
        for slot in range(slots):
            hit = place_ref[slot, pl.ds(bin_y, 1), :] == target
            total = total + jnp.where(hit, spread_ref[slot, pl.ds(first, species), :], 0.0)
        out_ref[:, pl.ds(pl.multiple_of(index * lanes, lanes), lanes)] = total
        return carry

    lax.fori_loop(0, BIN_XY * bins_y * BIN_XY, body, 0)


def deposit(secretion, occupancy, offsets):
    species, bins_x, bins_y, lanes = secretion.shape
    layers = lanes // SLOTS
    rates_slot = secretion.reshape(species, bins_y, layers, SLOTS)
    rates_slot = jnp.transpose(rates_slot, (3, 1, 0, 2)).reshape(SLOTS, bins_y * species, layers)
    code = jnp.where(occupancy != 0, offsets, -1).astype(jnp.float32).reshape(bins_y, layers, SLOTS)
    code = jnp.transpose(code, (2, 0, 1))
    out = pl.pallas_call(
        deposit_kernel,
        out_shape=jax.ShapeDtypeStruct((species, BIN_XY * bins_y * BIN_XY * layers * BIN_Z), jnp.float32),
        scratch_shapes=[
            pltpu.VMEM((SLOTS, bins_y * species, layers * BIN_Z), jnp.float32),
            pltpu.VMEM((SLOTS, bins_y, layers * BIN_Z), jnp.float32),
        ],
        cost_estimate=pl.CostEstimate(flops=10_000_000, transcendentals=0, bytes_accessed=1_300_000),
    )(rates_slot, code)
    return out.reshape(species, BIN_XY, bins_y * BIN_XY, layers * BIN_Z)

def pair_forces(points, padded, occupancy):
    planes, bins_x, bins_y, lanes = points.shape
    layers = lanes // SLOTS
    boxed = padded.reshape(planes, bins_x + 2, bins_y + 2, layers, SLOTS)
    boxed = jnp.pad(boxed, ((0, 0), (0, 0), (0, 0), (1, 1), (0, 0)))
    owned = points.reshape(planes, bins_x, bins_y, layers, SLOTS)[:3, :, :, :, :, None]
    force = jnp.zeros((3, bins_x, bins_y, layers, SLOTS), jnp.float32)
    for offset_x in range(3):
        nearby = jnp.concatenate(
            [
                boxed[
                    :,
                    offset_x : offset_x + bins_x,
                    offset_y : offset_y + bins_y,
                    offset_z : offset_z + layers,
                    :,
                ]
                for offset_y in range(3)
                for offset_z in range(3)
            ],
            axis=-1,
        )
        apart = owned - nearby[:3, :, :, :, None, :]
        strength = nearby[3][:, :, :, None, :] * jnp.exp(
            -jnp.sum(apart * apart, axis=0) / spread_sq
        )
        force = force + jnp.sum(apart * strength[None], axis=-1)
    active = occupancy.reshape(1, bins_x, bins_y, layers, SLOTS).astype(jnp.float32)
    return (move_step * active * force).reshape(3, bins_x, bins_y, lanes)


def storage_order(piece):
    return tuple(range(piece.ndim))


def pack(pieces):
    return jnp.concatenate(
        [jnp.transpose(piece, storage_order(piece)).reshape(-1, 128) for piece in pieces], axis=0
    )


def unpack(flat, pieces):
    out = []
    row = 0
    for piece in pieces:
        rows = piece.size // 128
        order = storage_order(piece)
        stored = flat[row : row + rows].reshape(tuple(piece.shape[axis] for axis in order))
        out.append(jnp.transpose(stored, tuple(order.index(axis) for axis in range(piece.ndim))))
        row += rows
    return out


def send_pair(axis, upward, downward):
    count = lax.axis_size(axis)
    up = [(i, i + 1) for i in range(count - 1)]
    down = [(i + 1, i) for i in range(count - 1)]
    below = lax.ppermute(pack(upward), axis, up)
    above = lax.ppermute(pack(downward), axis, down)
    return unpack(below, upward), unpack(above, downward), below, above


def forces_kernel(shifts, scale, own_ref, near_ref, occ_ref, start_ref, out_ref, mine_ref, other_ref):
    rows = own_ref.shape[1]
    lanes = own_ref.shape[-1]
    layers = lanes // SLOTS
    stacked = mine_ref.shape[1]
    groups = 9
    mine_ref[...] = jnp.zeros_like(mine_ref)
    other_ref[...] = jnp.zeros_like(other_ref)
    for plane in range(4):
        for offset_x in range(3):
            for offset_y in range(3):
                group = (offset_x * 3 + offset_y) * rows
                other_ref[plane, group : group + rows, :] = near_ref[plane, offset_x, offset_y : offset_y + rows, :]
                if plane < 3:
                    mine_ref[plane, group : group + rows, :] = own_ref[plane]
    px = mine_ref[0]
    py = mine_ref[1]
    pz = mine_ref[2]
    lane = lax.broadcasted_iota(jnp.int32, (stacked, lanes), 1)
    slot = lane % SLOTS
    layer = lane // SLOTS
    fx = start_ref[0]
    fy = start_ref[1]
    fz = start_ref[2]
    row = [other_ref[plane] for plane in range(4)]
    for offset_z in shifts:
        if offset_z == 0:
            base = row
        else:
            inside = (layer + offset_z >= 0) & (layer + offset_z < layers)
            base = [jnp.where(inside, pltpu.roll(part, (-offset_z * SLOTS) % lanes, 1), 0.0) for part in row]
        for turn in range(SLOTS):
            if turn == 0:
                other = base
            else:
                keep = slot + turn < SLOTS
                other = [
                    jnp.where(keep, pltpu.roll(part, lanes - turn, 1), pltpu.roll(part, SLOTS - turn, 1))
                    for part in base
                ]
            dx = px - other[0]
            dy = py - other[1]
            dz = pz - other[2]
            strength = other[3] * jnp.exp(-(dx * dx + dy * dy + dz * dz) / spread_sq)
            fx = fx + dx * strength
            fy = fy + dy * strength
            fz = fz + dz * strength
    if scale:
        active = move_step * occ_ref[...]
        for plane, total in enumerate((fx, fy, fz)):
            summed = total[0:rows]
            for group in range(1, groups):
                summed = summed + total[group * rows : (group + 1) * rows]
            out_ref[plane, 0:rows, :] = active * summed
    else:
        out_ref[0] = fx
        out_ref[1] = fy
        out_ref[2] = fz


def pallas_forces(points, bordered, occupancy, partial, shifts, scale):
    planes, _, rows, lanes = points.shape
    stacked = -(-9 * rows // 8) * 8
    if partial is None:
        partial = jnp.zeros((3, stacked, lanes), jnp.float32)
    out_rows = rows if scale else stacked
    return pl.pallas_call(
        functools.partial(forces_kernel, shifts, scale),
        out_shape=jax.ShapeDtypeStruct((3, out_rows, lanes), jnp.float32),
        scratch_shapes=[pltpu.VMEM((3, stacked, lanes), jnp.float32), pltpu.VMEM((4, stacked, lanes), jnp.float32)],
        cost_estimate=pl.CostEstimate(
            flops=3_000_000 * len(shifts), transcendentals=150_000 * len(shifts), bytes_accessed=150_000
        ),
    )(points[:, 0], bordered, occupancy[0].astype(jnp.float32), partial)


def arrived_kernel(starts, state, x_below, x_above, side_below, side_above, corner_below, corner_above, out_ref):
    along_x, beside, corner = starts
    span = state

    def rows(ref, first):
        return ref[first : first + span, :]

    out_ref[0] = rows(corner_above, corner)
    out_ref[1] = rows(x_above, along_x + span)
    out_ref[2] = rows(corner_below, corner)
    out_ref[3] = rows(side_above, beside)
    out_ref[4] = rows(side_below, beside)
    out_ref[5] = rows(corner_above, corner + span)
    out_ref[6] = rows(x_below, along_x + span)
    out_ref[7] = rows(corner_below, corner + span)


def gather_arrived(x_flats, side_flats, corner_flats, along_x, beside, corner, shape):
    state, lanes = shape
    return pl.pallas_call(
        functools.partial(arrived_kernel, (along_x, beside, corner), state),
        out_shape=jax.ShapeDtypeStruct((8, state, lanes), jnp.float32),
        cost_estimate=pl.CostEstimate(flops=0, transcendentals=0, bytes_accessed=300_000),
    )(*x_flats, *side_flats, *corner_flats)


def on_device(
    field,
    rates,
    mixing,
    secretion,
    positions,
    stiffness,
    occupancy,
    offsets,
    migrant_state,
    migrant_live,
):
    weight = stiffness * occupancy.astype(jnp.float32)
    points = jnp.concatenate([positions, weight[None]], axis=0)
    payload = migrant_state * migrant_live.astype(jnp.float32)
    source = deposit(secretion, occupancy, offsets)
    current = field

    (x_low, points_low, moved_up), (x_high, points_high, moved_down), *x_flats = send_pair(
        "gx",
        [current[:, -1:], points, payload[5:8]],
        [current[:, :1], points, payload[0:3]],
    )
    (y_low, beside_up), (y_high, beside_down), *side_flats = send_pair(
        "gy",
        [current[:, :, -1:], payload[4:5]],
        [current[:, :, :1], payload[3:4]],
    )
    current = fused_step(current, x_low, x_high, y_low, y_high, source, rates, mixing)

    row_points = jnp.concatenate([points_low, points, points_high], axis=1)
    x_low, x_high = halos(current, "gx", 1)
    (y_low, points_low, corner_up), (y_high, points_high, corner_down), *corner_flats = send_pair(
        "gy",
        [current[:, :, -1:], row_points[:, :, -1:], jnp.stack([moved_down[2], moved_up[2]])],
        [current[:, :, :1], row_points[:, :, :1], jnp.stack([moved_down[0], moved_up[0]])],
    )
    bordered = jnp.concatenate([points_low, row_points, points_high], axis=2)
    field_rows = x_low.size // 128
    side_rows = y_low.size // 128
    starts = (field_rows + points.size // 128, side_rows, side_rows + points_low.size // 128)
    rows = points.shape[2]
    arrived = gather_arrived(x_flats, side_flats, corner_flats, *starts, payload.shape[1:])
    partial = pallas_forces(points, bordered, occupancy, None, (-1, 0), False)
    current, arrived, partial = lax.optimization_barrier((current, arrived, partial))
    current = fused_step(current, x_low, x_high, y_low, y_high, source, rates, mixing)
    current, bordered, partial = lax.optimization_barrier((current, bordered, partial))

    def later_work():
        return pallas_forces(points, bordered, occupancy, partial, (1,), True)

    current, force = substep_beside(current, source, rates, mixing, later_work)
    current = substep(current, source, rates, mixing)
    displacement = force.reshape(3, 1, rows, points.shape[3])
    return (current, displacement, arrived)


def solution(mesh):
    return jax.shard_map(
        on_device,
        mesh=mesh,
        in_specs=(
            P(None, "gx", "gy", None),
            P(),
            P(),
            P(None, "gx", "gy", None),
            P(None, "gx", "gy", None),
            P("gx", "gy", None),
            P("gx", "gy", None),
            P("gx", "gy", None),
            P(None, "gx", "gy"),
            P(None, "gx", "gy"),
        ),
        out_specs=(P(None, "gx", "gy", None), P(None, "gx", "gy", None), P(None, "gx", "gy")),
        check_vma=False,
    )
```

```python
import functools

import jax
import jax.numpy as jnp
from jax import lax
from jax.experimental import pallas as pl
from jax.experimental.pallas import tpu as pltpu
from jax.sharding import PartitionSpec as P

BIN_XY = 4
BIN_Z = 8
SLOTS = 16
SUBSTEPS = 4


time_step = 0.15
move_step = 0.1
spread_sq = 8.0
shifts = ((-1, -1), (-1, 0), (-1, 1), (0, -1), (0, 1), (1, -1), (1, 0), (1, 1))


def padded_2(cells, sides, width):
    for axis, dim in sides:
        count = lax.axis_size(axis)
        ends = count - 1
        head = lax.slice_in_dim(cells, 0, width, axis=dim)
        tail = lax.slice_in_dim(cells, cells.shape[dim] - width, cells.shape[dim], axis=dim)
        cells = jnp.concatenate(
            [
                lax.ppermute(tail, axis, [(i, (i + 1) % count) for i in range(ends)]),
                cells,
                lax.ppermute(head, axis, [((i + 1) % count, i) for i in range(ends)]),
            ],
            axis=dim,
        )
    return cells


def halos(cells, axis, dim):
    count = lax.axis_size(axis)
    ends = count - 1
    head = lax.slice_in_dim(cells, 0, 1, axis=dim)
    tail = lax.slice_in_dim(cells, cells.shape[dim] - 1, cells.shape[dim], axis=dim)
    low = lax.ppermute(tail, axis, [(i, (i + 1) % count) for i in range(ends)])
    high = lax.ppermute(head, axis, [((i + 1) % count, i) for i in range(ends)])
    return low, high


def framed(cells, x_low, x_high, y_low, y_high):
    species, width, depth, lanes = cells.shape
    corner = jnp.zeros((species, 1, 1, lanes), cells.dtype)
    middle = jnp.concatenate([x_low, cells, x_high], axis=1)
    left = jnp.concatenate([corner, y_low, corner], axis=1)
    right = jnp.concatenate([corner, y_high, corner], axis=1)
    return jnp.concatenate([left, middle, right], axis=2)


def substep_beside(current, source, rates, mixing, work):
    x_low, x_high = halos(current, "gx", 1)
    y_low, y_high = halos(current, "gy", 2)
    done = work()
    current, done = lax.optimization_barrier((current, done))
    padded = framed(current, x_low, x_high, y_low, y_high)
    return advance(padded, source, rates, mixing), done


def substep(current, source, rates, mixing):
    x_low, x_high = halos(current, "gx", 1)
    y_low, y_high = halos(current, "gy", 2)
    padded = framed(current, x_low, x_high, y_low, y_high)
    return advance(padded, source, rates, mixing)


def shifted(block, axis, distance):
    devices = range(lax.axis_size(axis))
    route = [(i - distance, i) for i in devices if i - distance in devices]
    return lax.ppermute(block, axis, route)


def advance(padded, source, rates, mixing):
    center = padded[:, 1:-1, 1:-1, :]
    deeper = jnp.pad(center, ((0, 0), (0, 0), (0, 0), (1, 1)))
    beside = padded[:, 2:, 1:-1, :] + padded[:, :-2, 1:-1, :]
    beside = beside + padded[:, 1:-1, 2:, :] + padded[:, 1:-1, :-2, :]
    beside = beside + deeper[:, :, :, 2:] + deeper[:, :, :, :-2]
    laplace = beside - 6.0 * center
    species = center.shape[0]
    mixed = jnp.dot(mixing, center.reshape(species, -1), precision=lax.Precision.HIGHEST).reshape(
        center.shape
    )
    return (
        center
        + time_step * (rates[:, None, None, None] * laplace)
        + time_step * mixed
        + time_step * source
    )


def deposit_kernel(rates_ref, code_ref, out_ref, spread_ref, place_ref):
    slots, rows, layers = rates_ref.shape
    bins_y = code_ref.shape[1]
    species = rows // bins_y
    lanes = layers * BIN_Z
    layer_of = lax.broadcasted_iota(jnp.int32, (layers, lanes), 1) // BIN_Z
    expand = (lax.broadcasted_iota(jnp.int32, (layers, lanes), 0) == layer_of).astype(jnp.float32)
    for slot in range(slots):
        spread_ref[slot] = jnp.dot(rates_ref[slot], expand, precision=lax.Precision.HIGHEST, preferred_element_type=jnp.float32)
        place_ref[slot] = jnp.dot(code_ref[slot], expand, precision=lax.Precision.HIGHEST, preferred_element_type=jnp.float32)
    depth = lax.broadcasted_iota(jnp.int32, (1, lanes), 1) % BIN_Z

    def body(index, carry):
        cell_x = index // (bins_y * BIN_XY)
        row_y = index % (bins_y * BIN_XY)
        bin_y = row_y // BIN_XY
        cell_y = row_y % BIN_XY
        target = (depth + (cell_x * (BIN_XY * BIN_Z) + cell_y * BIN_Z)).astype(jnp.float32)
        first = pl.multiple_of(bin_y * species, species)
        total = jnp.zeros((species, lanes), jnp.float32)
        for slot in range(slots):
            hit = place_ref[slot, pl.ds(bin_y, 1), :] == target
            total = total + jnp.where(hit, spread_ref[slot, pl.ds(first, species), :], 0.0)
        out_ref[cell_x, row_y] = total
        return carry

    lax.fori_loop(0, BIN_XY * bins_y * BIN_XY, body, 0)


def deposit(secretion, occupancy, offsets):
    species, bins_x, bins_y, lanes = secretion.shape
    layers = lanes // SLOTS
    rates_slot = secretion.reshape(species, bins_y, layers, SLOTS)
    rates_slot = jnp.transpose(rates_slot, (3, 1, 0, 2)).reshape(SLOTS, bins_y * species, layers)
    code = jnp.where(occupancy != 0, offsets, -1).astype(jnp.float32).reshape(bins_y, layers, SLOTS)
    code = jnp.transpose(code, (2, 0, 1))
    out = pl.pallas_call(
        deposit_kernel,
        out_shape=jax.ShapeDtypeStruct((BIN_XY, bins_y * BIN_XY, species, layers * BIN_Z), jnp.float32),
        scratch_shapes=[
            pltpu.VMEM((SLOTS, bins_y * species, layers * BIN_Z), jnp.float32),
            pltpu.VMEM((SLOTS, bins_y, layers * BIN_Z), jnp.float32),
        ],
        cost_estimate=pl.CostEstimate(flops=10_000_000, transcendentals=0, bytes_accessed=1_300_000),
    )(rates_slot, code)
    return jnp.transpose(out, (2, 0, 1, 3))

def pair_forces(points, padded, occupancy):
    planes, bins_x, bins_y, lanes = points.shape
    layers = lanes // SLOTS
    boxed = padded.reshape(planes, bins_x + 2, bins_y + 2, layers, SLOTS)
    boxed = jnp.pad(boxed, ((0, 0), (0, 0), (0, 0), (1, 1), (0, 0)))
    owned = points.reshape(planes, bins_x, bins_y, layers, SLOTS)[:3, :, :, :, :, None]
    force = jnp.zeros((3, bins_x, bins_y, layers, SLOTS), jnp.float32)
    for offset_x in range(3):
        nearby = jnp.concatenate(
            [
                boxed[
                    :,
                    offset_x : offset_x + bins_x,
                    offset_y : offset_y + bins_y,
                    offset_z : offset_z + layers,
                    :,
                ]
                for offset_y in range(3)
                for offset_z in range(3)
            ],
            axis=-1,
        )
        apart = owned - nearby[:3, :, :, :, None, :]
        strength = nearby[3][:, :, :, None, :] * jnp.exp(
            -jnp.sum(apart * apart, axis=0) / spread_sq
        )
        force = force + jnp.sum(apart * strength[None], axis=-1)
    active = occupancy.reshape(1, bins_x, bins_y, layers, SLOTS).astype(jnp.float32)
    return (move_step * active * force).reshape(3, bins_x, bins_y, lanes)


def storage_order(piece):
    if piece.ndim == 4 and piece.shape[0] > 4:
        return (1, 2, 0, 3)
    return tuple(range(piece.ndim))


def pack(pieces):
    return jnp.concatenate(
        [jnp.transpose(piece, storage_order(piece)).reshape(-1, 128) for piece in pieces], axis=0
    )


def unpack(flat, pieces):
    out = []
    row = 0
    for piece in pieces:
        rows = piece.size // 128
        order = storage_order(piece)
        stored = flat[row : row + rows].reshape(tuple(piece.shape[axis] for axis in order))
        out.append(jnp.transpose(stored, tuple(order.index(axis) for axis in range(piece.ndim))))
        row += rows
    return out


def send_pair(axis, upward, downward):
    count = lax.axis_size(axis)
    up = [(i, i + 1) for i in range(count - 1)]
    down = [(i + 1, i) for i in range(count - 1)]
    below = lax.ppermute(pack(upward), axis, up)
    above = lax.ppermute(pack(downward), axis, down)
    return unpack(below, upward), unpack(above, downward), below, above


def forces_kernel(shifts, scale, own_ref, near_ref, occ_ref, start_ref, out_ref, mine_ref, other_ref):
    rows = own_ref.shape[1]
    lanes = own_ref.shape[-1]
    layers = lanes // SLOTS
    stacked = mine_ref.shape[1]
    groups = 9
    mine_ref[...] = jnp.zeros_like(mine_ref)
    other_ref[...] = jnp.zeros_like(other_ref)
    for plane in range(4):
        for offset_x in range(3):
            for offset_y in range(3):
                group = (offset_x * 3 + offset_y) * rows
                other_ref[plane, group : group + rows, :] = near_ref[plane, offset_x, offset_y : offset_y + rows, :]
                if plane < 3:
                    mine_ref[plane, group : group + rows, :] = own_ref[plane]
    px = mine_ref[0]
    py = mine_ref[1]
    pz = mine_ref[2]
    lane = lax.broadcasted_iota(jnp.int32, (stacked, lanes), 1)
    slot = lane % SLOTS
    layer = lane // SLOTS
    fx = start_ref[0]
    fy = start_ref[1]
    fz = start_ref[2]
    row = [other_ref[plane] for plane in range(4)]
    for offset_z in shifts:
        if offset_z == 0:
            base = row
        else:
            inside = (layer + offset_z >= 0) & (layer + offset_z < layers)
            base = [jnp.where(inside, pltpu.roll(part, (-offset_z * SLOTS) % lanes, 1), 0.0) for part in row]
        for turn in range(SLOTS):
            if turn == 0:
                other = base
            else:
                keep = slot + turn < SLOTS
                other = [
                    jnp.where(keep, pltpu.roll(part, lanes - turn, 1), pltpu.roll(part, SLOTS - turn, 1))
                    for part in base
                ]
            dx = px - other[0]
            dy = py - other[1]
            dz = pz - other[2]
            strength = other[3] * jnp.exp(-(dx * dx + dy * dy + dz * dz) / spread_sq)
            fx = fx + dx * strength
            fy = fy + dy * strength
            fz = fz + dz * strength
    if scale:
        active = move_step * occ_ref[...]
        for plane, total in enumerate((fx, fy, fz)):
            summed = total[0:rows]
            for group in range(1, groups):
                summed = summed + total[group * rows : (group + 1) * rows]
            out_ref[plane, 0:rows, :] = active * summed
    else:
        out_ref[0] = fx
        out_ref[1] = fy
        out_ref[2] = fz


def pallas_forces(points, bordered, occupancy, partial, shifts, scale):
    planes, _, rows, lanes = points.shape
    stacked = -(-9 * rows // 8) * 8
    if partial is None:
        partial = jnp.zeros((3, stacked, lanes), jnp.float32)
    out_rows = rows if scale else stacked
    return pl.pallas_call(
        functools.partial(forces_kernel, shifts, scale),
        out_shape=jax.ShapeDtypeStruct((3, out_rows, lanes), jnp.float32),
        scratch_shapes=[pltpu.VMEM((3, stacked, lanes), jnp.float32), pltpu.VMEM((4, stacked, lanes), jnp.float32)],
        cost_estimate=pl.CostEstimate(
            flops=3_000_000 * len(shifts), transcendentals=150_000 * len(shifts), bytes_accessed=150_000
        ),
    )(points[:, 0], bordered, occupancy[0].astype(jnp.float32), partial)


def arrived_kernel(starts, state, x_below, x_above, side_below, side_above, corner_below, corner_above, out_ref):
    along_x, beside, corner = starts
    span = state

    def rows(ref, first):
        return ref[first : first + span, :]

    out_ref[0] = rows(corner_above, corner)
    out_ref[1] = rows(x_above, along_x + span)
    out_ref[2] = rows(corner_below, corner)
    out_ref[3] = rows(side_above, beside)
    out_ref[4] = rows(side_below, beside)
    out_ref[5] = rows(corner_above, corner + span)
    out_ref[6] = rows(x_below, along_x + span)
    out_ref[7] = rows(corner_below, corner + span)


def gather_arrived(x_flats, side_flats, corner_flats, along_x, beside, corner, shape):
    state, lanes = shape
    return pl.pallas_call(
        functools.partial(arrived_kernel, (along_x, beside, corner), state),
        out_shape=jax.ShapeDtypeStruct((8, state, lanes), jnp.float32),
        cost_estimate=pl.CostEstimate(flops=0, transcendentals=0, bytes_accessed=300_000),
    )(*x_flats, *side_flats, *corner_flats)


def on_device(
    field,
    rates,
    mixing,
    secretion,
    positions,
    stiffness,
    occupancy,
    offsets,
    migrant_state,
    migrant_live,
):
    weight = stiffness * occupancy.astype(jnp.float32)
    points = jnp.concatenate([positions, weight[None]], axis=0)
    payload = migrant_state * migrant_live.astype(jnp.float32)
    source = deposit(secretion, occupancy, offsets)
    current = field

    (x_low, points_low, moved_up), (x_high, points_high, moved_down), *x_flats = send_pair(
        "gx",
        [current[:, -1:], points, payload[5:8]],
        [current[:, :1], points, payload[0:3]],
    )
    (y_low, beside_up), (y_high, beside_down), *side_flats = send_pair(
        "gy",
        [current[:, :, -1:], payload[4:5]],
        [current[:, :, :1], payload[3:4]],
    )
    current = advance(framed(current, x_low, x_high, y_low, y_high), source, rates, mixing)

    row_points = jnp.concatenate([points_low, points, points_high], axis=1)
    x_low, x_high = halos(current, "gx", 1)
    (y_low, points_low, corner_up), (y_high, points_high, corner_down), *corner_flats = send_pair(
        "gy",
        [current[:, :, -1:], row_points[:, :, -1:], jnp.stack([moved_down[2], moved_up[2]])],
        [current[:, :, :1], row_points[:, :, :1], jnp.stack([moved_down[0], moved_up[0]])],
    )
    bordered = jnp.concatenate([points_low, row_points, points_high], axis=2)
    field_rows = x_low.size // 128
    side_rows = y_low.size // 128
    starts = (field_rows + points.size // 128, side_rows, side_rows + points_low.size // 128)
    rows = points.shape[2]
    arrived = gather_arrived(x_flats, side_flats, corner_flats, *starts, payload.shape[1:])
    current, arrived = lax.optimization_barrier((current, arrived))
    current = advance(framed(current, x_low, x_high, y_low, y_high), source, rates, mixing)
    current, bordered = lax.optimization_barrier((current, bordered))

    def first_work():
        return pallas_forces(points, bordered, occupancy, None, (-1, 0), False)

    current, partial = substep_beside(current, source, rates, mixing, first_work)
    current, partial = lax.optimization_barrier((current, partial))

    def last_work():
        return pallas_forces(points, bordered, occupancy, partial, (1,), True)

    current, force = substep_beside(current, source, rates, mixing, last_work)
    displacement = force.reshape(3, 1, rows, points.shape[3])
    return (current, displacement, arrived)


def solution(mesh):
    return jax.shard_map(
        on_device,
        mesh=mesh,
        in_specs=(
            P(None, "gx", "gy", None),
            P(),
            P(),
            P(None, "gx", "gy", None),
            P(None, "gx", "gy", None),
            P("gx", "gy", None),
            P("gx", "gy", None),
            P("gx", "gy", None),
            P(None, "gx", "gy"),
            P(None, "gx", "gy"),
        ),
        out_specs=(P(None, "gx", "gy", None), P(None, "gx", "gy", None), P(None, "gx", "gy")),
        check_vma=False,
    )
```

```python
import functools

import jax
import jax.numpy as jnp
from jax import lax
from jax.experimental import pallas as pl
from jax.experimental.pallas import tpu as pltpu
from jax.sharding import PartitionSpec as P

BIN_XY = 4
BIN_Z = 8
SLOTS = 16
SUBSTEPS = 4


time_step = 0.15
move_step = 0.1
spread_sq = 8.0
shifts = ((-1, -1), (-1, 0), (-1, 1), (0, -1), (0, 1), (1, -1), (1, 0), (1, 1))


def padded_2(cells, sides, width):
    for axis, dim in sides:
        count = lax.axis_size(axis)
        ends = count - 1
        head = lax.slice_in_dim(cells, 0, width, axis=dim)
        tail = lax.slice_in_dim(cells, cells.shape[dim] - width, cells.shape[dim], axis=dim)
        cells = jnp.concatenate(
            [
                lax.ppermute(tail, axis, [(i, (i + 1) % count) for i in range(ends)]),
                cells,
                lax.ppermute(head, axis, [((i + 1) % count, i) for i in range(ends)]),
            ],
            axis=dim,
        )
    return cells


def halos(cells, axis, dim):
    count = lax.axis_size(axis)
    ends = count - 1
    head = lax.slice_in_dim(cells, 0, 1, axis=dim)
    tail = lax.slice_in_dim(cells, cells.shape[dim] - 1, cells.shape[dim], axis=dim)
    low = lax.ppermute(tail, axis, [(i, (i + 1) % count) for i in range(ends)])
    high = lax.ppermute(head, axis, [((i + 1) % count, i) for i in range(ends)])
    return low, high


def framed(cells, x_low, x_high, y_low, y_high):
    species, width, depth, lanes = cells.shape
    corner = jnp.zeros((species, 1, 1, lanes), cells.dtype)
    middle = jnp.concatenate([x_low, cells, x_high], axis=1)
    left = jnp.concatenate([corner, y_low, corner], axis=1)
    right = jnp.concatenate([corner, y_high, corner], axis=1)
    return jnp.concatenate([left, middle, right], axis=2)


def substep_beside(current, source, rates, mixing, work):
    x_low, x_high = halos(current, "gx", 1)
    y_low, y_high = halos(current, "gy", 2)
    done = work()
    current, done = lax.optimization_barrier((current, done))
    padded = framed(current, x_low, x_high, y_low, y_high)
    return advance(padded, source, rates, mixing), done


def substep(current, source, rates, mixing):
    x_low, x_high = halos(current, "gx", 1)
    y_low, y_high = halos(current, "gy", 2)
    padded = framed(current, x_low, x_high, y_low, y_high)
    return advance(padded, source, rates, mixing)


def shifted(block, axis, distance):
    devices = range(lax.axis_size(axis))
    route = [(i - distance, i) for i in devices if i - distance in devices]
    return lax.ppermute(block, axis, route)


def advance(padded, source, rates, mixing):
    center = padded[:, 1:-1, 1:-1, :]
    deeper = jnp.pad(center, ((0, 0), (0, 0), (0, 0), (1, 1)))
    beside = padded[:, 2:, 1:-1, :] + padded[:, :-2, 1:-1, :]
    beside = beside + padded[:, 1:-1, 2:, :] + padded[:, 1:-1, :-2, :]
    beside = beside + deeper[:, :, :, 2:] + deeper[:, :, :, :-2]
    laplace = beside - 6.0 * center
    species = center.shape[0]
    mixed = jnp.dot(mixing, center.reshape(species, -1), precision=lax.Precision.HIGHEST).reshape(
        center.shape
    )
    return (
        center
        + time_step * (rates[:, None, None, None] * laplace)
        + time_step * mixed
        + time_step * source
    )


def deposit_kernel(rates_ref, code_ref, out_ref, spread_ref, place_ref):
    slots, rows, layers = rates_ref.shape
    bins_y = code_ref.shape[1]
    species = rows // bins_y
    lanes = layers * BIN_Z
    layer_of = lax.broadcasted_iota(jnp.int32, (layers, lanes), 1) // BIN_Z
    expand = (lax.broadcasted_iota(jnp.int32, (layers, lanes), 0) == layer_of).astype(jnp.float32)
    for slot in range(slots):
        spread_ref[slot] = jnp.dot(rates_ref[slot], expand, precision=lax.Precision.HIGHEST, preferred_element_type=jnp.float32)
        place_ref[slot] = jnp.dot(code_ref[slot], expand, precision=lax.Precision.HIGHEST, preferred_element_type=jnp.float32)
    depth = lax.broadcasted_iota(jnp.int32, (1, lanes), 1) % BIN_Z

    def body(index, carry):
        cell_x = index // (bins_y * BIN_XY)
        row_y = index % (bins_y * BIN_XY)
        bin_y = row_y // BIN_XY
        cell_y = row_y % BIN_XY
        target = (depth + (cell_x * (BIN_XY * BIN_Z) + cell_y * BIN_Z)).astype(jnp.float32)
        first = pl.multiple_of(bin_y * species, species)
        total = jnp.zeros((species, lanes), jnp.float32)
        for slot in range(slots):
            hit = place_ref[slot, pl.ds(bin_y, 1), :] == target
            total = total + jnp.where(hit, spread_ref[slot, pl.ds(first, species), :], 0.0)
        out_ref[cell_x, row_y] = total
        return carry

    lax.fori_loop(0, BIN_XY * bins_y * BIN_XY, body, 0)


def deposit(secretion, occupancy, offsets):
    species, bins_x, bins_y, lanes = secretion.shape
    layers = lanes // SLOTS
    rates_slot = secretion.reshape(species, bins_y, layers, SLOTS)
    rates_slot = jnp.transpose(rates_slot, (3, 1, 0, 2)).reshape(SLOTS, bins_y * species, layers)
    code = jnp.where(occupancy != 0, offsets, -1).astype(jnp.float32).reshape(bins_y, layers, SLOTS)
    code = jnp.transpose(code, (2, 0, 1))
    out = pl.pallas_call(
        deposit_kernel,
        out_shape=jax.ShapeDtypeStruct((BIN_XY, bins_y * BIN_XY, species, layers * BIN_Z), jnp.float32),
        scratch_shapes=[
            pltpu.VMEM((SLOTS, bins_y * species, layers * BIN_Z), jnp.float32),
            pltpu.VMEM((SLOTS, bins_y, layers * BIN_Z), jnp.float32),
        ],
        cost_estimate=pl.CostEstimate(flops=10_000_000, transcendentals=0, bytes_accessed=1_300_000),
    )(rates_slot, code)
    return jnp.transpose(out, (2, 0, 1, 3))

def pair_forces(points, padded, occupancy):
    planes, bins_x, bins_y, lanes = points.shape
    layers = lanes // SLOTS
    boxed = padded.reshape(planes, bins_x + 2, bins_y + 2, layers, SLOTS)
    boxed = jnp.pad(boxed, ((0, 0), (0, 0), (0, 0), (1, 1), (0, 0)))
    owned = points.reshape(planes, bins_x, bins_y, layers, SLOTS)[:3, :, :, :, :, None]
    force = jnp.zeros((3, bins_x, bins_y, layers, SLOTS), jnp.float32)
    for offset_x in range(3):
        nearby = jnp.concatenate(
            [
                boxed[
                    :,
                    offset_x : offset_x + bins_x,
                    offset_y : offset_y + bins_y,
                    offset_z : offset_z + layers,
                    :,
                ]
                for offset_y in range(3)
                for offset_z in range(3)
            ],
            axis=-1,
        )
        apart = owned - nearby[:3, :, :, :, None, :]
        strength = nearby[3][:, :, :, None, :] * jnp.exp(
            -jnp.sum(apart * apart, axis=0) / spread_sq
        )
        force = force + jnp.sum(apart * strength[None], axis=-1)
    active = occupancy.reshape(1, bins_x, bins_y, layers, SLOTS).astype(jnp.float32)
    return (move_step * active * force).reshape(3, bins_x, bins_y, lanes)


def storage_order(piece):
    if piece.ndim == 4 and piece.shape[0] > 4:
        return (1, 2, 0, 3)
    return tuple(range(piece.ndim))


def pack(pieces):
    return jnp.concatenate(
        [jnp.transpose(piece, storage_order(piece)).reshape(-1, 128) for piece in pieces], axis=0
    )


def unpack(flat, pieces):
    out = []
    row = 0
    for piece in pieces:
        rows = piece.size // 128
        order = storage_order(piece)
        stored = flat[row : row + rows].reshape(tuple(piece.shape[axis] for axis in order))
        out.append(jnp.transpose(stored, tuple(order.index(axis) for axis in range(piece.ndim))))
        row += rows
    return out


def send_pair(axis, upward, downward):
    count = lax.axis_size(axis)
    up = [(i, i + 1) for i in range(count - 1)]
    down = [(i + 1, i) for i in range(count - 1)]
    below = lax.ppermute(pack(upward), axis, up)
    above = lax.ppermute(pack(downward), axis, down)
    return unpack(below, upward), unpack(above, downward), below, above


def forces_kernel(shifts, scale, own_ref, near_ref, occ_ref, start_ref, out_ref, mine_ref, other_ref):
    rows = own_ref.shape[1]
    lanes = own_ref.shape[-1]
    layers = lanes // SLOTS
    stacked = mine_ref.shape[1]
    groups = 9
    mine_ref[...] = jnp.zeros_like(mine_ref)
    other_ref[...] = jnp.zeros_like(other_ref)
    for plane in range(4):
        for offset_x in range(3):
            for offset_y in range(3):
                group = (offset_x * 3 + offset_y) * rows
                other_ref[plane, group : group + rows, :] = near_ref[plane, offset_x, offset_y : offset_y + rows, :]
                if plane < 3:
                    mine_ref[plane, group : group + rows, :] = own_ref[plane]
    px = mine_ref[0]
    py = mine_ref[1]
    pz = mine_ref[2]
    lane = lax.broadcasted_iota(jnp.int32, (stacked, lanes), 1)
    slot = lane % SLOTS
    layer = lane // SLOTS
    fx = start_ref[0]
    fy = start_ref[1]
    fz = start_ref[2]
    row = [other_ref[plane] for plane in range(4)]
    for offset_z in shifts:
        if offset_z == 0:
            base = row
        else:
            inside = (layer + offset_z >= 0) & (layer + offset_z < layers)
            base = [jnp.where(inside, pltpu.roll(part, (-offset_z * SLOTS) % lanes, 1), 0.0) for part in row]
        for turn in range(SLOTS):
            if turn == 0:
                other = base
            else:
                keep = slot + turn < SLOTS
                other = [
                    jnp.where(keep, pltpu.roll(part, lanes - turn, 1), pltpu.roll(part, SLOTS - turn, 1))
                    for part in base
                ]
            dx = px - other[0]
            dy = py - other[1]
            dz = pz - other[2]
            strength = other[3] * jnp.exp(-(dx * dx + dy * dy + dz * dz) / spread_sq)
            fx = fx + dx * strength
            fy = fy + dy * strength
            fz = fz + dz * strength
    if scale:
        active = move_step * occ_ref[...]
        for plane, total in enumerate((fx, fy, fz)):
            summed = total[0:rows]
            for group in range(1, groups):
                summed = summed + total[group * rows : (group + 1) * rows]
            out_ref[plane, 0:rows, :] = active * summed
    else:
        out_ref[0] = fx
        out_ref[1] = fy
        out_ref[2] = fz


def pallas_forces(points, bordered, occupancy, partial, shifts, scale):
    planes, _, rows, lanes = points.shape
    stacked = -(-9 * rows // 8) * 8
    if partial is None:
        partial = jnp.zeros((3, stacked, lanes), jnp.float32)
    out_rows = rows if scale else stacked
    return pl.pallas_call(
        functools.partial(forces_kernel, shifts, scale),
        out_shape=jax.ShapeDtypeStruct((3, out_rows, lanes), jnp.float32),
        scratch_shapes=[pltpu.VMEM((3, stacked, lanes), jnp.float32), pltpu.VMEM((4, stacked, lanes), jnp.float32)],
        cost_estimate=pl.CostEstimate(
            flops=3_000_000 * len(shifts), transcendentals=150_000 * len(shifts), bytes_accessed=150_000
        ),
    )(points[:, 0], bordered, occupancy[0].astype(jnp.float32), partial)


def arrived_kernel(starts, state, x_below, x_above, side_below, side_above, corner_below, corner_above, out_ref):
    along_x, beside, corner = starts
    span = state

    def rows(ref, first):
        return ref[first : first + span, :]

    out_ref[0] = rows(corner_above, corner)
    out_ref[1] = rows(x_above, along_x + span)
    out_ref[2] = rows(corner_below, corner)
    out_ref[3] = rows(side_above, beside)
    out_ref[4] = rows(side_below, beside)
    out_ref[5] = rows(corner_above, corner + span)
    out_ref[6] = rows(x_below, along_x + span)
    out_ref[7] = rows(corner_below, corner + span)


def gather_arrived(x_flats, side_flats, corner_flats, along_x, beside, corner, shape):
    state, lanes = shape
    return pl.pallas_call(
        functools.partial(arrived_kernel, (along_x, beside, corner), state),
        out_shape=jax.ShapeDtypeStruct((8, state, lanes), jnp.float32),
        cost_estimate=pl.CostEstimate(flops=0, transcendentals=0, bytes_accessed=300_000),
    )(*x_flats, *side_flats, *corner_flats)


def on_device(
    field,
    rates,
    mixing,
    secretion,
    positions,
    stiffness,
    occupancy,
    offsets,
    migrant_state,
    migrant_live,
):
    weight = stiffness * occupancy.astype(jnp.float32)
    points = jnp.concatenate([positions, weight[None]], axis=0)
    payload = migrant_state * migrant_live.astype(jnp.float32)
    source = deposit(secretion, occupancy, offsets)
    current = field

    (x_low, points_low, moved_up), (x_high, points_high, moved_down), *x_flats = send_pair(
        "gx",
        [current[:, -1:], points, payload[5:8]],
        [current[:, :1], points, payload[0:3]],
    )
    (y_low, beside_up), (y_high, beside_down), *side_flats = send_pair(
        "gy",
        [current[:, :, -1:], payload[4:5]],
        [current[:, :, :1], payload[3:4]],
    )
    current = advance(framed(current, x_low, x_high, y_low, y_high), source, rates, mixing)

    row_points = jnp.concatenate([points_low, points, points_high], axis=1)
    x_low, x_high = halos(current, "gx", 1)
    (y_low, points_low, corner_up), (y_high, points_high, corner_down), *corner_flats = send_pair(
        "gy",
        [current[:, :, -1:], row_points[:, :, -1:], jnp.stack([moved_down[2], moved_up[2]])],
        [current[:, :, :1], row_points[:, :, :1], jnp.stack([moved_down[0], moved_up[0]])],
    )
    bordered = jnp.concatenate([points_low, row_points, points_high], axis=2)
    field_rows = x_low.size // 128
    side_rows = y_low.size // 128
    starts = (field_rows + points.size // 128, side_rows, side_rows + points_low.size // 128)
    rows = points.shape[2]
    arrived = gather_arrived(x_flats, side_flats, corner_flats, *starts, payload.shape[1:])
    force = pallas_forces(points, bordered, occupancy, None, (-1, 0, 1), True)
    current, arrived, force = lax.optimization_barrier((current, arrived, force))
    current = advance(framed(current, x_low, x_high, y_low, y_high), source, rates, mixing)
    current = substep(current, source, rates, mixing)
    current = substep(current, source, rates, mixing)
    displacement = force.reshape(3, 1, rows, points.shape[3])
    return (current, displacement, arrived)


def solution(mesh):
    return jax.shard_map(
        on_device,
        mesh=mesh,
        in_specs=(
            P(None, "gx", "gy", None),
            P(),
            P(),
            P(None, "gx", "gy", None),
            P(None, "gx", "gy", None),
            P("gx", "gy", None),
            P("gx", "gy", None),
            P("gx", "gy", None),
            P(None, "gx", "gy"),
            P(None, "gx", "gy"),
        ),
        out_specs=(P(None, "gx", "gy", None), P(None, "gx", "gy", None), P(None, "gx", "gy")),
        check_vma=False,
    )
```

```python
import functools

import jax
import jax.numpy as jnp
from jax import lax
from jax.experimental import pallas as pl
from jax.experimental.pallas import tpu as pltpu
from jax.sharding import PartitionSpec as P

BIN_XY = 4
BIN_Z = 8
SLOTS = 16
SUBSTEPS = 4


time_step = 0.15
move_step = 0.1
spread_sq = 8.0
shifts = ((-1, -1), (-1, 0), (-1, 1), (0, -1), (0, 1), (1, -1), (1, 0), (1, 1))


def padded_2(cells, sides, width):
    for axis, dim in sides:
        count = lax.axis_size(axis)
        ends = count - 1
        head = lax.slice_in_dim(cells, 0, width, axis=dim)
        tail = lax.slice_in_dim(cells, cells.shape[dim] - width, cells.shape[dim], axis=dim)
        cells = jnp.concatenate(
            [
                lax.ppermute(tail, axis, [(i, (i + 1) % count) for i in range(ends)]),
                cells,
                lax.ppermute(head, axis, [((i + 1) % count, i) for i in range(ends)]),
            ],
            axis=dim,
        )
    return cells


def halos(cells, axis, dim):
    count = lax.axis_size(axis)
    ends = count - 1
    head = lax.slice_in_dim(cells, 0, 1, axis=dim)
    tail = lax.slice_in_dim(cells, cells.shape[dim] - 1, cells.shape[dim], axis=dim)
    low = lax.ppermute(tail, axis, [(i, (i + 1) % count) for i in range(ends)])
    high = lax.ppermute(head, axis, [((i + 1) % count, i) for i in range(ends)])
    return low, high


def framed(cells, x_low, x_high, y_low, y_high):
    species, width, depth, lanes = cells.shape
    corner = jnp.zeros((species, 1, 1, lanes), cells.dtype)
    middle = jnp.concatenate([x_low, cells, x_high], axis=1)
    left = jnp.concatenate([corner, y_low, corner], axis=1)
    right = jnp.concatenate([corner, y_high, corner], axis=1)
    return jnp.concatenate([left, middle, right], axis=2)


def substep_beside(current, source, rates, mixing, work):
    x_low, x_high = halos(current, "gx", 1)
    y_low, y_high = halos(current, "gy", 2)
    done = work()
    current, done = lax.optimization_barrier((current, done))
    padded = framed(current, x_low, x_high, y_low, y_high)
    return advance(padded, source, rates, mixing), done


def substep(current, source, rates, mixing):
    x_low, x_high = halos(current, "gx", 1)
    y_low, y_high = halos(current, "gy", 2)
    padded = framed(current, x_low, x_high, y_low, y_high)
    return advance(padded, source, rates, mixing)


def shifted(block, axis, distance):
    devices = range(lax.axis_size(axis))
    route = [(i - distance, i) for i in devices if i - distance in devices]
    return lax.ppermute(block, axis, route)


def advance(padded, source, rates, mixing):
    center = padded[:, 1:-1, 1:-1, :]
    deeper = jnp.pad(center, ((0, 0), (0, 0), (0, 0), (1, 1)))
    beside = padded[:, 2:, 1:-1, :] + padded[:, :-2, 1:-1, :]
    beside = beside + padded[:, 1:-1, 2:, :] + padded[:, 1:-1, :-2, :]
    beside = beside + deeper[:, :, :, 2:] + deeper[:, :, :, :-2]
    laplace = beside - 6.0 * center
    species = center.shape[0]
    mixed = jnp.dot(mixing, center.reshape(species, -1), precision=lax.Precision.HIGHEST).reshape(
        center.shape
    )
    return (
        center
        + time_step * (rates[:, None, None, None] * laplace)
        + time_step * mixed
        + time_step * source
    )


def deposit_kernel(rates_ref, code_ref, out_ref, spread_ref, place_ref):
    slots, rows, layers = rates_ref.shape
    bins_y = code_ref.shape[1]
    species = rows // bins_y
    lanes = layers * BIN_Z
    layer_of = lax.broadcasted_iota(jnp.int32, (layers, lanes), 1) // BIN_Z
    expand = (lax.broadcasted_iota(jnp.int32, (layers, lanes), 0) == layer_of).astype(jnp.float32)
    for slot in range(slots):
        spread_ref[slot] = jnp.dot(rates_ref[slot], expand, precision=lax.Precision.HIGHEST, preferred_element_type=jnp.float32)
        place_ref[slot] = jnp.dot(code_ref[slot], expand, precision=lax.Precision.HIGHEST, preferred_element_type=jnp.float32)
    depth = lax.broadcasted_iota(jnp.int32, (1, lanes), 1) % BIN_Z

    def body(index, carry):
        cell_x = index // (bins_y * BIN_XY)
        row_y = index % (bins_y * BIN_XY)
        bin_y = row_y // BIN_XY
        cell_y = row_y % BIN_XY
        target = (depth + (cell_x * (BIN_XY * BIN_Z) + cell_y * BIN_Z)).astype(jnp.float32)
        first = pl.multiple_of(bin_y * species, species)
        total = jnp.zeros((species, lanes), jnp.float32)
        for slot in range(slots):
            hit = place_ref[slot, pl.ds(bin_y, 1), :] == target
            total = total + jnp.where(hit, spread_ref[slot, pl.ds(first, species), :], 0.0)
        out_ref[cell_x, row_y] = total
        return carry

    lax.fori_loop(0, BIN_XY * bins_y * BIN_XY, body, 0)


def deposit(secretion, occupancy, offsets):
    species, bins_x, bins_y, lanes = secretion.shape
    layers = lanes // SLOTS
    rates_slot = secretion.reshape(species, bins_y, layers, SLOTS)
    rates_slot = jnp.transpose(rates_slot, (3, 1, 0, 2)).reshape(SLOTS, bins_y * species, layers)
    code = jnp.where(occupancy != 0, offsets, -1).astype(jnp.float32).reshape(bins_y, layers, SLOTS)
    code = jnp.transpose(code, (2, 0, 1))
    out = pl.pallas_call(
        deposit_kernel,
        out_shape=jax.ShapeDtypeStruct((BIN_XY, bins_y * BIN_XY, species, layers * BIN_Z), jnp.float32),
        scratch_shapes=[
            pltpu.VMEM((SLOTS, bins_y * species, layers * BIN_Z), jnp.float32),
            pltpu.VMEM((SLOTS, bins_y, layers * BIN_Z), jnp.float32),
        ],
        cost_estimate=pl.CostEstimate(flops=10_000_000, transcendentals=0, bytes_accessed=1_300_000),
    )(rates_slot, code)
    return jnp.transpose(out, (2, 0, 1, 3))

def pair_forces(points, padded, occupancy):
    planes, bins_x, bins_y, lanes = points.shape
    layers = lanes // SLOTS
    boxed = padded.reshape(planes, bins_x + 2, bins_y + 2, layers, SLOTS)
    boxed = jnp.pad(boxed, ((0, 0), (0, 0), (0, 0), (1, 1), (0, 0)))
    owned = points.reshape(planes, bins_x, bins_y, layers, SLOTS)[:3, :, :, :, :, None]
    force = jnp.zeros((3, bins_x, bins_y, layers, SLOTS), jnp.float32)
    for offset_x in range(3):
        nearby = jnp.concatenate(
            [
                boxed[
                    :,
                    offset_x : offset_x + bins_x,
                    offset_y : offset_y + bins_y,
                    offset_z : offset_z + layers,
                    :,
                ]
                for offset_y in range(3)
                for offset_z in range(3)
            ],
            axis=-1,
        )
        apart = owned - nearby[:3, :, :, :, None, :]
        strength = nearby[3][:, :, :, None, :] * jnp.exp(
            -jnp.sum(apart * apart, axis=0) / spread_sq
        )
        force = force + jnp.sum(apart * strength[None], axis=-1)
    active = occupancy.reshape(1, bins_x, bins_y, layers, SLOTS).astype(jnp.float32)
    return (move_step * active * force).reshape(3, bins_x, bins_y, lanes)


def storage_order(piece):
    if piece.ndim == 4 and piece.shape[0] > 4:
        return (1, 2, 0, 3)
    return tuple(range(piece.ndim))


def pack(pieces):
    return jnp.concatenate(
        [jnp.transpose(piece, storage_order(piece)).reshape(-1, 128) for piece in pieces], axis=0
    )


def unpack(flat, pieces):
    out = []
    row = 0
    for piece in pieces:
        rows = piece.size // 128
        order = storage_order(piece)
        stored = flat[row : row + rows].reshape(tuple(piece.shape[axis] for axis in order))
        out.append(jnp.transpose(stored, tuple(order.index(axis) for axis in range(piece.ndim))))
        row += rows
    return out


def send_pair(axis, upward, downward):
    count = lax.axis_size(axis)
    up = [(i, i + 1) for i in range(count - 1)]
    down = [(i + 1, i) for i in range(count - 1)]
    below = lax.ppermute(pack(upward), axis, up)
    above = lax.ppermute(pack(downward), axis, down)
    return unpack(below, upward), unpack(above, downward), below, above


def forces_kernel(shifts, scale, own_ref, near_ref, occ_ref, start_ref, out_ref, mine_ref, other_ref):
    rows = own_ref.shape[1]
    lanes = own_ref.shape[-1]
    layers = lanes // SLOTS
    stacked = mine_ref.shape[1]
    groups = 9
    mine_ref[...] = jnp.zeros_like(mine_ref)
    other_ref[...] = jnp.zeros_like(other_ref)
    for plane in range(4):
        for offset_x in range(3):
            for offset_y in range(3):
                group = (offset_x * 3 + offset_y) * rows
                other_ref[plane, group : group + rows, :] = near_ref[plane, offset_x, offset_y : offset_y + rows, :]
                if plane < 3:
                    mine_ref[plane, group : group + rows, :] = own_ref[plane]
    px = mine_ref[0]
    py = mine_ref[1]
    pz = mine_ref[2]
    lane = lax.broadcasted_iota(jnp.int32, (stacked, lanes), 1)
    slot = lane % SLOTS
    layer = lane // SLOTS
    fx = start_ref[0]
    fy = start_ref[1]
    fz = start_ref[2]
    row = [other_ref[plane] for plane in range(4)]
    for offset_z in shifts:
        if offset_z == 0:
            base = row
        else:
            inside = (layer + offset_z >= 0) & (layer + offset_z < layers)
            base = [jnp.where(inside, pltpu.roll(part, (-offset_z * SLOTS) % lanes, 1), 0.0) for part in row]
        for turn in range(SLOTS):
            if turn == 0:
                other = base
            else:
                keep = slot + turn < SLOTS
                other = [
                    jnp.where(keep, pltpu.roll(part, lanes - turn, 1), pltpu.roll(part, SLOTS - turn, 1))
                    for part in base
                ]
            dx = px - other[0]
            dy = py - other[1]
            dz = pz - other[2]
            strength = other[3] * jnp.exp(-(dx * dx + dy * dy + dz * dz) / spread_sq)
            fx = fx + dx * strength
            fy = fy + dy * strength
            fz = fz + dz * strength
    if scale:
        active = move_step * occ_ref[...]
        for plane, total in enumerate((fx, fy, fz)):
            summed = total[0:rows]
            for group in range(1, groups):
                summed = summed + total[group * rows : (group + 1) * rows]
            out_ref[plane, 0:rows, :] = active * summed
    else:
        out_ref[0] = fx
        out_ref[1] = fy
        out_ref[2] = fz


def pallas_forces(points, bordered, occupancy, partial, shifts, scale):
    planes, _, rows, lanes = points.shape
    stacked = -(-9 * rows // 8) * 8
    if partial is None:
        partial = jnp.zeros((3, stacked, lanes), jnp.float32)
    out_rows = rows if scale else stacked
    return pl.pallas_call(
        functools.partial(forces_kernel, shifts, scale),
        out_shape=jax.ShapeDtypeStruct((3, out_rows, lanes), jnp.float32),
        scratch_shapes=[pltpu.VMEM((3, stacked, lanes), jnp.float32), pltpu.VMEM((4, stacked, lanes), jnp.float32)],
        cost_estimate=pl.CostEstimate(
            flops=3_000_000 * len(shifts), transcendentals=150_000 * len(shifts), bytes_accessed=150_000
        ),
    )(points[:, 0], bordered, occupancy[0].astype(jnp.float32), partial)


def arrived_kernel(starts, state, x_below, x_above, side_below, side_above, corner_below, corner_above, out_ref):
    along_x, beside, corner = starts
    span = state

    def rows(ref, first):
        return ref[first : first + span, :]

    out_ref[0] = rows(corner_above, corner)
    out_ref[1] = rows(x_above, along_x + span)
    out_ref[2] = rows(corner_below, corner)
    out_ref[3] = rows(side_above, beside)
    out_ref[4] = rows(side_below, beside)
    out_ref[5] = rows(corner_above, corner + span)
    out_ref[6] = rows(x_below, along_x + span)
    out_ref[7] = rows(corner_below, corner + span)


def gather_arrived(x_flats, side_flats, corner_flats, along_x, beside, corner, shape):
    state, lanes = shape
    return pl.pallas_call(
        functools.partial(arrived_kernel, (along_x, beside, corner), state),
        out_shape=jax.ShapeDtypeStruct((8, state, lanes), jnp.float32),
        cost_estimate=pl.CostEstimate(flops=0, transcendentals=0, bytes_accessed=300_000),
    )(*x_flats, *side_flats, *corner_flats)


def on_device(
    field,
    rates,
    mixing,
    secretion,
    positions,
    stiffness,
    occupancy,
    offsets,
    migrant_state,
    migrant_live,
):
    weight = stiffness * occupancy.astype(jnp.float32)
    points = jnp.concatenate([positions, weight[None]], axis=0)
    payload = migrant_state * migrant_live.astype(jnp.float32)
    source = deposit(secretion, occupancy, offsets)
    current = field

    (x_low, points_low, moved_up), (x_high, points_high, moved_down), *x_flats = send_pair(
        "gx",
        [current[:, -1:], points, payload[5:8]],
        [current[:, :1], points, payload[0:3]],
    )
    (y_low, beside_up), (y_high, beside_down), *side_flats = send_pair(
        "gy",
        [current[:, :, -1:], payload[4:5]],
        [current[:, :, :1], payload[3:4]],
    )
    current = advance(framed(current, x_low, x_high, y_low, y_high), source, rates, mixing)

    row_points = jnp.concatenate([points_low, points, points_high], axis=1)
    x_low, x_high = halos(current, "gx", 1)
    (y_low, points_low, corner_up), (y_high, points_high, corner_down), *corner_flats = send_pair(
        "gy",
        [current[:, :, -1:], row_points[:, :, -1:], jnp.stack([moved_down[2], moved_up[2]])],
        [current[:, :, :1], row_points[:, :, :1], jnp.stack([moved_down[0], moved_up[0]])],
    )
    bordered = jnp.concatenate([points_low, row_points, points_high], axis=2)
    field_rows = x_low.size // 128
    side_rows = y_low.size // 128
    starts = (field_rows + points.size // 128, side_rows, side_rows + points_low.size // 128)
    rows = points.shape[2]
    force = pallas_forces(points, bordered, occupancy, None, (-1, 0, 1), True)
    current, force = lax.optimization_barrier((current, force))
    current = advance(framed(current, x_low, x_high, y_low, y_high), source, rates, mixing)
    current, x_flats, side_flats, corner_flats = lax.optimization_barrier((current, x_flats, side_flats, corner_flats))

    def gather():
        return gather_arrived(x_flats, side_flats, corner_flats, *starts, payload.shape[1:])

    current, arrived = substep_beside(current, source, rates, mixing, gather)
    current = substep(current, source, rates, mixing)
    displacement = force.reshape(3, 1, rows, points.shape[3])
    return (current, displacement, arrived)


def solution(mesh):
    return jax.shard_map(
        on_device,
        mesh=mesh,
        in_specs=(
            P(None, "gx", "gy", None),
            P(),
            P(),
            P(None, "gx", "gy", None),
            P(None, "gx", "gy", None),
            P("gx", "gy", None),
            P("gx", "gy", None),
            P("gx", "gy", None),
            P(None, "gx", "gy"),
            P(None, "gx", "gy"),
        ),
        out_specs=(P(None, "gx", "gy", None), P(None, "gx", "gy", None), P(None, "gx", "gy")),
        check_vma=False,
    )
```

```python
import functools

import jax
import jax.numpy as jnp
from jax import lax
from jax.experimental import pallas as pl
from jax.experimental.pallas import tpu as pltpu
from jax.sharding import PartitionSpec as P

BIN_XY = 4
BIN_Z = 8
SLOTS = 16
SUBSTEPS = 4


time_step = 0.15
move_step = 0.1
spread_sq = 8.0
shifts = ((-1, -1), (-1, 0), (-1, 1), (0, -1), (0, 1), (1, -1), (1, 0), (1, 1))


def padded_2(cells, sides, width):
    for axis, dim in sides:
        count = lax.axis_size(axis)
        ends = count - 1
        head = lax.slice_in_dim(cells, 0, width, axis=dim)
        tail = lax.slice_in_dim(cells, cells.shape[dim] - width, cells.shape[dim], axis=dim)
        cells = jnp.concatenate(
            [
                lax.ppermute(tail, axis, [(i, (i + 1) % count) for i in range(ends)]),
                cells,
                lax.ppermute(head, axis, [((i + 1) % count, i) for i in range(ends)]),
            ],
            axis=dim,
        )
    return cells


def halos(cells, axis, dim):
    count = lax.axis_size(axis)
    ends = count - 1
    head = lax.slice_in_dim(cells, 0, 1, axis=dim)
    tail = lax.slice_in_dim(cells, cells.shape[dim] - 1, cells.shape[dim], axis=dim)
    low = lax.ppermute(tail, axis, [(i, (i + 1) % count) for i in range(ends)])
    high = lax.ppermute(head, axis, [((i + 1) % count, i) for i in range(ends)])
    return low, high


def framed(cells, x_low, x_high, y_low, y_high):
    species, width, depth, lanes = cells.shape
    corner = jnp.zeros((species, 1, 1, lanes), cells.dtype)
    middle = jnp.concatenate([x_low, cells, x_high], axis=1)
    left = jnp.concatenate([corner, y_low, corner], axis=1)
    right = jnp.concatenate([corner, y_high, corner], axis=1)
    return jnp.concatenate([left, middle, right], axis=2)


def substep_beside(current, source, rates, mixing, work):
    x_low, x_high = halos(current, "gx", 1)
    y_low, y_high = halos(current, "gy", 2)
    done = work()
    current, done = lax.optimization_barrier((current, done))
    padded = framed(current, x_low, x_high, y_low, y_high)
    return advance(padded, source, rates, mixing), done


def substep(current, source, rates, mixing):
    x_low, x_high = halos(current, "gx", 1)
    y_low, y_high = halos(current, "gy", 2)
    padded = framed(current, x_low, x_high, y_low, y_high)
    return advance(padded, source, rates, mixing)


def shifted(block, axis, distance):
    devices = range(lax.axis_size(axis))
    route = [(i - distance, i) for i in devices if i - distance in devices]
    return lax.ppermute(block, axis, route)


def advance(padded, source, rates, mixing):
    center = padded[:, 1:-1, 1:-1, :]
    deeper = jnp.pad(center, ((0, 0), (0, 0), (0, 0), (1, 1)))
    beside = padded[:, 2:, 1:-1, :] + padded[:, :-2, 1:-1, :]
    beside = beside + padded[:, 1:-1, 2:, :] + padded[:, 1:-1, :-2, :]
    beside = beside + deeper[:, :, :, 2:] + deeper[:, :, :, :-2]
    laplace = beside - 6.0 * center
    species = center.shape[0]
    mixed = jnp.dot(mixing, center.reshape(species, -1), precision=lax.Precision.HIGHEST).reshape(
        center.shape
    )
    return (
        center
        + time_step * (rates[:, None, None, None] * laplace)
        + time_step * mixed
        + time_step * source
    )


def deposit_kernel(rates_ref, code_ref, out_ref, spread_ref, place_ref):
    slots, rows, layers = rates_ref.shape
    bins_y = code_ref.shape[1]
    species = rows // bins_y
    lanes = layers * BIN_Z
    layer_of = lax.broadcasted_iota(jnp.int32, (layers, lanes), 1) // BIN_Z
    expand = (lax.broadcasted_iota(jnp.int32, (layers, lanes), 0) == layer_of).astype(jnp.float32)
    for slot in range(slots):
        spread_ref[slot] = jnp.dot(rates_ref[slot], expand, precision=lax.Precision.HIGHEST, preferred_element_type=jnp.float32)
        place_ref[slot] = jnp.dot(code_ref[slot], expand, precision=lax.Precision.HIGHEST, preferred_element_type=jnp.float32)
    depth = lax.broadcasted_iota(jnp.int32, (1, lanes), 1) % BIN_Z

    def body(index, carry):
        cell_x = index // (bins_y * BIN_XY)
        row_y = index % (bins_y * BIN_XY)
        bin_y = row_y // BIN_XY
        cell_y = row_y % BIN_XY
        target = (depth + (cell_x * (BIN_XY * BIN_Z) + cell_y * BIN_Z)).astype(jnp.float32)
        first = pl.multiple_of(bin_y * species, species)
        total = jnp.zeros((species, lanes), jnp.float32)
        for slot in range(slots):
            hit = place_ref[slot, pl.ds(bin_y, 1), :] == target
            total = total + jnp.where(hit, spread_ref[slot, pl.ds(first, species), :], 0.0)
        out_ref[cell_x, row_y] = total
        return carry

    lax.fori_loop(0, BIN_XY * bins_y * BIN_XY, body, 0)


def deposit(secretion, occupancy, offsets):
    species, bins_x, bins_y, lanes = secretion.shape
    layers = lanes // SLOTS
    rates_slot = secretion.reshape(species, bins_y, layers, SLOTS)
    rates_slot = jnp.transpose(rates_slot, (3, 1, 0, 2)).reshape(SLOTS, bins_y * species, layers)
    code = jnp.where(occupancy != 0, offsets, -1).astype(jnp.float32).reshape(bins_y, layers, SLOTS)
    code = jnp.transpose(code, (2, 0, 1))
    out = pl.pallas_call(
        deposit_kernel,
        out_shape=jax.ShapeDtypeStruct((BIN_XY, bins_y * BIN_XY, species, layers * BIN_Z), jnp.float32),
        scratch_shapes=[
            pltpu.VMEM((SLOTS, bins_y * species, layers * BIN_Z), jnp.float32),
            pltpu.VMEM((SLOTS, bins_y, layers * BIN_Z), jnp.float32),
        ],
        cost_estimate=pl.CostEstimate(flops=10_000_000, transcendentals=0, bytes_accessed=1_300_000),
    )(rates_slot, code)
    return jnp.transpose(out, (2, 0, 1, 3))

def pair_forces(points, padded, occupancy):
    planes, bins_x, bins_y, lanes = points.shape
    layers = lanes // SLOTS
    boxed = padded.reshape(planes, bins_x + 2, bins_y + 2, layers, SLOTS)
    boxed = jnp.pad(boxed, ((0, 0), (0, 0), (0, 0), (1, 1), (0, 0)))
    owned = points.reshape(planes, bins_x, bins_y, layers, SLOTS)[:3, :, :, :, :, None]
    force = jnp.zeros((3, bins_x, bins_y, layers, SLOTS), jnp.float32)
    for offset_x in range(3):
        nearby = jnp.concatenate(
            [
                boxed[
                    :,
                    offset_x : offset_x + bins_x,
                    offset_y : offset_y + bins_y,
                    offset_z : offset_z + layers,
                    :,
                ]
                for offset_y in range(3)
                for offset_z in range(3)
            ],
            axis=-1,
        )
        apart = owned - nearby[:3, :, :, :, None, :]
        strength = nearby[3][:, :, :, None, :] * jnp.exp(
            -jnp.sum(apart * apart, axis=0) / spread_sq
        )
        force = force + jnp.sum(apart * strength[None], axis=-1)
    active = occupancy.reshape(1, bins_x, bins_y, layers, SLOTS).astype(jnp.float32)
    return (move_step * active * force).reshape(3, bins_x, bins_y, lanes)


def storage_order(piece):
    if piece.ndim == 4 and piece.shape[0] > 4:
        return (1, 2, 0, 3)
    return tuple(range(piece.ndim))


def pack(pieces):
    return jnp.concatenate(
        [jnp.transpose(piece, storage_order(piece)).reshape(-1, 128) for piece in pieces], axis=0
    )


def unpack(flat, pieces):
    out = []
    row = 0
    for piece in pieces:
        rows = piece.size // 128
        order = storage_order(piece)
        stored = flat[row : row + rows].reshape(tuple(piece.shape[axis] for axis in order))
        out.append(jnp.transpose(stored, tuple(order.index(axis) for axis in range(piece.ndim))))
        row += rows
    return out


def send_pair(axis, upward, downward):
    count = lax.axis_size(axis)
    up = [(i, i + 1) for i in range(count - 1)]
    down = [(i + 1, i) for i in range(count - 1)]
    below = lax.ppermute(pack(upward), axis, up)
    above = lax.ppermute(pack(downward), axis, down)
    return unpack(below, upward), unpack(above, downward), below, above


def forces_kernel(shifts, scale, own_ref, near_ref, occ_ref, start_ref, out_ref, mine_ref, other_ref):
    rows = own_ref.shape[1]
    lanes = own_ref.shape[-1]
    layers = lanes // SLOTS
    stacked = mine_ref.shape[1]
    groups = 9
    mine_ref[...] = jnp.zeros_like(mine_ref)
    other_ref[...] = jnp.zeros_like(other_ref)
    for plane in range(4):
        for offset_x in range(3):
            for offset_y in range(3):
                group = (offset_x * 3 + offset_y) * rows
                other_ref[plane, group : group + rows, :] = near_ref[plane, offset_x, offset_y : offset_y + rows, :]
                if plane < 3:
                    mine_ref[plane, group : group + rows, :] = own_ref[plane]
    px = mine_ref[0]
    py = mine_ref[1]
    pz = mine_ref[2]
    lane = lax.broadcasted_iota(jnp.int32, (stacked, lanes), 1)
    slot = lane % SLOTS
    layer = lane // SLOTS
    fx = start_ref[0]
    fy = start_ref[1]
    fz = start_ref[2]
    row = [other_ref[plane] for plane in range(4)]
    for offset_z in shifts:
        if offset_z == 0:
            base = row
        else:
            inside = (layer + offset_z >= 0) & (layer + offset_z < layers)
            base = [jnp.where(inside, pltpu.roll(part, (-offset_z * SLOTS) % lanes, 1), 0.0) for part in row]
        for turn in range(SLOTS):
            if turn == 0:
                other = base
            else:
                keep = slot + turn < SLOTS
                other = [
                    jnp.where(keep, pltpu.roll(part, lanes - turn, 1), pltpu.roll(part, SLOTS - turn, 1))
                    for part in base
                ]
            dx = px - other[0]
            dy = py - other[1]
            dz = pz - other[2]
            strength = other[3] * jnp.exp(-(dx * dx + dy * dy + dz * dz) / spread_sq)
            fx = fx + dx * strength
            fy = fy + dy * strength
            fz = fz + dz * strength
    if scale:
        active = move_step * occ_ref[...]
        for plane, total in enumerate((fx, fy, fz)):
            summed = total[0:rows]
            for group in range(1, groups):
                summed = summed + total[group * rows : (group + 1) * rows]
            out_ref[plane, 0:rows, :] = active * summed
    else:
        out_ref[0] = fx
        out_ref[1] = fy
        out_ref[2] = fz


def pallas_forces(points, bordered, occupancy, partial, shifts, scale):
    planes, _, rows, lanes = points.shape
    stacked = -(-9 * rows // 8) * 8
    if partial is None:
        partial = jnp.zeros((3, stacked, lanes), jnp.float32)
    out_rows = rows if scale else stacked
    return pl.pallas_call(
        functools.partial(forces_kernel, shifts, scale),
        out_shape=jax.ShapeDtypeStruct((3, out_rows, lanes), jnp.float32),
        scratch_shapes=[pltpu.VMEM((3, stacked, lanes), jnp.float32), pltpu.VMEM((4, stacked, lanes), jnp.float32)],
        cost_estimate=pl.CostEstimate(
            flops=3_000_000 * len(shifts), transcendentals=150_000 * len(shifts), bytes_accessed=150_000
        ),
    )(points[:, 0], bordered, occupancy[0].astype(jnp.float32), partial)


def arrived_kernel(starts, state, x_below, x_above, side_below, side_above, corner_below, corner_above, out_ref):
    along_x, beside, corner = starts
    span = state

    def rows(ref, first):
        return ref[first : first + span, :]

    out_ref[0] = rows(corner_above, corner)
    out_ref[1] = rows(x_above, along_x + span)
    out_ref[2] = rows(corner_below, corner)
    out_ref[3] = rows(side_above, beside)
    out_ref[4] = rows(side_below, beside)
    out_ref[5] = rows(corner_above, corner + span)
    out_ref[6] = rows(x_below, along_x + span)
    out_ref[7] = rows(corner_below, corner + span)


def gather_arrived(x_flats, side_flats, corner_flats, along_x, beside, corner, shape):
    state, lanes = shape
    return pl.pallas_call(
        functools.partial(arrived_kernel, (along_x, beside, corner), state),
        out_shape=jax.ShapeDtypeStruct((8, state, lanes), jnp.float32),
        cost_estimate=pl.CostEstimate(flops=0, transcendentals=0, bytes_accessed=300_000),
    )(*x_flats, *side_flats, *corner_flats)


def on_device(
    field,
    rates,
    mixing,
    secretion,
    positions,
    stiffness,
    occupancy,
    offsets,
    migrant_state,
    migrant_live,
):
    weight = stiffness * occupancy.astype(jnp.float32)
    points = jnp.concatenate([positions, weight[None]], axis=0)
    payload = migrant_state * migrant_live.astype(jnp.float32)
    source = deposit(secretion, occupancy, offsets)
    current = field

    (x_low, points_low, moved_up), (x_high, points_high, moved_down), *x_flats = send_pair(
        "gx",
        [current[:, -1:], points, payload[5:8]],
        [current[:, :1], points, payload[0:3]],
    )
    (y_low, beside_up), (y_high, beside_down), *side_flats = send_pair(
        "gy",
        [current[:, :, -1:], payload[4:5]],
        [current[:, :, :1], payload[3:4]],
    )
    current = advance(framed(current, x_low, x_high, y_low, y_high), source, rates, mixing)

    row_points = jnp.concatenate([points_low, points, points_high], axis=1)
    x_low, x_high = halos(current, "gx", 1)
    (y_low, points_low, corner_up), (y_high, points_high, corner_down), *corner_flats = send_pair(
        "gy",
        [current[:, :, -1:], row_points[:, :, -1:], jnp.stack([moved_down[2], moved_up[2]])],
        [current[:, :, :1], row_points[:, :, :1], jnp.stack([moved_down[0], moved_up[0]])],
    )
    bordered = jnp.concatenate([points_low, row_points, points_high], axis=2)
    field_rows = x_low.size // 128
    side_rows = y_low.size // 128
    starts = (field_rows + points.size // 128, side_rows, side_rows + points_low.size // 128)
    rows = points.shape[2]
    partial = pallas_forces(points, bordered, occupancy, None, (-1, 0), False)
    current, partial = lax.optimization_barrier((current, partial))
    current = advance(framed(current, x_low, x_high, y_low, y_high), source, rates, mixing)
    current, x_flats, side_flats, corner_flats = lax.optimization_barrier((current, x_flats, side_flats, corner_flats))

    def gather():
        return gather_arrived(x_flats, side_flats, corner_flats, *starts, payload.shape[1:])

    current, arrived = substep_beside(current, source, rates, mixing, gather)
    current, partial = lax.optimization_barrier((current, partial))

    def finish():
        return pallas_forces(points, bordered, occupancy, partial, (1,), True)

    current, force = substep_beside(current, source, rates, mixing, finish)
    displacement = force.reshape(3, 1, rows, points.shape[3])
    return (current, displacement, arrived)


def solution(mesh):
    return jax.shard_map(
        on_device,
        mesh=mesh,
        in_specs=(
            P(None, "gx", "gy", None),
            P(),
            P(),
            P(None, "gx", "gy", None),
            P(None, "gx", "gy", None),
            P("gx", "gy", None),
            P("gx", "gy", None),
            P("gx", "gy", None),
            P(None, "gx", "gy"),
            P(None, "gx", "gy"),
        ),
        out_specs=(P(None, "gx", "gy", None), P(None, "gx", "gy", None), P(None, "gx", "gy")),
        check_vma=False,
    )
```

```python
import functools

import jax
import jax.numpy as jnp
from jax import lax
from jax.experimental import pallas as pl
from jax.experimental.pallas import tpu as pltpu
from jax.sharding import PartitionSpec as P

BIN_XY = 4
BIN_Z = 8
SLOTS = 16
SUBSTEPS = 4


time_step = 0.15
move_step = 0.1
spread_sq = 8.0
shifts = ((-1, -1), (-1, 0), (-1, 1), (0, -1), (0, 1), (1, -1), (1, 0), (1, 1))


def padded_2(cells, sides, width):
    for axis, dim in sides:
        count = lax.axis_size(axis)
        ends = count - 1
        head = lax.slice_in_dim(cells, 0, width, axis=dim)
        tail = lax.slice_in_dim(cells, cells.shape[dim] - width, cells.shape[dim], axis=dim)
        cells = jnp.concatenate(
            [
                lax.ppermute(tail, axis, [(i, (i + 1) % count) for i in range(ends)]),
                cells,
                lax.ppermute(head, axis, [((i + 1) % count, i) for i in range(ends)]),
            ],
            axis=dim,
        )
    return cells


def halos(cells, axis, dim):
    count = lax.axis_size(axis)
    ends = count - 1
    head = lax.slice_in_dim(cells, 0, 1, axis=dim)
    tail = lax.slice_in_dim(cells, cells.shape[dim] - 1, cells.shape[dim], axis=dim)
    low = lax.ppermute(tail, axis, [(i, (i + 1) % count) for i in range(ends)])
    high = lax.ppermute(head, axis, [((i + 1) % count, i) for i in range(ends)])
    return low, high


def framed(cells, x_low, x_high, y_low, y_high):
    species, width, depth, lanes = cells.shape
    corner = jnp.zeros((species, 1, 1, lanes), cells.dtype)
    middle = jnp.concatenate([x_low, cells, x_high], axis=1)
    left = jnp.concatenate([corner, y_low, corner], axis=1)
    right = jnp.concatenate([corner, y_high, corner], axis=1)
    return jnp.concatenate([left, middle, right], axis=2)


def substep_beside(current, source, rates, mixing, work):
    x_low, x_high = halos(current, "gx", 1)
    y_low, y_high = halos(current, "gy", 2)
    done = work()
    current, done = lax.optimization_barrier((current, done))
    padded = framed(current, x_low, x_high, y_low, y_high)
    return advance(padded, source, rates, mixing), done


def substep(current, source, rates, mixing):
    x_low, x_high = halos(current, "gx", 1)
    y_low, y_high = halos(current, "gy", 2)
    padded = framed(current, x_low, x_high, y_low, y_high)
    return advance(padded, source, rates, mixing)


def shifted(block, axis, distance):
    devices = range(lax.axis_size(axis))
    route = [(i - distance, i) for i in devices if i - distance in devices]
    return lax.ppermute(block, axis, route)


def advance(padded, source, rates, mixing):
    center = padded[:, 1:-1, 1:-1, :]
    deeper = jnp.pad(center, ((0, 0), (0, 0), (0, 0), (1, 1)))
    beside = padded[:, 2:, 1:-1, :] + padded[:, :-2, 1:-1, :]
    beside = beside + padded[:, 1:-1, 2:, :] + padded[:, 1:-1, :-2, :]
    beside = beside + deeper[:, :, :, 2:] + deeper[:, :, :, :-2]
    laplace = beside - 6.0 * center
    species = center.shape[0]
    mixed = jnp.dot(mixing, center.reshape(species, -1), precision=lax.Precision.HIGHEST).reshape(
        center.shape
    )
    return (
        center
        + time_step * (rates[:, None, None, None] * laplace)
        + time_step * mixed
        + time_step * source
    )


def deposit_kernel(rates_ref, code_ref, out_ref, spread_ref, place_ref):
    slots, rows, layers = rates_ref.shape
    bins_y = code_ref.shape[1]
    species = rows // bins_y
    lanes = layers * BIN_Z
    layer_of = lax.broadcasted_iota(jnp.int32, (layers, lanes), 1) // BIN_Z
    expand = (lax.broadcasted_iota(jnp.int32, (layers, lanes), 0) == layer_of).astype(jnp.float32)
    for slot in range(slots):
        spread_ref[slot] = jnp.dot(rates_ref[slot], expand, precision=lax.Precision.HIGHEST, preferred_element_type=jnp.float32)
        place_ref[slot] = jnp.dot(code_ref[slot], expand, precision=lax.Precision.HIGHEST, preferred_element_type=jnp.float32)
    depth = lax.broadcasted_iota(jnp.int32, (1, lanes), 1) % BIN_Z

    def body(index, carry):
        cell_x = index // (bins_y * BIN_XY)
        row_y = index % (bins_y * BIN_XY)
        bin_y = row_y // BIN_XY
        cell_y = row_y % BIN_XY
        target = (depth + (cell_x * (BIN_XY * BIN_Z) + cell_y * BIN_Z)).astype(jnp.float32)
        first = pl.multiple_of(bin_y * species, species)
        total = jnp.zeros((species, lanes), jnp.float32)
        for slot in range(slots):
            hit = place_ref[slot, pl.ds(bin_y, 1), :] == target
            total = total + jnp.where(hit, spread_ref[slot, pl.ds(first, species), :], 0.0)
        out_ref[cell_x, row_y] = total
        return carry

    lax.fori_loop(0, BIN_XY * bins_y * BIN_XY, body, 0)


def deposit(secretion, occupancy, offsets):
    species, bins_x, bins_y, lanes = secretion.shape
    layers = lanes // SLOTS
    rates_slot = secretion.reshape(species, bins_y, layers, SLOTS)
    rates_slot = jnp.transpose(rates_slot, (3, 1, 0, 2)).reshape(SLOTS, bins_y * species, layers)
    code = jnp.where(occupancy != 0, offsets, -1).astype(jnp.float32).reshape(bins_y, layers, SLOTS)
    code = jnp.transpose(code, (2, 0, 1))
    out = pl.pallas_call(
        deposit_kernel,
        out_shape=jax.ShapeDtypeStruct((BIN_XY, bins_y * BIN_XY, species, layers * BIN_Z), jnp.float32),
        scratch_shapes=[
            pltpu.VMEM((SLOTS, bins_y * species, layers * BIN_Z), jnp.float32),
            pltpu.VMEM((SLOTS, bins_y, layers * BIN_Z), jnp.float32),
        ],
        cost_estimate=pl.CostEstimate(flops=10_000_000, transcendentals=0, bytes_accessed=1_300_000),
    )(rates_slot, code)
    return jnp.transpose(out, (2, 0, 1, 3))

def pair_forces(points, padded, occupancy):
    planes, bins_x, bins_y, lanes = points.shape
    layers = lanes // SLOTS
    boxed = padded.reshape(planes, bins_x + 2, bins_y + 2, layers, SLOTS)
    boxed = jnp.pad(boxed, ((0, 0), (0, 0), (0, 0), (1, 1), (0, 0)))
    owned = points.reshape(planes, bins_x, bins_y, layers, SLOTS)[:3, :, :, :, :, None]
    force = jnp.zeros((3, bins_x, bins_y, layers, SLOTS), jnp.float32)
    for offset_x in range(3):
        nearby = jnp.concatenate(
            [
                boxed[
                    :,
                    offset_x : offset_x + bins_x,
                    offset_y : offset_y + bins_y,
                    offset_z : offset_z + layers,
                    :,
                ]
                for offset_y in range(3)
                for offset_z in range(3)
            ],
            axis=-1,
        )
        apart = owned - nearby[:3, :, :, :, None, :]
        strength = nearby[3][:, :, :, None, :] * jnp.exp(
            -jnp.sum(apart * apart, axis=0) / spread_sq
        )
        force = force + jnp.sum(apart * strength[None], axis=-1)
    active = occupancy.reshape(1, bins_x, bins_y, layers, SLOTS).astype(jnp.float32)
    return (move_step * active * force).reshape(3, bins_x, bins_y, lanes)


def storage_order(piece):
    if piece.ndim == 4 and piece.shape[0] > 4:
        return (1, 2, 0, 3)
    return tuple(range(piece.ndim))


def pack(pieces):
    return jnp.concatenate(
        [jnp.transpose(piece, storage_order(piece)).reshape(-1, 128) for piece in pieces], axis=0
    )


def unpack(flat, pieces):
    out = []
    row = 0
    for piece in pieces:
        rows = piece.size // 128
        order = storage_order(piece)
        stored = flat[row : row + rows].reshape(tuple(piece.shape[axis] for axis in order))
        out.append(jnp.transpose(stored, tuple(order.index(axis) for axis in range(piece.ndim))))
        row += rows
    return out


def send_pair(axis, upward, downward):
    count = lax.axis_size(axis)
    up = [(i, i + 1) for i in range(count - 1)]
    down = [(i + 1, i) for i in range(count - 1)]
    below = lax.ppermute(pack(upward), axis, up)
    above = lax.ppermute(pack(downward), axis, down)
    return unpack(below, upward), unpack(above, downward), below, above


def forces_kernel(shifts, scale, own_ref, near_ref, occ_ref, start_ref, out_ref, mine_ref, other_ref):
    rows = own_ref.shape[1]
    lanes = own_ref.shape[-1]
    layers = lanes // SLOTS
    stacked = mine_ref.shape[1]
    groups = 9
    mine_ref[...] = jnp.zeros_like(mine_ref)
    other_ref[...] = jnp.zeros_like(other_ref)
    for plane in range(4):
        for offset_x in range(3):
            for offset_y in range(3):
                group = (offset_x * 3 + offset_y) * rows
                other_ref[plane, group : group + rows, :] = near_ref[plane, offset_x, offset_y : offset_y + rows, :]
                if plane < 3:
                    mine_ref[plane, group : group + rows, :] = own_ref[plane]
    px = mine_ref[0]
    py = mine_ref[1]
    pz = mine_ref[2]
    lane = lax.broadcasted_iota(jnp.int32, (stacked, lanes), 1)
    slot = lane % SLOTS
    layer = lane // SLOTS
    fx = start_ref[0]
    fy = start_ref[1]
    fz = start_ref[2]
    row = [other_ref[plane] for plane in range(4)]
    for offset_z in shifts:
        if offset_z == 0:
            base = row
        else:
            inside = (layer + offset_z >= 0) & (layer + offset_z < layers)
            base = [jnp.where(inside, pltpu.roll(part, (-offset_z * SLOTS) % lanes, 1), 0.0) for part in row]
        for turn in range(SLOTS):
            if turn == 0:
                other = base
            else:
                keep = slot + turn < SLOTS
                other = [
                    jnp.where(keep, pltpu.roll(part, lanes - turn, 1), pltpu.roll(part, SLOTS - turn, 1))
                    for part in base
                ]
            dx = px - other[0]
            dy = py - other[1]
            dz = pz - other[2]
            strength = other[3] * jnp.exp(-(dx * dx + dy * dy + dz * dz) / spread_sq)
            fx = fx + dx * strength
            fy = fy + dy * strength
            fz = fz + dz * strength
    if scale:
        active = move_step * occ_ref[...]
        for plane, total in enumerate((fx, fy, fz)):
            summed = total[0:rows]
            for group in range(1, groups):
                summed = summed + total[group * rows : (group + 1) * rows]
            out_ref[plane, 0:rows, :] = active * summed
    else:
        out_ref[0] = fx
        out_ref[1] = fy
        out_ref[2] = fz


def pallas_forces(points, bordered, occupancy, partial, shifts, scale):
    planes, _, rows, lanes = points.shape
    stacked = -(-9 * rows // 8) * 8
    if partial is None:
        partial = jnp.zeros((3, stacked, lanes), jnp.float32)
    out_rows = rows if scale else stacked
    return pl.pallas_call(
        functools.partial(forces_kernel, shifts, scale),
        out_shape=jax.ShapeDtypeStruct((3, out_rows, lanes), jnp.float32),
        scratch_shapes=[pltpu.VMEM((3, stacked, lanes), jnp.float32), pltpu.VMEM((4, stacked, lanes), jnp.float32)],
        cost_estimate=pl.CostEstimate(
            flops=3_000_000 * len(shifts), transcendentals=150_000 * len(shifts), bytes_accessed=150_000
        ),
    )(points[:, 0], bordered, occupancy[0].astype(jnp.float32), partial)


def arrived_kernel(starts, state, x_below, x_above, side_below, side_above, corner_below, corner_above, out_ref):
    along_x, beside, corner = starts
    span = state

    def rows(ref, first):
        return ref[first : first + span, :]

    out_ref[0] = rows(corner_above, corner)
    out_ref[1] = rows(x_above, along_x + span)
    out_ref[2] = rows(corner_below, corner)
    out_ref[3] = rows(side_above, beside)
    out_ref[4] = rows(side_below, beside)
    out_ref[5] = rows(corner_above, corner + span)
    out_ref[6] = rows(x_below, along_x + span)
    out_ref[7] = rows(corner_below, corner + span)


def gather_arrived(x_flats, side_flats, corner_flats, along_x, beside, corner, shape):
    state, lanes = shape
    return pl.pallas_call(
        functools.partial(arrived_kernel, (along_x, beside, corner), state),
        out_shape=jax.ShapeDtypeStruct((8, state, lanes), jnp.float32),
        cost_estimate=pl.CostEstimate(flops=0, transcendentals=0, bytes_accessed=300_000),
    )(*x_flats, *side_flats, *corner_flats)


def on_device(
    field,
    rates,
    mixing,
    secretion,
    positions,
    stiffness,
    occupancy,
    offsets,
    migrant_state,
    migrant_live,
):
    weight = stiffness * occupancy.astype(jnp.float32)
    points = jnp.concatenate([positions, weight[None]], axis=0)
    payload = migrant_state * migrant_live.astype(jnp.float32)
    source = deposit(secretion, occupancy, offsets)
    current = field

    (x_low, points_low, moved_up), (x_high, points_high, moved_down), *x_flats = send_pair(
        "gx",
        [current[:, -1:], points, payload[5:8]],
        [current[:, :1], points, payload[0:3]],
    )
    (y_low, beside_up), (y_high, beside_down), *side_flats = send_pair(
        "gy",
        [current[:, :, -1:], payload[4:5]],
        [current[:, :, :1], payload[3:4]],
    )
    current = advance(framed(current, x_low, x_high, y_low, y_high), source, rates, mixing)

    row_points = jnp.concatenate([points_low, points, points_high], axis=1)
    x_low, x_high = halos(current, "gx", 1)
    (y_low, points_low, corner_up), (y_high, points_high, corner_down), *corner_flats = send_pair(
        "gy",
        [current[:, :, -1:], row_points[:, :, -1:], jnp.stack([moved_down[2], moved_up[2]])],
        [current[:, :, :1], row_points[:, :, :1], jnp.stack([moved_down[0], moved_up[0]])],
    )
    bordered = jnp.concatenate([points_low, row_points, points_high], axis=2)
    field_rows = x_low.size // 128
    side_rows = y_low.size // 128
    starts = (field_rows + points.size // 128, side_rows, side_rows + points_low.size // 128)
    rows = points.shape[2]
    force = pallas_forces(points, bordered, occupancy, None, (-1, 0, 1), True)
    current, force = lax.optimization_barrier((current, force))
    current = advance(framed(current, x_low, x_high, y_low, y_high), source, rates, mixing)
    current, x_flats, side_flats, corner_flats = lax.optimization_barrier((current, x_flats, side_flats, corner_flats))

    def gather():
        return gather_arrived(x_flats, side_flats, corner_flats, *starts, payload.shape[1:])

    current = substep(current, source, rates, mixing)
    current, arrived = substep_beside(current, source, rates, mixing, gather)
    displacement = force.reshape(3, 1, rows, points.shape[3])
    return (current, displacement, arrived)


def solution(mesh):
    return jax.shard_map(
        on_device,
        mesh=mesh,
        in_specs=(
            P(None, "gx", "gy", None),
            P(),
            P(),
            P(None, "gx", "gy", None),
            P(None, "gx", "gy", None),
            P("gx", "gy", None),
            P("gx", "gy", None),
            P("gx", "gy", None),
            P(None, "gx", "gy"),
            P(None, "gx", "gy"),
        ),
        out_specs=(P(None, "gx", "gy", None), P(None, "gx", "gy", None), P(None, "gx", "gy")),
        check_vma=False,
    )
```
